128 devices in a mesh: seq: 16 (over x, y), resp: 8 (over z, core).
Axes of the slice: x: 4, y: 4, z: 4, core: 2. Of those that a mesh axis runs over, the one named last changes fastest.
Arguments:
- prompt_keys: bfloat16 [2, 2048, 1024], P(None, 'seq'), may hold values from -6.1 to 6.1
- prompt_values: bfloat16 [2, 2048, 1024], P(None, 'seq'), may hold values from -6 to 6
- resp_query: bfloat16 [16, 1024, 8192], P('resp', None, 'seq'), may hold values from -121 to 121
- resp_keys: bfloat16 [16, 1024, 1024], P('resp'), may hold values from -6 to 6
- resp_values: bfloat16 [16, 1024, 1024], P('resp'), may hold values from -6 to 6
- prompt_x: bfloat16 [2, 2048, 16384], P(None, 'seq', 'resp'), may hold values from -6 to 6
- prompt_dt: float32 [2, 256, 2048], P(None, 'resp', 'seq'), may hold values from 0 to 0.5, as said below
- prompt_b: bfloat16 [2, 2048, 128], P(None, 'seq'), may hold values from -6 to 6
- prompt_c: bfloat16 [2, 2048, 128], P(None, 'seq'), may hold values from -0.5 to 0.5
- resp_x: bfloat16 [16, 1024, 16384], P('resp', None, 'seq'), may hold values from -6 to 6
- resp_dt: float32 [16, 256, 1024], P('resp', 'seq'), may hold values from 0 to 0.5, as said below
- resp_b: bfloat16 [16, 1024, 128], P('resp'), may hold values from -6 to 6
- resp_c: bfloat16 [16, 1024, 128], P('resp'), may hold values from -0.5 to 0.5
- ssm_rate: float32 [256], replicated, may hold values from 0.7 to 1.4
- resp_group: int32 [16], P('resp'), may hold values from 0 to 1
- resp_len: int32 [16], P('resp'), may hold values from 1 to 1024, 10240 in all
Outputs:
- resp_attn_out: bfloat16 [16, 1024, 8192], P('resp', None, 'seq')
- resp_ssm_out: bfloat16 [16, 1024, 16384], P('resp', None, 'seq')
- prompt_ssm_out: bfloat16 [2, 2048, 16384], P(None, 'seq', 'resp')
The draws below stay inside these ranges and needn't reach their ends.
Inputs may be any that keep to these rules, and one draw needn't show every extreme that they name: `prompt_dt`: positive step sizes. `resp_dt`: positive step sizes.
All inputs are finite; a program needn't handle non-finite values. No bound on the sum of `resp_len` on one device may be relied on, other than what follows from the above.
Results may differ from the reference program's by a relative error of at most 0.0048.
Values may be sent and summed in bfloat16 or wider, within the bound.
No kernel may reach another device: no remote copies, remote signals or barrier semaphores. Data moves between devices by JAX's collectives and lax.ppermute only.
A program may use at most 192 MiB of HBM per device.

```python
import math
import jax
import jax.numpy as jnp
import numpy as np
from jax import lax

HDIM = 128
QPK = 8
HEADS = 64
KVH = 8
SP = 64
NST = 128
SSM_HEADS = 256
QS = 128
PROMPTS = 2
P_DEV = 128
PLEN = 2048
RESPONSES = 16
RLEN = 1024


def key_table(key):
    table = jax.random.normal(jax.random.fold_in(key, 1), (PROMPTS, PLEN, KVH * HDIM), jnp.float32)
    return jnp.clip(table, -6.0, 6.0)


def draw_prompt_keys(key, part):
    table = key_table(key)
    return table.astype(jnp.bfloat16)


def draw_resp_query(key, part):
    queries = 2.5 * jnp.clip(jax.random.normal(jax.random.fold_in(key, 2), (RESPONSES, RLEN, HEADS * HDIM), jnp.float32), -6.0, 6.0)
    return queries.astype(jnp.bfloat16)


def draw_prompt_x(key, part):
    shards = PLEN // P_DEV
    shape = (PROMPTS, shards, P_DEV, SSM_HEADS, SP)
    base = jnp.clip(jax.random.normal(jax.random.fold_in(key, 41), shape, jnp.float32), -6.0, 6.0)
    loud = jax.random.uniform(jax.random.fold_in(key, 42), (PROMPTS, shards, 1, SSM_HEADS, 1)) < 0.5
    level = jax.random.uniform(jax.random.fold_in(key, 43), (PROMPTS, shards, 1, SSM_HEADS, 1))
    amplitude = jnp.where(loud, jnp.exp(jnp.log(0.5) * level), 0.02 * jnp.exp(jnp.log(1.5) * level))
    return (base * amplitude).reshape(PROMPTS, PLEN, SSM_HEADS * SP).astype(jnp.bfloat16)


def slow_heads(key):
    share = 0.5
    return jax.random.uniform(jax.random.fold_in(key, 21), (SSM_HEADS,)) < share


def change_sizes_abs(key, diagonal_lookup_vector, element_tally, window_extent, packet_clusters):
    span = PLEN + RLEN
    slow = slow_heads(key)
    unit_draw = jax.random.uniform(jax.random.fold_in(diagonal_lookup_vector, 1), (element_tally, SSM_HEADS, 1))
    gradual_rate_floor = jnp.exp(jnp.log(0.05 / span) + unit_draw * jnp.log(6.0))
    fast_base = jnp.exp(jnp.log(0.008) + unit_draw * jnp.log(6.25))
    base_rate = jnp.where(slow[None, :, None], gradual_rate_floor, fast_base)
    rough = jnp.exp(jax.random.uniform(jax.random.fold_in(diagonal_lookup_vector, 2), (element_tally, SSM_HEADS, window_extent), jnp.float32, -0.4, 0.4))
    block_factor = jnp.exp(jax.random.uniform(jax.random.fold_in(diagonal_lookup_vector, 3), (element_tally, SSM_HEADS, window_extent // QS, 1), jnp.float32, jnp.log(0.5), jnp.log(2.0)))
    block_factor = jnp.broadcast_to(block_factor, (element_tally, SSM_HEADS, window_extent // QS, QS)).reshape(element_tally, SSM_HEADS, window_extent)
    destination_places = jax.random.randint(jax.random.fold_in(diagonal_lookup_vector, 4), (element_tally, packet_clusters), 0, window_extent)
    struck = jnp.any(jnp.arange(window_extent)[None, None, :] == destination_places[:, :, None], axis=1)
    return base_rate * rough * block_factor + 0.32 * struck[:, None, :].astype(jnp.float32)


def draw_prompt_dt(key, part):
    return change_sizes_abs(key, jax.random.fold_in(key, 31), PROMPTS, PLEN, 2)


def draw_resp_dt(key, part):
    return change_sizes_abs(key, jax.random.fold_in(key, 32), RESPONSES, RLEN, 1)


def place_ends(entries, own_key, smallest, top_value):
    extent = entries.shape
    place = [jax.random.randint(jax.random.fold_in(own_key, axis), (), 0, extent[axis]) for axis in range(len(extent))]
    entries = entries.at[tuple(place)].set(smallest)
    longest = extent.index(max(extent))
    place[longest] = (place[longest] + 1) % extent[longest]
    return entries.at[tuple(place)].set(top_value)


def levels(stream_key, extent, pieces, low, largest):
    gain = 1.0
    for dim, blocks in pieces:
        heights = jax.random.uniform(jax.random.fold_in(jax.random.fold_in(stream_key, 6), dim), (blocks,), jnp.float32, low / len(pieces), largest / len(pieces))
        gain = gain * jnp.repeat(jnp.exp(heights), extent[dim] // blocks).reshape((-1,) + (1,) * (len(extent) - 1 - dim))
    return gain


def profile(count, total, bound, lean):
    portions = [(1 << 20) // math.isqrt(grade ** lean) + 1 for grade in range(2, count + 1)]
    spare, counts = total - bound - (count - 1), [1] * (count - 1)
    while spare > 0:
        candidates = [i for i in range(count - 1) if counts[i] < bound]
        mass, budget = sum([portions[i] for i in candidates]), spare
        for i in candidates:
            addition = min(bound - counts[i], max(1, budget * portions[i] // mass), spare)
            counts[i] = counts[i] + addition
            spare = spare - addition
    return np.array([bound] + counts)


def uneven_parts(rng, amount, total, reach, lean):
    if amount == 2:
        one = jax.random.randint(rng, (), max(1, total - reach), min(reach, total - 1) + 1)
        return jnp.stack([one, total - one])
    lengths = jnp.asarray(profile(amount, total, reach, lean), jnp.int32)
    twos = (amount - 1) // 2
    donor, receiver = lengths[1:1 + 2 * twos:2], lengths[2:2 + 2 * twos:2]
    room = jnp.minimum(donor - 1, reach - receiver)
    moved = jax.random.randint(jax.random.fold_in(rng, 1), (twos,), 0, 1 << 20) % (room + 1)
    lengths = lengths.at[1:1 + 2 * twos:2].set(donor - moved).at[2:2 + 2 * twos:2].set(receiver + moved)
    return lengths[jax.random.permutation(jax.random.fold_in(rng, 2), amount)]


def normal_values(rng, dims, scale, reach, cuts=(), held_as=jnp.bfloat16):
    drawn = jax.random.normal(rng, dims, jnp.float32) * scale
    if len(cuts) > 0:
        drawn = levels(rng, dims, cuts, -0.22, 0.18) * drawn
    return jnp.clip(drawn, min=-reach, max=reach).astype(held_as)


def setup_inputs(seed: int = 0) -> dict:
    key_list = jax.random.split(jax.random.key(seed), 17)
    return {
        "prompt_keys": draw_prompt_keys(jax.random.fold_in(key_list[16], 71), 0),
        "prompt_values": normal_values(key_list[1], (PROMPTS, PLEN, KVH * HDIM), 1.0, 6.0, ((1, 16),)),
        "resp_query": draw_resp_query(jax.random.fold_in(key_list[16], 71), 0),
        "resp_keys": normal_values(key_list[3], (RESPONSES, RLEN, KVH * HDIM), 1.0, 6.0, ((0, 8),)),
        "resp_values": normal_values(key_list[4], (RESPONSES, RLEN, KVH * HDIM), 1.0, 6.0, ((0, 8),)),
        "prompt_x": draw_prompt_x(jax.random.fold_in(key_list[16], 71), 0),
        "prompt_dt": draw_prompt_dt(jax.random.fold_in(key_list[16], 71), 0),
        "prompt_b": normal_values(key_list[7], (PROMPTS, PLEN, NST), 1.0, 6.0, ((1, 16),)),
        "prompt_c": normal_values(key_list[8], (PROMPTS, PLEN, NST), NST ** -0.5, 0.5, ((1, 16),)),
        "resp_x": normal_values(key_list[9], (RESPONSES, RLEN, SSM_HEADS * SP), 1.0, 6.0, ((0, 8), (2, 16))),
        "resp_dt": draw_resp_dt(jax.random.fold_in(key_list[16], 71), 0),
        "resp_b": normal_values(key_list[11], (RESPONSES, RLEN, NST), 1.0, 6.0, ((0, 8),)),
        "resp_c": normal_values(key_list[12], (RESPONSES, RLEN, NST), NST ** -0.5, 0.5, ((0, 8),)),
        "ssm_rate": jnp.clip(jnp.exp(jax.random.uniform(key_list[13], (SSM_HEADS,), jnp.float32, math.log(0.7), math.log(1.4))), 0.7, 1.4),
        "resp_group": place_ends(jax.random.randint(key_list[14], (RESPONSES,), 0, PROMPTS), jax.random.fold_in(key_list[14], 1), 0, PROMPTS - 1).astype(jnp.int32),
        "resp_len": uneven_parts(key_list[15], RESPONSES, RESPONSES * RLEN * 5 // 8, RLEN, 1).astype(jnp.int32),
    }


EPS = 1e-05

def block_ref(inputs, steps, b_rows, c_rows, rates, state):
    exponent = jnp.cumsum(-steps * rates[:, None], axis=1)
    width = inputs.shape[0]
    lower = jnp.arange(width)[:, None] >= jnp.arange(width)[None, :]
    spread = jnp.where(lower[None], exponent[:, :, None] - exponent[:, None, :], -jnp.inf)
    gram = jnp.dot(c_rows, b_rows.T, preferred_element_type=jnp.float32)
    mixing = (jnp.exp(spread) * gram[None] * steps[:, None, :]).astype(jnp.bfloat16)
    local = jnp.einsum('hts,shp->thp', mixing.astype(jnp.float32), inputs.astype(jnp.float32))
    carried = jnp.einsum('tn,hpn->thp', c_rows.astype(jnp.float32), state, precision=lax.Precision.HIGHEST)
    output = local + carried * jnp.exp(exponent).T[:, :, None]
    last = exponent[:, -1]
    weighted = (inputs.astype(jnp.float32) * (jnp.exp(last[:, None] - exponent) * steps).T[:, :, None]).astype(jnp.bfloat16)
    fresh = jnp.einsum('thp,tn->hpn', weighted.astype(jnp.float32), b_rows.astype(jnp.float32))
    return (output, jnp.exp(last)[:, None, None] * state + fresh)

def sequence_ref(inputs, steps, b_rows, c_rows, rates, state):
    window_extent = inputs.shape[0]
    heads = steps.shape[0]
    blocks = window_extent // QS
    xs = inputs.reshape(blocks, QS, heads, SP)
    ss = steps.reshape(heads, blocks, QS).transpose(1, 0, 2)
    bs = b_rows.reshape(blocks, QS, NST)
    cs = c_rows.reshape(blocks, QS, NST)

    def advance(carry, block):
        out, carry_next = block_ref(block[0], block[1], block[2], block[3], rates, carry)
        return (carry_next, out)
    final, outs = lax.scan(advance, state, (xs, ss, bs, cs))
    return (outs.reshape(window_extent, heads, SP), final)

def head_norm(values):
    scale = lax.rsqrt(lax.optimization_barrier(jnp.mean(values * values, axis=-1, keepdims=True)) + EPS)
    return (values * scale).reshape(values.shape[0], -1)

def reference(prompt_keys, prompt_values, resp_query, resp_keys, resp_values, prompt_x, prompt_dt, prompt_b, prompt_c, resp_x, resp_dt, resp_b, resp_c, ssm_rate, resp_group, resp_len):
    prompt_outs = []
    finals = []
    for prompt in range(PROMPTS):
        out, final = sequence_ref(prompt_x[prompt], prompt_dt[prompt], prompt_b[prompt], prompt_c[prompt], ssm_rate, jnp.zeros((SSM_HEADS, SP, NST), jnp.float32))
        prompt_outs.append(head_norm(out).astype(jnp.bfloat16))
        finals.append(final)
    prompt_ssm_out = jnp.stack(prompt_outs)
    finals = jnp.stack(finals)

    def one_state(items):
        inputs, steps, b_rows, c_rows, group, window_extent = items
        start = lax.dynamic_index_in_dim(finals, group.astype(jnp.int32), 0, keepdims=False)
        out, final = sequence_ref(inputs, steps, b_rows, c_rows, ssm_rate, start)
        valid = jnp.arange(RLEN) < window_extent
        return jnp.where(valid[:, None], head_norm(out), 0.0).astype(jnp.bfloat16)
    resp_ssm_out = lax.map(one_state, (resp_x, resp_dt, resp_b, resp_c, resp_group, resp_len))
    scale = 1.0 / HDIM ** 0.5

    def one_attention(items):
        queries, own_keys, own_values, group, window_extent = items
        group = group.astype(jnp.int32)
        key_rows = jnp.concatenate([lax.dynamic_index_in_dim(prompt_keys, group, 0, keepdims=False), own_keys], axis=0)
        value_rows = jnp.concatenate([lax.dynamic_index_in_dim(prompt_values, group, 0, keepdims=False), own_values], axis=0)
        element_tally = PLEN + RLEN
        key_rows = key_rows.reshape(element_tally, KVH, HDIM).transpose(1, 0, 2)
        value_rows = value_rows.reshape(element_tally, KVH, HDIM).transpose(1, 0, 2)
        grouped = queries.reshape(RLEN, KVH, QPK, HDIM).transpose(1, 0, 2, 3)
        position = jnp.arange(RLEN)
        column = jnp.arange(element_tally)
        allowed = (column[None, :] < PLEN) | (column[None, :] - PLEN <= position[:, None])
        valid = position < window_extent

        def per_head(parts):
            head_queries, head_keys, head_values = parts
            score = jnp.einsum('tqd,sd->tqs', head_queries.astype(jnp.float32), head_keys.astype(jnp.float32)) * scale
            score = jnp.where(allowed[:, None, :], score, -jnp.inf)
            top = lax.optimization_barrier(jnp.max(score, axis=-1, keepdims=True))
            raised = jnp.exp(score - top)
            total = lax.optimization_barrier(jnp.sum(raised, axis=-1, keepdims=True))
            weights = raised.astype(jnp.bfloat16)
            mixed = jnp.einsum('tqs,sd->tqd', weights.astype(jnp.float32), head_values.astype(jnp.float32)) / total
            return jnp.where(valid[:, None, None], mixed, 0.0).astype(jnp.bfloat16)
        result = lax.map(per_head, (grouped, key_rows, value_rows))
        return result.transpose(1, 0, 2, 3).reshape(RLEN, HEADS * HDIM)
    resp_attn_out = lax.map(one_attention, (resp_query, resp_keys, resp_values, resp_group, resp_len))
    return (resp_attn_out, resp_ssm_out, prompt_ssm_out)
```

```python
import math

import jax
import jax.numpy as jnp
from jax import lax
from jax.sharding import PartitionSpec as P

HDIM = 128
SP = 64
NST = 128
QS = 128


EPS = 1e-05


def from_behind(block, axis, distance):
    devices = range(lax.axis_size(axis))
    route = [(i - distance, i) for i in devices if i - distance in devices]
    return lax.ppermute(block, axis, route)


def broadcast(value, axis, source):
    kept = jnp.where(lax.axis_index(axis) == source, value, 0).astype(value.dtype)
    return lax.psum(kept, axis)


def block_pass(inputs, steps, b_rows, c_rows, rates, state):
    exponent = jnp.cumsum(-steps * rates[:, None], axis=1)
    width = inputs.shape[0]
    lower = lax.broadcasted_iota(jnp.int32, (width, width), 0) >= lax.broadcasted_iota(
        jnp.int32, (width, width), 1
    )
    spread = jnp.where(lower[None], exponent[:, :, None] - exponent[:, None, :], -jnp.inf)
    gram = jnp.dot(c_rows, b_rows.T, preferred_element_type=jnp.float32)
    mixing = (jnp.exp(spread) * gram[None] * steps[:, None, :]).astype(jnp.bfloat16)
    local = jnp.einsum("hts,shp->thp", mixing, inputs, preferred_element_type=jnp.float32)
    carried = jnp.einsum(
        "tn,hpn->thp", c_rows.astype(jnp.float32), state, precision=lax.Precision.HIGHEST
    )
    output = local + carried * jnp.exp(exponent).T[:, :, None]
    last = exponent[:, -1]
    weighted = (
        inputs.astype(jnp.float32) * (jnp.exp(last[:, None] - exponent) * steps).T[:, :, None]
    ).astype(jnp.bfloat16)
    fresh = jnp.einsum("thp,tn->hpn", weighted, b_rows, preferred_element_type=jnp.float32)
    return (output, jnp.exp(last)[:, None, None] * state + fresh, exponent)


def sequence_pass(inputs, steps, b_rows, c_rows, rates):
    window_extent = inputs.shape[0]
    heads = steps.shape[0]
    blocks = window_extent // QS
    xs = inputs.reshape(blocks, QS, heads, SP)
    ss = steps.reshape(heads, blocks, QS).transpose(1, 0, 2)
    bs = b_rows.reshape(blocks, QS, NST)
    cs = c_rows.reshape(blocks, QS, NST)

    def advance(carry, block):
        state, offset = carry
        out, state_next, exponent = block_pass(block[0], block[1], block[2], block[3], rates, state)
        return ((state_next, offset + exponent[:, -1]), (out, offset[:, None] + exponent))

    start = (jnp.zeros((heads, SP, NST), jnp.float32), jnp.zeros((heads,), jnp.float32))
    (final, total), (outs, decays_to) = lax.scan(advance, start, (xs, ss, bs, cs))
    decays_to = decays_to.transpose(1, 0, 2).reshape(heads, window_extent)
    return (outs.reshape(window_extent, heads, SP), final, decays_to, total)


def head_norm(values):
    scale = lax.rsqrt(jnp.mean(values * values, axis=-1, keepdims=True) + EPS)
    return (values * scale).reshape(values.shape[0], -1)


def linkage_merge(earlier, later):
    return (earlier[0] * later[0], later[0][:, :, None, None] * earlier[1] + later[1])


def body(
    prompt_keys,
    prompt_values,
    resp_query,
    resp_keys,
    resp_values,
    prompt_x,
    prompt_dt,
    prompt_b,
    prompt_c,
    resp_x,
    resp_dt,
    resp_b,
    resp_c,
    ssm_rate,
    resp_group,
    resp_len,
):
    seq_index = lax.axis_index("seq")
    resp_index = lax.axis_index("resp")
    seq_count = lax.axis_size("seq")
    prompt_count = prompt_x.shape[0]
    prompt_heads = prompt_dt.shape[1]
    resp_heads = resp_dt.shape[1]
    responses_here = resp_x.shape[0]
    slots = resp_x.shape[1]
    memory_head_number = prompt_keys.shape[2] // HDIM
    repeat = seq_count // memory_head_number
    shard_rows = prompt_keys.shape[1]
    spread_keys = jnp.repeat(
        prompt_keys.reshape(prompt_count, shard_rows, memory_head_number, HDIM), repeat, axis=2
    ).reshape(prompt_count, shard_rows, seq_count * HDIM)
    spread_values = jnp.repeat(
        prompt_values.reshape(prompt_count, shard_rows, memory_head_number, HDIM), repeat, axis=2
    ).reshape(prompt_count, shard_rows, seq_count * HDIM)
    moved_keys, moved_values = (
        lax.all_to_all(spread_keys, "seq", split_axis=2, concat_axis=1, tiled=True),
        lax.all_to_all(spread_values, "seq", split_axis=2, concat_axis=1, tiled=True),
    )
    resp_rates = lax.dynamic_slice_in_dim(ssm_rate, seq_index * resp_heads, resp_heads)
    resp_locals = []
    for item in range(responses_here):
        resp_locals.append(
            sequence_pass(resp_x[item], resp_dt[item], resp_b[item], resp_c[item], resp_rates)
        )
    prompt_rates = lax.dynamic_slice_in_dim(ssm_rate, resp_index * prompt_heads, prompt_heads)
    local_outs = []
    local_states = []
    prompt_decays = []
    log_totals = []
    for prompt in range(prompt_count):
        out, final, decays_to, total = sequence_pass(
            prompt_x[prompt], prompt_dt[prompt], prompt_b[prompt], prompt_c[prompt], prompt_rates
        )
        local_outs.append(out)
        local_states.append(final)
        prompt_decays.append(decays_to)
        log_totals.append(total)
    local_state = jnp.stack(local_states)
    decay_total = jnp.exp(jnp.stack(log_totals))
    gathered_states = lax.all_gather(local_state, "seq")
    gathered_decays = lax.all_gather(decay_total, "seq")
    shard = lax.broadcasted_iota(jnp.int32, (seq_count, seq_count), 0)
    later = lax.broadcasted_iota(jnp.int32, (seq_count, seq_count), 1)
    between = (later > shard) & (later < seq_index)
    after = later > shard
    factors = gathered_decays[None]
    before_weights = jnp.prod(jnp.where(between[:, :, None, None], factors, 1.0), axis=1)
    before_weights = jnp.where((shard[:, 0] < seq_index)[:, None, None], before_weights, 0.0)
    final_weights = jnp.prod(jnp.where(after[:, :, None, None], factors, 1.0), axis=1)
    arriving_state = jnp.sum(before_weights[:, :, :, None, None] * gathered_states, axis=0)
    inclusive = jnp.sum(final_weights[:, :, :, None, None] * gathered_states, axis=0)
    prompt_outs = []
    for prompt in range(prompt_count):
        carried = jnp.einsum(
            "tn,hdn->thd",
            prompt_c[prompt].astype(jnp.float32),
            arriving_state[prompt],
            precision=lax.Precision.HIGHEST,
        )
        corrected = local_outs[prompt] + jnp.exp(prompt_decays[prompt]).T[:, :, None] * carried
        prompt_outs.append(head_norm(corrected).astype(jnp.bfloat16))
    prompt_ssm_out = jnp.stack(prompt_outs)
    finals = inclusive
    ratio = seq_count // lax.axis_size("resp")
    piece = lax.dynamic_slice_in_dim(finals, seq_index % ratio * resp_heads, resp_heads, 1)
    start_states = broadcast(piece, "resp", seq_index // ratio)
    positions = lax.broadcasted_iota(jnp.int32, (slots,), 0)
    resp_outs = []
    for item in range(responses_here):
        out, final, decays_to, total = resp_locals[item]
        initial = lax.dynamic_index_in_dim(start_states, resp_group[item], 0, keepdims=False)
        carried = jnp.einsum(
            "tn,hdn->thd",
            resp_c[item].astype(jnp.float32),
            initial,
            precision=lax.Precision.HIGHEST,
        )
        corrected = out + jnp.exp(decays_to).T[:, :, None] * carried
        valid = positions < resp_len[item]
        resp_outs.append(jnp.where(valid[:, None], head_norm(corrected), 0.0).astype(jnp.bfloat16))
    resp_ssm_out = jnp.stack(resp_outs)
    heads_here = resp_query.shape[2] // HDIM
    own_head = seq_index // repeat
    own_keys = lax.dynamic_slice_in_dim(resp_keys, own_head * HDIM, HDIM, 2)
    own_values = lax.dynamic_slice_in_dim(resp_values, own_head * HDIM, HDIM, 2)
    prompt_len = moved_keys.shape[1]
    block = min(512, slots)
    scale = 1.0 / math.sqrt(HDIM)
    attn_outs = []
    for item in range(responses_here):
        group = resp_group[item]
        window_extent = resp_len[item]
        key_rows = jnp.concatenate(
            [lax.dynamic_index_in_dim(moved_keys, group, 0, keepdims=False), own_keys[item]], axis=0
        )
        value_rows = jnp.concatenate(
            [lax.dynamic_index_in_dim(moved_values, group, 0, keepdims=False), own_values[item]],
            axis=0,
        )
        queries = resp_query[item].reshape(slots * heads_here, HDIM)
        element_tally = key_rows.shape[0]

        def attend(start):
            rows = lax.dynamic_slice_in_dim(queries, start * heads_here, block * heads_here, 0)
            score = (
                lax.dot_general(
                    rows, key_rows, (((1,), (1,)), ((), ())), preferred_element_type=jnp.float32
                )
                * scale
            )
            position = (
                start + lax.broadcasted_iota(jnp.int32, (block * heads_here,), 0) // heads_here
            )
            column = lax.broadcasted_iota(jnp.int32, (1, element_tally), 1)
            allowed = (column < prompt_len) | (column - prompt_len <= position[:, None])
            score = jnp.where(allowed, score, -jnp.inf)
            top = jnp.max(score, axis=1, keepdims=True)
            raised = jnp.exp(score - top)
            total = jnp.sum(raised, axis=1, keepdims=True)
            weights = raised.astype(jnp.bfloat16)
            mixed = jnp.dot(weights, value_rows, preferred_element_type=jnp.float32) / total
            valid = position < window_extent
            return (
                jnp.where(valid[:, None], mixed, 0.0)
                .astype(jnp.bfloat16)
                .reshape(block, heads_here * HDIM)
            )

        def attend_block(start):
            return attend(start)

        starts = jnp.arange(slots // block, dtype=jnp.int32) * block
        attn_outs.append(lax.map(attend_block, starts).reshape(slots, heads_here * HDIM))
    resp_attn_out = jnp.stack(attn_outs)
    return (resp_attn_out, resp_ssm_out, prompt_ssm_out)


def solution(mesh):
    placed = (
        P(None, "seq", None),
        P(None, "seq", None),
        P("resp", None, "seq"),
        P("resp", None, None),
        P("resp", None, None),
        P(None, "seq", "resp"),
        P(None, "resp", "seq"),
        P(None, "seq", None),
        P(None, "seq", None),
        P("resp", None, "seq"),
        P("resp", "seq", None),
        P("resp", None, None),
        P("resp", None, None),
        P(),
        P("resp"),
        P("resp"),
    )
    return jax.shard_map(
        body,
        mesh=mesh,
        in_specs=placed,
        out_specs=(P("resp", None, "seq"), P("resp", None, "seq"), P(None, "seq", "resp")),
        check_vma=False,
    )
```

```python
import math

import jax
import jax.numpy as jnp
from jax import lax
from jax.experimental import pallas as pl
from jax.experimental.pallas import tpu as pltpu
from jax.sharding import PartitionSpec as P

HDIM = 128
SP = 64
NST = 128
QS = 128


EPS = 1e-05


def from_behind(block, axis, distance):
    devices = range(lax.axis_size(axis))
    route = [(i - distance, i) for i in devices if i - distance in devices]
    return lax.ppermute(block, axis, route)


def broadcast(value, axis, source):
    kept = jnp.where(lax.axis_index(axis) == source, value, 0).astype(value.dtype)
    return lax.psum(kept, axis)


def block_pass(inputs, steps, b_rows, c_rows, rates, state):
    exponent = jnp.cumsum(-steps * rates[:, None], axis=1)
    width = inputs.shape[0]
    lower = lax.broadcasted_iota(jnp.int32, (width, width), 0) >= lax.broadcasted_iota(
        jnp.int32, (width, width), 1
    )
    spread = jnp.where(lower[None], exponent[:, :, None] - exponent[:, None, :], -jnp.inf)
    gram = jnp.dot(c_rows, b_rows.T, preferred_element_type=jnp.float32)
    mixing = (jnp.exp(spread) * gram[None] * steps[:, None, :]).astype(jnp.bfloat16)
    local = jnp.einsum("hts,shp->thp", mixing, inputs, preferred_element_type=jnp.float32)
    carried = jnp.einsum(
        "tn,hpn->thp", c_rows.astype(jnp.float32), state, precision=lax.Precision.HIGHEST
    )
    output = local + carried * jnp.exp(exponent).T[:, :, None]
    last = exponent[:, -1]
    weighted = (
        inputs.astype(jnp.float32) * (jnp.exp(last[:, None] - exponent) * steps).T[:, :, None]
    ).astype(jnp.bfloat16)
    fresh = jnp.einsum("thp,tn->hpn", weighted, b_rows, preferred_element_type=jnp.float32)
    return (output, jnp.exp(last)[:, None, None] * state + fresh, exponent)


def sequence_pass(inputs, steps, b_rows, c_rows, rates):
    window_extent = inputs.shape[0]
    heads = steps.shape[0]
    blocks = window_extent // QS
    xs = inputs.reshape(blocks, QS, heads, SP)
    ss = steps.reshape(heads, blocks, QS).transpose(1, 0, 2)
    bs = b_rows.reshape(blocks, QS, NST)
    cs = c_rows.reshape(blocks, QS, NST)

    def advance(carry, block):
        state, offset = carry
        out, state_next, exponent = block_pass(block[0], block[1], block[2], block[3], rates, state)
        return ((state_next, offset + exponent[:, -1]), (out, offset[:, None] + exponent))

    start = (jnp.zeros((heads, SP, NST), jnp.float32), jnp.zeros((heads,), jnp.float32))
    (final, total), (outs, decays_to) = lax.scan(advance, start, (xs, ss, bs, cs))
    decays_to = decays_to.transpose(1, 0, 2).reshape(heads, window_extent)
    return (outs.reshape(window_extent, heads, SP), final, decays_to, total)


def head_norm(values):
    scale = lax.rsqrt(jnp.mean(values * values, axis=-1, keepdims=True) + EPS)
    return (values * scale).reshape(values.shape[0], -1)


def linkage_merge(earlier, later):
    return (earlier[0] * later[0], later[0][:, :, None, None] * earlier[1] + later[1])


def body(
    prompt_keys,
    prompt_values,
    resp_query,
    resp_keys,
    resp_values,
    prompt_x,
    prompt_dt,
    prompt_b,
    prompt_c,
    resp_x,
    resp_dt,
    resp_b,
    resp_c,
    ssm_rate,
    resp_group,
    resp_len,
):
    seq_index = lax.axis_index("seq")
    resp_index = lax.axis_index("resp")
    seq_count = lax.axis_size("seq")
    prompt_count = prompt_x.shape[0]
    prompt_heads = prompt_dt.shape[1]
    resp_heads = resp_dt.shape[1]
    responses_here = resp_x.shape[0]
    slots = resp_x.shape[1]
    memory_head_number = prompt_keys.shape[2] // HDIM
    repeat = seq_count // memory_head_number
    shard_rows = prompt_keys.shape[1]
    spread_keys = jnp.repeat(
        prompt_keys.reshape(prompt_count, shard_rows, memory_head_number, HDIM), repeat, axis=2
    ).reshape(prompt_count, shard_rows, seq_count * HDIM)
    spread_values = jnp.repeat(
        prompt_values.reshape(prompt_count, shard_rows, memory_head_number, HDIM), repeat, axis=2
    ).reshape(prompt_count, shard_rows, seq_count * HDIM)
    moved_keys, moved_values = (
        lax.all_to_all(spread_keys, "seq", split_axis=2, concat_axis=1, tiled=True),
        lax.all_to_all(spread_values, "seq", split_axis=2, concat_axis=1, tiled=True),
    )
    resp_rates = lax.dynamic_slice_in_dim(ssm_rate, seq_index * resp_heads, resp_heads)
    resp_locals = []
    for item in range(responses_here):
        resp_locals.append(
            sequence_pass(resp_x[item], resp_dt[item], resp_b[item], resp_c[item], resp_rates)
        )
    prompt_rates = lax.dynamic_slice_in_dim(ssm_rate, resp_index * prompt_heads, prompt_heads)
    local_outs = []
    local_states = []
    prompt_decays = []
    log_totals = []
    for prompt in range(prompt_count):
        out, final, decays_to, total = sequence_pass(
            prompt_x[prompt], prompt_dt[prompt], prompt_b[prompt], prompt_c[prompt], prompt_rates
        )
        local_outs.append(out)
        local_states.append(final)
        prompt_decays.append(decays_to)
        log_totals.append(total)
    local_state = jnp.stack(local_states)
    decay_total = jnp.exp(jnp.stack(log_totals))
    gathered_states = lax.all_gather(local_state, "seq")
    gathered_decays = lax.all_gather(decay_total, "seq")
    shard = lax.broadcasted_iota(jnp.int32, (seq_count, seq_count), 0)
    later = lax.broadcasted_iota(jnp.int32, (seq_count, seq_count), 1)
    between = (later > shard) & (later < seq_index)
    after = later > shard
    factors = gathered_decays[None]
    before_weights = jnp.prod(jnp.where(between[:, :, None, None], factors, 1.0), axis=1)
    before_weights = jnp.where((shard[:, 0] < seq_index)[:, None, None], before_weights, 0.0)
    final_weights = jnp.prod(jnp.where(after[:, :, None, None], factors, 1.0), axis=1)
    arriving_state = jnp.sum(before_weights[:, :, :, None, None] * gathered_states, axis=0)
    inclusive = jnp.sum(final_weights[:, :, :, None, None] * gathered_states, axis=0)
    prompt_outs = []
    for prompt in range(prompt_count):
        carried = jnp.einsum(
            "tn,hdn->thd",
            prompt_c[prompt].astype(jnp.float32),
            arriving_state[prompt],
            precision=lax.Precision.HIGHEST,
        )
        corrected = local_outs[prompt] + jnp.exp(prompt_decays[prompt]).T[:, :, None] * carried
        prompt_outs.append(head_norm(corrected).astype(jnp.bfloat16))
    prompt_ssm_out = jnp.stack(prompt_outs)
    finals = inclusive
    ratio = seq_count // lax.axis_size("resp")
    piece = lax.dynamic_slice_in_dim(finals, seq_index % ratio * resp_heads, resp_heads, 1)
    piece, resp_query = lax.optimization_barrier((piece, resp_query))
    start_states = broadcast(piece, "resp", seq_index // ratio)
    positions = lax.broadcasted_iota(jnp.int32, (slots,), 0)
    resp_outs = []
    for item in range(responses_here):
        out, final, decays_to, total = resp_locals[item]
        initial = lax.dynamic_index_in_dim(start_states, resp_group[item], 0, keepdims=False)
        carried = jnp.einsum(
            "tn,hdn->thd",
            resp_c[item].astype(jnp.float32),
            initial,
            precision=lax.Precision.HIGHEST,
        )
        corrected = out + jnp.exp(decays_to).T[:, :, None] * carried
        valid = positions < resp_len[item]
        resp_outs.append(jnp.where(valid[:, None], head_norm(corrected), 0.0).astype(jnp.bfloat16))
    resp_ssm_out = jnp.stack(resp_outs)
    heads_here = resp_query.shape[2] // HDIM
    own_head = seq_index // repeat
    resp_attn_out = response_attention(
        resp_query, moved_keys, moved_values, resp_keys, resp_values, resp_group, resp_len, own_head
    )
    return (resp_attn_out, resp_ssm_out, prompt_ssm_out)


ROWS = 512

def response_attention(resp_query, prompt_keys, prompt_values, resp_keys, resp_values, group, length, head):
    items, slots, width = resp_query.shape
    heads = width // HDIM
    rows = slots * heads
    queries = resp_query.reshape(items, rows, HDIM)
    prompt_len = prompt_keys.shape[1]
    tile = min(ROWS, rows)
    scale = 1.0 / math.sqrt(HDIM)

    def kernel(group_ref, len_ref, head_ref, q_ref, pk_ref, pv_ref, rk_ref, rv_ref, o_ref):
        item = pl.program_id(0)
        block = pl.program_id(1)
        window_extent = len_ref[item]
        first = block * (tile // heads)

        @pl.when(first >= window_extent)
        def _():
            o_ref[...] = jnp.zeros_like(o_ref)

        @pl.when(first < window_extent)
        def _():
            q = q_ref[0]
            dims = (((1,), (1,)), ((), ()))
            s1 = lax.dot_general(q, pk_ref[0], dims, preferred_element_type=jnp.float32) * scale
            s2 = lax.dot_general(q, rk_ref[0], dims, preferred_element_type=jnp.float32) * scale
            position = first + lax.broadcasted_iota(jnp.int32, (tile, 1), 0) // heads
            column = lax.broadcasted_iota(jnp.int32, s2.shape, 1)
            s2 = jnp.where(column <= position, s2, -jnp.inf)
            top = jnp.maximum(
                jnp.max(s1, axis=1, keepdims=True), jnp.max(s2, axis=1, keepdims=True)
            )
            e1 = jnp.exp(s1 - top)
            e2 = jnp.exp(s2 - top)
            total = jnp.sum(e1, axis=1, keepdims=True) + jnp.sum(e2, axis=1, keepdims=True)
            mixed = jnp.dot(
                e1.astype(jnp.bfloat16), pv_ref[0], preferred_element_type=jnp.float32
            ) + jnp.dot(e2.astype(jnp.bfloat16), rv_ref[0], preferred_element_type=jnp.float32)
            mixed = mixed / total
            o_ref[0] = jnp.where(position < window_extent, mixed, 0.0).astype(o_ref.dtype)

    keys_total = prompt_len + slots
    cost = pl.CostEstimate(
        flops=4 * items * rows * keys_total * HDIM,
        transcendentals=items * rows * keys_total,
        bytes_accessed=2 * (2 * items * rows * HDIM + 2 * items * keys_total * HDIM),
    )
    grid_spec = pltpu.PrefetchScalarGridSpec(
        num_scalar_prefetch=3,
        grid=(items, rows // tile),
        in_specs=[
            pl.BlockSpec((1, tile, HDIM), lambda i, b, g, n, h: (i, b, 0)),
            pl.BlockSpec((1, prompt_len, HDIM), lambda i, b, g, n, h: (g[i], 0, 0)),
            pl.BlockSpec((1, prompt_len, HDIM), lambda i, b, g, n, h: (g[i], 0, 0)),
            pl.BlockSpec((1, slots, HDIM), lambda i, b, g, n, h: (i, 0, h[0])),
            pl.BlockSpec((1, slots, HDIM), lambda i, b, g, n, h: (i, 0, h[0])),
        ],
        out_specs=pl.BlockSpec((1, tile, HDIM), lambda i, b, g, n, h: (i, b, 0)),
    )
    out = pl.pallas_call(
        kernel,
        grid_spec=grid_spec,
        out_shape=jax.ShapeDtypeStruct((items, rows, HDIM), jnp.bfloat16),
        compiler_params=pltpu.CompilerParams(vmem_limit_bytes=60 * 1024 * 1024),
        cost_estimate=cost,
    )(group.astype(jnp.int32), length.astype(jnp.int32), jnp.reshape(head, (1,)).astype(jnp.int32),
      queries, prompt_keys, prompt_values, resp_keys, resp_values)
    return out.reshape(items, slots, width)


def solution(mesh):
    placed = (
        P(None, "seq", None),
        P(None, "seq", None),
        P("resp", None, "seq"),
        P("resp", None, None),
        P("resp", None, None),
        P(None, "seq", "resp"),
        P(None, "resp", "seq"),
        P(None, "seq", None),
        P(None, "seq", None),
        P("resp", None, "seq"),
        P("resp", "seq", None),
        P("resp", None, None),
        P("resp", None, None),
        P(),
        P("resp"),
        P("resp"),
    )
    return jax.shard_map(
        body,
        mesh=mesh,
        in_specs=placed,
        out_specs=(P("resp", None, "seq"), P("resp", None, "seq"), P(None, "seq", "resp")),
        check_vma=False,
    )
```

```python
import math

import jax
import jax.numpy as jnp
from jax import lax
from jax.experimental import pallas as pl
from jax.experimental.pallas import tpu as pltpu
from jax.sharding import PartitionSpec as P

HDIM = 128
SP = 64
NST = 128
QS = 128


EPS = 1e-05


def from_behind(block, axis, distance):
    devices = range(lax.axis_size(axis))
    route = [(i - distance, i) for i in devices if i - distance in devices]
    return lax.ppermute(block, axis, route)


def broadcast(value, axis, source):
    kept = jnp.where(lax.axis_index(axis) == source, value, 0).astype(value.dtype)
    return lax.psum(kept, axis)


def block_pass(inputs, steps, b_rows, c_rows, rates, state):
    exponent = jnp.cumsum(-steps * rates[:, None], axis=1)
    width = inputs.shape[0]
    lower = lax.broadcasted_iota(jnp.int32, (width, width), 0) >= lax.broadcasted_iota(
        jnp.int32, (width, width), 1
    )
    spread = jnp.where(lower[None], exponent[:, :, None] - exponent[:, None, :], -jnp.inf)
    gram = jnp.dot(c_rows, b_rows.T, preferred_element_type=jnp.float32)
    mixing = (jnp.exp(spread) * gram[None] * steps[:, None, :]).astype(jnp.bfloat16)
    local = jnp.einsum("hts,shp->thp", mixing, inputs, preferred_element_type=jnp.float32)
    carried = jnp.einsum(
        "tn,hpn->thp", c_rows.astype(jnp.float32), state, precision=lax.Precision.HIGHEST
    )
    output = local + carried * jnp.exp(exponent).T[:, :, None]
    last = exponent[:, -1]
    weighted = (
        inputs.astype(jnp.float32) * (jnp.exp(last[:, None] - exponent) * steps).T[:, :, None]
    ).astype(jnp.bfloat16)
    fresh = jnp.einsum("thp,tn->hpn", weighted, b_rows, preferred_element_type=jnp.float32)
    return (output, jnp.exp(last)[:, None, None] * state + fresh, exponent)


def sequence_pass(inputs, steps, b_rows, c_rows, rates):
    window_extent = inputs.shape[0]
    heads = steps.shape[0]
    blocks = window_extent // QS
    xs = inputs.reshape(blocks, QS, heads, SP)
    ss = steps.reshape(heads, blocks, QS).transpose(1, 0, 2)
    bs = b_rows.reshape(blocks, QS, NST)
    cs = c_rows.reshape(blocks, QS, NST)

    def advance(carry, block):
        state, offset = carry
        out, state_next, exponent = block_pass(block[0], block[1], block[2], block[3], rates, state)
        return ((state_next, offset + exponent[:, -1]), (out, offset[:, None] + exponent))

    start = (jnp.zeros((heads, SP, NST), jnp.float32), jnp.zeros((heads,), jnp.float32))
    (final, total), (outs, decays_to) = lax.scan(advance, start, (xs, ss, bs, cs))
    decays_to = decays_to.transpose(1, 0, 2).reshape(heads, window_extent)
    return (outs.reshape(window_extent, heads, SP), final, decays_to, total)


def chunked_pass(inputs, steps, b_rows, c_rows, rates):
    window_extent = inputs.shape[0]
    heads = steps.shape[0]
    blocks = window_extent // QS
    xs = inputs.reshape(blocks, QS, heads, SP).transpose(0, 2, 1, 3)
    ss = steps.reshape(heads, blocks, QS).transpose(1, 0, 2)
    bs = b_rows.reshape(blocks, QS, NST)
    cs = c_rows.reshape(blocks, QS, NST)
    exponent = jnp.cumsum(-ss * rates[None, :, None], axis=2)
    lower = lax.broadcasted_iota(jnp.int32, (QS, QS), 0) >= lax.broadcasted_iota(
        jnp.int32, (QS, QS), 1
    )
    spread = jnp.where(
        lower[None, None], exponent[:, :, :, None] - exponent[:, :, None, :], -jnp.inf
    )
    gram = jnp.einsum("ctn,cun->ctu", cs, bs, preferred_element_type=jnp.float32)
    mixing = (jnp.exp(spread) * gram[:, None] * ss[:, :, None, :]).astype(jnp.bfloat16)
    local = jnp.einsum("chtu,chup->chtp", mixing, xs, preferred_element_type=jnp.float32)
    last = exponent[:, :, -1]
    weighted = (
        xs.astype(jnp.float32) * (jnp.exp(last[:, :, None] - exponent) * ss)[:, :, :, None]
    ).astype(jnp.bfloat16)
    fresh = jnp.einsum("chup,cun->chpn", weighted, bs, preferred_element_type=jnp.float32)
    decay = jnp.exp(last)
    state = jnp.zeros((heads, SP, NST), jnp.float32)
    offset = jnp.zeros((heads,), jnp.float32)
    befores = []
    offsets = []
    for index in range(blocks):
        befores.append(state)
        offsets.append(offset)
        state = decay[index][:, None, None] * state + fresh[index]
        offset = offset + last[index]
    before = jnp.stack(befores)
    carried = jnp.einsum(
        "ctn,chpn->chtp", cs.astype(jnp.float32), before, precision=lax.Precision.HIGHEST
    )
    output = local + carried * jnp.exp(exponent)[:, :, :, None]
    decays_to = jnp.stack(offsets)[:, :, None] + exponent
    output = output.transpose(0, 2, 1, 3).reshape(window_extent, heads, SP)
    decays_to = decays_to.transpose(1, 0, 2).reshape(heads, window_extent)
    return (output, state, decays_to, offset)


def head_norm(values):
    scale = lax.rsqrt(jnp.mean(values * values, axis=-1, keepdims=True) + EPS)
    return (values * scale).reshape(values.shape[0], -1)


def linkage_merge(earlier, later):
    return (earlier[0] * later[0], later[0][:, :, None, None] * earlier[1] + later[1])


def body(
    prompt_keys,
    prompt_values,
    resp_query,
    resp_keys,
    resp_values,
    prompt_x,
    prompt_dt,
    prompt_b,
    prompt_c,
    resp_x,
    resp_dt,
    resp_b,
    resp_c,
    ssm_rate,
    resp_group,
    resp_len,
):
    seq_index = lax.axis_index("seq")
    resp_index = lax.axis_index("resp")
    seq_count = lax.axis_size("seq")
    prompt_count = prompt_x.shape[0]
    prompt_heads = prompt_dt.shape[1]
    resp_heads = resp_dt.shape[1]
    responses_here = resp_x.shape[0]
    slots = resp_x.shape[1]
    memory_head_number = prompt_keys.shape[2] // HDIM
    repeat = seq_count // memory_head_number
    shard_rows = prompt_keys.shape[1]
    spread_keys = jnp.repeat(
        prompt_keys.reshape(prompt_count, shard_rows, memory_head_number, HDIM), repeat, axis=2
    ).reshape(prompt_count, shard_rows, seq_count * HDIM)
    spread_values = jnp.repeat(
        prompt_values.reshape(prompt_count, shard_rows, memory_head_number, HDIM), repeat, axis=2
    ).reshape(prompt_count, shard_rows, seq_count * HDIM)
    moved_keys, moved_values = (
        lax.all_to_all(spread_keys, "seq", split_axis=2, concat_axis=1, tiled=True),
        lax.all_to_all(spread_values, "seq", split_axis=2, concat_axis=1, tiled=True),
    )
    resp_rates = lax.dynamic_slice_in_dim(ssm_rate, seq_index * resp_heads, resp_heads)
    resp_locals = []
    for item in range(responses_here):
        resp_locals.append(
            chunked_pass(resp_x[item], resp_dt[item], resp_b[item], resp_c[item], resp_rates)
        )
    prompt_rates = lax.dynamic_slice_in_dim(ssm_rate, resp_index * prompt_heads, prompt_heads)
    local_outs = []
    local_states = []
    prompt_decays = []
    log_totals = []
    for prompt in range(prompt_count):
        out, final, decays_to, total = sequence_pass(
            prompt_x[prompt], prompt_dt[prompt], prompt_b[prompt], prompt_c[prompt], prompt_rates
        )
        local_outs.append(out)
        local_states.append(final)
        prompt_decays.append(decays_to)
        log_totals.append(total)
    local_state = jnp.stack(local_states)
    decay_total = jnp.exp(jnp.stack(log_totals))
    gathered_states = lax.all_gather(local_state, "seq")
    gathered_decays = lax.all_gather(decay_total, "seq")
    shard = lax.broadcasted_iota(jnp.int32, (seq_count, seq_count), 0)
    later = lax.broadcasted_iota(jnp.int32, (seq_count, seq_count), 1)
    between = (later > shard) & (later < seq_index)
    after = later > shard
    factors = gathered_decays[None]
    before_weights = jnp.prod(jnp.where(between[:, :, None, None], factors, 1.0), axis=1)
    before_weights = jnp.where((shard[:, 0] < seq_index)[:, None, None], before_weights, 0.0)
    final_weights = jnp.prod(jnp.where(after[:, :, None, None], factors, 1.0), axis=1)
    arriving_state = jnp.sum(before_weights[:, :, :, None, None] * gathered_states, axis=0)
    inclusive = jnp.sum(final_weights[:, :, :, None, None] * gathered_states, axis=0)
    prompt_outs = []
    for prompt in range(prompt_count):
        carried = jnp.einsum(
            "tn,hdn->thd",
            prompt_c[prompt].astype(jnp.float32),
            arriving_state[prompt],
            precision=lax.Precision.HIGHEST,
        )
        corrected = local_outs[prompt] + jnp.exp(prompt_decays[prompt]).T[:, :, None] * carried
        prompt_outs.append(head_norm(corrected).astype(jnp.bfloat16))
    prompt_ssm_out = jnp.stack(prompt_outs)
    finals = inclusive
    ratio = seq_count // lax.axis_size("resp")
    piece = lax.dynamic_slice_in_dim(finals, seq_index % ratio * resp_heads, resp_heads, 1)
    piece, resp_query = lax.optimization_barrier((piece, resp_query))
    start_states = broadcast(piece, "resp", seq_index // ratio)
    positions = lax.broadcasted_iota(jnp.int32, (slots,), 0)
    resp_outs = []
    for item in range(responses_here):
        out, final, decays_to, total = resp_locals[item]
        initial = lax.dynamic_index_in_dim(start_states, resp_group[item], 0, keepdims=False)
        carried = jnp.einsum(
            "tn,hdn->thd",
            resp_c[item].astype(jnp.float32),
            initial,
            precision=lax.Precision.HIGHEST,
        )
        corrected = out + jnp.exp(decays_to).T[:, :, None] * carried
        valid = positions < resp_len[item]
        resp_outs.append(jnp.where(valid[:, None], head_norm(corrected), 0.0).astype(jnp.bfloat16))
    resp_ssm_out = jnp.stack(resp_outs)
    heads_here = resp_query.shape[2] // HDIM
    own_head = seq_index // repeat
    resp_attn_out = response_attention(
        resp_query, moved_keys, moved_values, resp_keys, resp_values, resp_group, resp_len, own_head
    )
    return (resp_attn_out, resp_ssm_out, prompt_ssm_out)


ROWS = 512

def response_attention(resp_query, prompt_keys, prompt_values, resp_keys, resp_values, group, length, head):
    items, slots, width = resp_query.shape
    heads = width // HDIM
    rows = slots * heads
    queries = resp_query.reshape(items, rows, HDIM)
    prompt_len = prompt_keys.shape[1]
    tile = min(ROWS, rows)
    scale = 1.0 / math.sqrt(HDIM)

    def kernel(group_ref, len_ref, head_ref, q_ref, pk_ref, pv_ref, rk_ref, rv_ref, o_ref):
        item = pl.program_id(0)
        block = pl.program_id(1)
        window_extent = len_ref[item]
        first = block * (tile // heads)

        @pl.when(first >= window_extent)
        def _():
            o_ref[...] = jnp.zeros_like(o_ref)

        @pl.when(first < window_extent)
        def _():
            q = q_ref[0]
            dims = (((1,), (1,)), ((), ()))
            s1 = lax.dot_general(q, pk_ref[0], dims, preferred_element_type=jnp.float32) * scale
            s2 = lax.dot_general(q, rk_ref[0], dims, preferred_element_type=jnp.float32) * scale
            position = first + lax.broadcasted_iota(jnp.int32, (tile, 1), 0) // heads
            column = lax.broadcasted_iota(jnp.int32, s2.shape, 1)
            s2 = jnp.where(column <= position, s2, -jnp.inf)
            top = jnp.maximum(
                jnp.max(s1, axis=1, keepdims=True), jnp.max(s2, axis=1, keepdims=True)
            )
            e1 = jnp.exp(s1 - top)
            e2 = jnp.exp(s2 - top)
            total = jnp.sum(e1, axis=1, keepdims=True) + jnp.sum(e2, axis=1, keepdims=True)
            mixed = jnp.dot(
                e1.astype(jnp.bfloat16), pv_ref[0], preferred_element_type=jnp.float32
            ) + jnp.dot(e2.astype(jnp.bfloat16), rv_ref[0], preferred_element_type=jnp.float32)
            mixed = mixed / total
            o_ref[0] = jnp.where(position < window_extent, mixed, 0.0).astype(o_ref.dtype)

    keys_total = prompt_len + slots
    cost = pl.CostEstimate(
        flops=4 * items * rows * keys_total * HDIM,
        transcendentals=items * rows * keys_total,
        bytes_accessed=2 * (2 * items * rows * HDIM + 2 * items * keys_total * HDIM),
    )
    grid_spec = pltpu.PrefetchScalarGridSpec(
        num_scalar_prefetch=3,
        grid=(items, rows // tile),
        in_specs=[
            pl.BlockSpec((1, tile, HDIM), lambda i, b, g, n, h: (i, b, 0)),
            pl.BlockSpec((1, prompt_len, HDIM), lambda i, b, g, n, h: (g[i], 0, 0)),
            pl.BlockSpec((1, prompt_len, HDIM), lambda i, b, g, n, h: (g[i], 0, 0)),
            pl.BlockSpec((1, slots, HDIM), lambda i, b, g, n, h: (i, 0, h[0])),
            pl.BlockSpec((1, slots, HDIM), lambda i, b, g, n, h: (i, 0, h[0])),
        ],
        out_specs=pl.BlockSpec((1, tile, HDIM), lambda i, b, g, n, h: (i, b, 0)),
    )
    out = pl.pallas_call(
        kernel,
        grid_spec=grid_spec,
        out_shape=jax.ShapeDtypeStruct((items, rows, HDIM), jnp.bfloat16),
        compiler_params=pltpu.CompilerParams(vmem_limit_bytes=60 * 1024 * 1024),
        cost_estimate=cost,
    )(group.astype(jnp.int32), length.astype(jnp.int32), jnp.reshape(head, (1,)).astype(jnp.int32),
      queries, prompt_keys, prompt_values, resp_keys, resp_values)
    return out.reshape(items, slots, width)


def solution(mesh):
    placed = (
        P(None, "seq", None),
        P(None, "seq", None),
        P("resp", None, "seq"),
        P("resp", None, None),
        P("resp", None, None),
        P(None, "seq", "resp"),
        P(None, "resp", "seq"),
        P(None, "seq", None),
        P(None, "seq", None),
        P("resp", None, "seq"),
        P("resp", "seq", None),
        P("resp", None, None),
        P("resp", None, None),
        P(),
        P("resp"),
        P("resp"),
    )
    return jax.shard_map(
        body,
        mesh=mesh,
        in_specs=placed,
        out_specs=(P("resp", None, "seq"), P("resp", None, "seq"), P(None, "seq", "resp")),
        check_vma=False,
    )
```

```python
import math

import jax
import jax.numpy as jnp
from jax import lax
from jax.experimental import pallas as pl
from jax.experimental.pallas import tpu as pltpu
from jax.sharding import PartitionSpec as P

HDIM = 128
SP = 64
NST = 128
QS = 128


EPS = 1e-05


def from_behind(block, axis, distance):
    devices = range(lax.axis_size(axis))
    route = [(i - distance, i) for i in devices if i - distance in devices]
    return lax.ppermute(block, axis, route)


def broadcast(value, axis, source):
    kept = jnp.where(lax.axis_index(axis) == source, value, 0).astype(value.dtype)
    return lax.psum(kept, axis)


def block_pass(inputs, steps, b_rows, c_rows, rates, state):
    exponent = jnp.cumsum(-steps * rates[:, None], axis=1)
    width = inputs.shape[0]
    lower = lax.broadcasted_iota(jnp.int32, (width, width), 0) >= lax.broadcasted_iota(
        jnp.int32, (width, width), 1
    )
    spread = jnp.where(lower[None], exponent[:, :, None] - exponent[:, None, :], -jnp.inf)
    gram = jnp.dot(c_rows, b_rows.T, preferred_element_type=jnp.float32)
    mixing = (jnp.exp(spread) * gram[None] * steps[:, None, :]).astype(jnp.bfloat16)
    local = jnp.einsum("hts,shp->thp", mixing, inputs, preferred_element_type=jnp.float32)
    carried = jnp.einsum(
        "tn,hpn->thp", c_rows.astype(jnp.float32), state, precision=lax.Precision.HIGHEST
    )
    output = local + carried * jnp.exp(exponent).T[:, :, None]
    last = exponent[:, -1]
    weighted = (
        inputs.astype(jnp.float32) * (jnp.exp(last[:, None] - exponent) * steps).T[:, :, None]
    ).astype(jnp.bfloat16)
    fresh = jnp.einsum("thp,tn->hpn", weighted, b_rows, preferred_element_type=jnp.float32)
    return (output, jnp.exp(last)[:, None, None] * state + fresh, exponent)


def sequence_pass(inputs, steps, b_rows, c_rows, rates):
    window_extent = inputs.shape[0]
    heads = steps.shape[0]
    blocks = window_extent // QS
    xs = inputs.reshape(blocks, QS, heads, SP)
    ss = steps.reshape(heads, blocks, QS).transpose(1, 0, 2)
    bs = b_rows.reshape(blocks, QS, NST)
    cs = c_rows.reshape(blocks, QS, NST)

    def advance(carry, block):
        state, offset = carry
        out, state_next, exponent = block_pass(block[0], block[1], block[2], block[3], rates, state)
        return ((state_next, offset + exponent[:, -1]), (out, offset[:, None] + exponent))

    start = (jnp.zeros((heads, SP, NST), jnp.float32), jnp.zeros((heads,), jnp.float32))
    (final, total), (outs, decays_to) = lax.scan(advance, start, (xs, ss, bs, cs))
    decays_to = decays_to.transpose(1, 0, 2).reshape(heads, window_extent)
    return (outs.reshape(window_extent, heads, SP), final, decays_to, total)


def chunked_pass(inputs, steps, b_rows, c_rows, rates):
    window_extent = inputs.shape[0]
    heads = steps.shape[0]
    blocks = window_extent // QS
    xs = inputs.reshape(blocks, QS, heads, SP).transpose(0, 2, 1, 3)
    ss = steps.reshape(heads, blocks, QS).transpose(1, 0, 2)
    bs = b_rows.reshape(blocks, QS, NST)
    cs = c_rows.reshape(blocks, QS, NST)
    exponent = jnp.cumsum(-ss * rates[None, :, None], axis=2)
    lower = lax.broadcasted_iota(jnp.int32, (QS, QS), 0) >= lax.broadcasted_iota(
        jnp.int32, (QS, QS), 1
    )
    spread = jnp.where(
        lower[None, None], exponent[:, :, :, None] - exponent[:, :, None, :], -jnp.inf
    )
    gram = jnp.einsum("ctn,cun->ctu", cs, bs, preferred_element_type=jnp.float32)
    mixing = (jnp.exp(spread) * gram[:, None] * ss[:, :, None, :]).astype(jnp.bfloat16)
    local = jnp.einsum("chtu,chup->chtp", mixing, xs, preferred_element_type=jnp.float32)
    last = exponent[:, :, -1]
    weighted = (
        xs.astype(jnp.float32) * (jnp.exp(last[:, :, None] - exponent) * ss)[:, :, :, None]
    ).astype(jnp.bfloat16)
    fresh = jnp.einsum("chup,cun->chpn", weighted, bs, preferred_element_type=jnp.float32)
    decay = jnp.exp(last)
    state = jnp.zeros((heads, SP, NST), jnp.float32)
    offset = jnp.zeros((heads,), jnp.float32)
    befores = []
    offsets = []
    for index in range(blocks):
        befores.append(state)
        offsets.append(offset)
        state = decay[index][:, None, None] * state + fresh[index]
        offset = offset + last[index]
    before = jnp.stack(befores)
    carried = jnp.einsum(
        "ctn,chpn->chtp", cs.astype(jnp.float32), before, precision=lax.Precision.HIGHEST
    )
    output = local + carried * jnp.exp(exponent)[:, :, :, None]
    decays_to = jnp.stack(offsets)[:, :, None] + exponent
    output = output.transpose(0, 2, 1, 3).reshape(window_extent, heads, SP)
    decays_to = decays_to.transpose(1, 0, 2).reshape(heads, window_extent)
    return (output, state, decays_to, offset)


def head_norm(values):
    scale = lax.rsqrt(jnp.mean(values * values, axis=-1, keepdims=True) + EPS)
    return (values * scale).reshape(values.shape[0], -1)


def linkage_merge(earlier, later):
    return (earlier[0] * later[0], later[0][:, :, None, None] * earlier[1] + later[1])


def body(
    prompt_keys,
    prompt_values,
    resp_query,
    resp_keys,
    resp_values,
    prompt_x,
    prompt_dt,
    prompt_b,
    prompt_c,
    resp_x,
    resp_dt,
    resp_b,
    resp_c,
    ssm_rate,
    resp_group,
    resp_len,
):
    seq_index = lax.axis_index("seq")
    resp_index = lax.axis_index("resp")
    seq_count = lax.axis_size("seq")
    prompt_count = prompt_x.shape[0]
    prompt_heads = prompt_dt.shape[1]
    resp_heads = resp_dt.shape[1]
    responses_here = resp_x.shape[0]
    slots = resp_x.shape[1]
    memory_head_number = prompt_keys.shape[2] // HDIM
    repeat = seq_count // memory_head_number
    shard_rows = prompt_keys.shape[1]
    spread_keys = jnp.repeat(
        prompt_keys.reshape(prompt_count, shard_rows, memory_head_number, HDIM), repeat, axis=2
    ).reshape(prompt_count, shard_rows, seq_count * HDIM)
    spread_values = jnp.repeat(
        prompt_values.reshape(prompt_count, shard_rows, memory_head_number, HDIM), repeat, axis=2
    ).reshape(prompt_count, shard_rows, seq_count * HDIM)
    moved_keys, moved_values = (
        lax.all_to_all(spread_keys, "seq", split_axis=2, concat_axis=1, tiled=True),
        lax.all_to_all(spread_values, "seq", split_axis=2, concat_axis=1, tiled=True),
    )
    resp_rates = lax.dynamic_slice_in_dim(ssm_rate, seq_index * resp_heads, resp_heads)
    resp_locals = []
    for item in range(responses_here):
        resp_locals.append(
            chunked_pass(resp_x[item], resp_dt[item], resp_b[item], resp_c[item], resp_rates)
        )
    prompt_rates = lax.dynamic_slice_in_dim(ssm_rate, resp_index * prompt_heads, prompt_heads)
    local_outs = []
    local_states = []
    prompt_decays = []
    log_totals = []
    for prompt in range(prompt_count):
        out, final, decays_to, total = sequence_pass(
            prompt_x[prompt], prompt_dt[prompt], prompt_b[prompt], prompt_c[prompt], prompt_rates
        )
        local_outs.append(out)
        local_states.append(final)
        prompt_decays.append(decays_to)
        log_totals.append(total)
    local_state = jnp.stack(local_states)
    decay_total = jnp.exp(jnp.stack(log_totals))
    gathered_states = lax.all_gather(local_state, "seq")
    slot = lax.broadcasted_iota(jnp.int32, (seq_count,) + decay_total.shape, 0)
    gathered_decays = lax.psum(jnp.where(slot == seq_index, decay_total[None], 0.0), "seq")
    heads_here = resp_query.shape[2] // HDIM
    own_head = seq_index // repeat
    resp_attn_out = response_attention(
        resp_query, moved_keys, moved_values, resp_keys, resp_values, resp_group, resp_len, own_head
    )
    gathered_states, resp_attn_out = lax.optimization_barrier((gathered_states, resp_attn_out))
    shard = lax.broadcasted_iota(jnp.int32, (seq_count, seq_count), 0)
    later = lax.broadcasted_iota(jnp.int32, (seq_count, seq_count), 1)
    between = (later > shard) & (later < seq_index)
    after = later > shard
    factors = gathered_decays[None]
    before_weights = jnp.prod(jnp.where(between[:, :, None, None], factors, 1.0), axis=1)
    before_weights = jnp.where((shard[:, 0] < seq_index)[:, None, None], before_weights, 0.0)
    final_weights = jnp.prod(jnp.where(after[:, :, None, None], factors, 1.0), axis=1)
    arriving_state = jnp.sum(before_weights[:, :, :, None, None] * gathered_states, axis=0)
    inclusive = jnp.sum(final_weights[:, :, :, None, None] * gathered_states, axis=0)
    prompt_outs = []
    for prompt in range(prompt_count):
        carried = jnp.einsum(
            "tn,hdn->thd",
            prompt_c[prompt].astype(jnp.float32),
            arriving_state[prompt],
            precision=lax.Precision.HIGHEST,
        )
        corrected = local_outs[prompt] + jnp.exp(prompt_decays[prompt]).T[:, :, None] * carried
        prompt_outs.append(head_norm(corrected).astype(jnp.bfloat16))
    prompt_ssm_out = jnp.stack(prompt_outs)
    finals = inclusive
    ratio = seq_count // lax.axis_size("resp")
    piece = lax.dynamic_slice_in_dim(finals, seq_index % ratio * resp_heads, resp_heads, 1)
    start_states = broadcast(piece, "resp", seq_index // ratio)
    positions = lax.broadcasted_iota(jnp.int32, (slots,), 0)
    resp_outs = []
    for item in range(responses_here):
        out, final, decays_to, total = resp_locals[item]
        initial = lax.dynamic_index_in_dim(start_states, resp_group[item], 0, keepdims=False)
        carried = jnp.einsum(
            "tn,hdn->thd",
            resp_c[item].astype(jnp.float32),
            initial,
            precision=lax.Precision.HIGHEST,
        )
        corrected = out + jnp.exp(decays_to).T[:, :, None] * carried
        valid = positions < resp_len[item]
        resp_outs.append(jnp.where(valid[:, None], head_norm(corrected), 0.0).astype(jnp.bfloat16))
    resp_ssm_out = jnp.stack(resp_outs)
    return (resp_attn_out, resp_ssm_out, prompt_ssm_out)


ROWS = 512

def response_attention(resp_query, prompt_keys, prompt_values, resp_keys, resp_values, group, length, head):
    items, slots, width = resp_query.shape
    heads = width // HDIM
    rows = slots * heads
    queries = resp_query.reshape(items, rows, HDIM)
    prompt_len = prompt_keys.shape[1]
    tile = min(ROWS, rows)
    scale = 1.0 / math.sqrt(HDIM)

    def kernel(group_ref, len_ref, head_ref, q_ref, pk_ref, pv_ref, rk_ref, rv_ref, o_ref):
        item = pl.program_id(0)
        block = pl.program_id(1)
        window_extent = len_ref[item]
        first = block * (tile // heads)

        @pl.when(first >= window_extent)
        def _():
            o_ref[...] = jnp.zeros_like(o_ref)

        @pl.when(first < window_extent)
        def _():
            q = q_ref[0]
            dims = (((1,), (1,)), ((), ()))
            s1 = lax.dot_general(q, pk_ref[0], dims, preferred_element_type=jnp.float32) * scale
            s2 = lax.dot_general(q, rk_ref[0], dims, preferred_element_type=jnp.float32) * scale
            position = first + lax.broadcasted_iota(jnp.int32, (tile, 1), 0) // heads
            column = lax.broadcasted_iota(jnp.int32, s2.shape, 1)
            s2 = jnp.where(column <= position, s2, -jnp.inf)
            top = jnp.maximum(
                jnp.max(s1, axis=1, keepdims=True), jnp.max(s2, axis=1, keepdims=True)
            )
            e1 = jnp.exp(s1 - top)
            e2 = jnp.exp(s2 - top)
            total = jnp.sum(e1, axis=1, keepdims=True) + jnp.sum(e2, axis=1, keepdims=True)
            mixed = jnp.dot(
                e1.astype(jnp.bfloat16), pv_ref[0], preferred_element_type=jnp.float32
            ) + jnp.dot(e2.astype(jnp.bfloat16), rv_ref[0], preferred_element_type=jnp.float32)
            mixed = mixed / total
            o_ref[0] = jnp.where(position < window_extent, mixed, 0.0).astype(o_ref.dtype)

    keys_total = prompt_len + slots
    cost = pl.CostEstimate(
        flops=4 * items * rows * keys_total * HDIM,
        transcendentals=items * rows * keys_total,
        bytes_accessed=2 * (2 * items * rows * HDIM + 2 * items * keys_total * HDIM),
    )
    grid_spec = pltpu.PrefetchScalarGridSpec(
        num_scalar_prefetch=3,
        grid=(items, rows // tile),
        in_specs=[
            pl.BlockSpec((1, tile, HDIM), lambda i, b, g, n, h: (i, b, 0)),
            pl.BlockSpec((1, prompt_len, HDIM), lambda i, b, g, n, h: (g[i], 0, 0)),
            pl.BlockSpec((1, prompt_len, HDIM), lambda i, b, g, n, h: (g[i], 0, 0)),
            pl.BlockSpec((1, slots, HDIM), lambda i, b, g, n, h: (i, 0, h[0])),
            pl.BlockSpec((1, slots, HDIM), lambda i, b, g, n, h: (i, 0, h[0])),
        ],
        out_specs=pl.BlockSpec((1, tile, HDIM), lambda i, b, g, n, h: (i, b, 0)),
    )
    out = pl.pallas_call(
        kernel,
        grid_spec=grid_spec,
        out_shape=jax.ShapeDtypeStruct((items, rows, HDIM), jnp.bfloat16),
        compiler_params=pltpu.CompilerParams(vmem_limit_bytes=60 * 1024 * 1024),
        cost_estimate=cost,
    )(group.astype(jnp.int32), length.astype(jnp.int32), jnp.reshape(head, (1,)).astype(jnp.int32),
      queries, prompt_keys, prompt_values, resp_keys, resp_values)
    return out.reshape(items, slots, width)


def solution(mesh):
    placed = (
        P(None, "seq", None),
        P(None, "seq", None),
        P("resp", None, "seq"),
        P("resp", None, None),
        P("resp", None, None),
        P(None, "seq", "resp"),
        P(None, "resp", "seq"),
        P(None, "seq", None),
        P(None, "seq", None),
        P("resp", None, "seq"),
        P("resp", "seq", None),
        P("resp", None, None),
        P("resp", None, None),
        P(),
        P("resp"),
        P("resp"),
    )
    return jax.shard_map(
        body,
        mesh=mesh,
        in_specs=placed,
        out_specs=(P("resp", None, "seq"), P("resp", None, "seq"), P(None, "seq", "resp")),
        check_vma=False,
    )
```

```python
import math

import jax
import jax.numpy as jnp
from jax import lax
from jax.experimental import pallas as pl
from jax.experimental.pallas import tpu as pltpu
from jax.sharding import PartitionSpec as P

HDIM = 128
SP = 64
NST = 128
QS = 128


EPS = 1e-05


def from_behind(block, axis, distance):
    devices = range(lax.axis_size(axis))
    route = [(i - distance, i) for i in devices if i - distance in devices]
    return lax.ppermute(block, axis, route)


def broadcast(value, axis, source):
    kept = jnp.where(lax.axis_index(axis) == source, value, 0).astype(value.dtype)
    return lax.psum(kept, axis)


def block_pass(inputs, steps, b_rows, c_rows, rates, state):
    exponent = jnp.cumsum(-steps * rates[:, None], axis=1)
    width = inputs.shape[0]
    lower = lax.broadcasted_iota(jnp.int32, (width, width), 0) >= lax.broadcasted_iota(
        jnp.int32, (width, width), 1
    )
    spread = jnp.where(lower[None], exponent[:, :, None] - exponent[:, None, :], -jnp.inf)
    gram = jnp.dot(c_rows, b_rows.T, preferred_element_type=jnp.float32)
    mixing = (jnp.exp(spread) * gram[None] * steps[:, None, :]).astype(jnp.bfloat16)
    local = jnp.einsum("hts,shp->thp", mixing, inputs, preferred_element_type=jnp.float32)
    carried = jnp.einsum(
        "tn,hpn->thp", c_rows.astype(jnp.float32), state, precision=lax.Precision.HIGHEST
    )
    output = local + carried * jnp.exp(exponent).T[:, :, None]
    last = exponent[:, -1]
    weighted = (
        inputs.astype(jnp.float32) * (jnp.exp(last[:, None] - exponent) * steps).T[:, :, None]
    ).astype(jnp.bfloat16)
    fresh = jnp.einsum("thp,tn->hpn", weighted, b_rows, preferred_element_type=jnp.float32)
    return (output, jnp.exp(last)[:, None, None] * state + fresh, exponent)


def sequence_pass(inputs, steps, b_rows, c_rows, rates):
    window_extent = inputs.shape[0]
    heads = steps.shape[0]
    blocks = window_extent // QS
    xs = inputs.reshape(blocks, QS, heads, SP)
    ss = steps.reshape(heads, blocks, QS).transpose(1, 0, 2)
    bs = b_rows.reshape(blocks, QS, NST)
    cs = c_rows.reshape(blocks, QS, NST)

    def advance(carry, block):
        state, offset = carry
        out, state_next, exponent = block_pass(block[0], block[1], block[2], block[3], rates, state)
        return ((state_next, offset + exponent[:, -1]), (out, offset[:, None] + exponent))

    start = (jnp.zeros((heads, SP, NST), jnp.float32), jnp.zeros((heads,), jnp.float32))
    (final, total), (outs, decays_to) = lax.scan(advance, start, (xs, ss, bs, cs))
    decays_to = decays_to.transpose(1, 0, 2).reshape(heads, window_extent)
    return (outs.reshape(window_extent, heads, SP), final, decays_to, total)


def chunked_pass(inputs, steps, b_rows, c_rows, rates):
    window_extent = inputs.shape[0]
    heads = steps.shape[0]
    blocks = window_extent // QS
    xs = inputs.reshape(blocks, QS, heads, SP).transpose(0, 2, 1, 3)
    ss = steps.reshape(heads, blocks, QS).transpose(1, 0, 2)
    bs = b_rows.reshape(blocks, QS, NST)
    cs = c_rows.reshape(blocks, QS, NST)
    exponent = jnp.cumsum(-ss * rates[None, :, None], axis=2)
    lower = lax.broadcasted_iota(jnp.int32, (QS, QS), 0) >= lax.broadcasted_iota(
        jnp.int32, (QS, QS), 1
    )
    spread = jnp.where(
        lower[None, None], exponent[:, :, :, None] - exponent[:, :, None, :], -jnp.inf
    )
    gram = jnp.einsum("ctn,cun->ctu", cs, bs, preferred_element_type=jnp.float32)
    mixing = (jnp.exp(spread) * gram[:, None] * ss[:, :, None, :]).astype(jnp.bfloat16)
    local = jnp.einsum("chtu,chup->chtp", mixing, xs, preferred_element_type=jnp.float32)
    last = exponent[:, :, -1]
    weighted = (
        xs.astype(jnp.float32) * (jnp.exp(last[:, :, None] - exponent) * ss)[:, :, :, None]
    ).astype(jnp.bfloat16)
    fresh = jnp.einsum("chup,cun->chpn", weighted, bs, preferred_element_type=jnp.float32)
    decay = jnp.exp(last)
    state = jnp.zeros((heads, SP, NST), jnp.float32)
    offset = jnp.zeros((heads,), jnp.float32)
    befores = []
    offsets = []
    for index in range(blocks):
        befores.append(state)
        offsets.append(offset)
        state = decay[index][:, None, None] * state + fresh[index]
        offset = offset + last[index]
    before = jnp.stack(befores)
    carried = jnp.einsum(
        "ctn,chpn->chtp", cs.astype(jnp.float32), before, precision=lax.Precision.HIGHEST
    )
    output = local + carried * jnp.exp(exponent)[:, :, :, None]
    decays_to = jnp.stack(offsets)[:, :, None] + exponent
    output = output.transpose(0, 2, 1, 3).reshape(window_extent, heads, SP)
    decays_to = decays_to.transpose(1, 0, 2).reshape(heads, window_extent)
    return (output, state, decays_to, offset)


def head_norm(values):
    scale = lax.rsqrt(jnp.mean(values * values, axis=-1, keepdims=True) + EPS)
    return (values * scale).reshape(values.shape[0], -1)


def linkage_merge(earlier, later):
    return (earlier[0] * later[0], later[0][:, :, None, None] * earlier[1] + later[1])


def body(
    prompt_keys,
    prompt_values,
    resp_query,
    resp_keys,
    resp_values,
    prompt_x,
    prompt_dt,
    prompt_b,
    prompt_c,
    resp_x,
    resp_dt,
    resp_b,
    resp_c,
    ssm_rate,
    resp_group,
    resp_len,
):
    seq_index = lax.axis_index("seq")
    resp_index = lax.axis_index("resp")
    seq_count = lax.axis_size("seq")
    prompt_count = prompt_x.shape[0]
    prompt_heads = prompt_dt.shape[1]
    resp_heads = resp_dt.shape[1]
    responses_here = resp_x.shape[0]
    slots = resp_x.shape[1]
    memory_head_number = prompt_keys.shape[2] // HDIM
    repeat = seq_count // memory_head_number
    shard_rows = prompt_keys.shape[1]
    spread_keys = jnp.repeat(
        prompt_keys.reshape(prompt_count, shard_rows, memory_head_number, HDIM), repeat, axis=2
    ).reshape(prompt_count, shard_rows, seq_count * HDIM)
    spread_values = jnp.repeat(
        prompt_values.reshape(prompt_count, shard_rows, memory_head_number, HDIM), repeat, axis=2
    ).reshape(prompt_count, shard_rows, seq_count * HDIM)
    moved_keys, moved_values = (
        lax.all_to_all(spread_keys, "seq", split_axis=2, concat_axis=1, tiled=True),
        lax.all_to_all(spread_values, "seq", split_axis=2, concat_axis=1, tiled=True),
    )
    resp_rates = lax.dynamic_slice_in_dim(ssm_rate, seq_index * resp_heads, resp_heads)
    resp_locals = []
    for item in range(responses_here):
        resp_locals.append(
            chunked_pass(resp_x[item], resp_dt[item], resp_b[item], resp_c[item], resp_rates)
        )
    heads_per_chain = prompt_heads // seq_count
    chain_x = lax.all_to_all(prompt_x, "seq", split_axis=2, concat_axis=1, tiled=True)
    chain_dt = lax.all_to_all(prompt_dt, "seq", split_axis=1, concat_axis=2, tiled=True)
    chain_b = lax.all_gather(prompt_b, "seq", axis=1, tiled=True)
    chain_c = lax.all_gather(prompt_c, "seq", axis=1, tiled=True)
    chain_rates = lax.dynamic_slice_in_dim(
        ssm_rate, resp_index * prompt_heads + seq_index * heads_per_chain, heads_per_chain
    )
    chain_outs = []
    chain_finals = []
    for prompt in range(prompt_count):
        out, final, decays_to, total = chunked_pass(
            chain_x[prompt], chain_dt[prompt], chain_b[prompt], chain_c[prompt], chain_rates
        )
        chain_outs.append(head_norm(out).astype(jnp.bfloat16))
        chain_finals.append(final)
    prompt_ssm_out = lax.all_to_all(
        jnp.stack(chain_outs), "seq", split_axis=1, concat_axis=2, tiled=True
    )
    finals = lax.all_gather(jnp.stack(chain_finals), "seq", axis=1, tiled=True)
    heads_here = resp_query.shape[2] // HDIM
    own_head = seq_index // repeat
    resp_attn_out = response_attention(
        resp_query, moved_keys, moved_values, resp_keys, resp_values, resp_group, resp_len, own_head
    )
    ratio = seq_count // lax.axis_size("resp")
    piece = lax.dynamic_slice_in_dim(finals, seq_index % ratio * resp_heads, resp_heads, 1)
    start_states = broadcast(piece, "resp", seq_index // ratio)
    positions = lax.broadcasted_iota(jnp.int32, (slots,), 0)
    resp_outs = []
    for item in range(responses_here):
        out, final, decays_to, total = resp_locals[item]
        initial = lax.dynamic_index_in_dim(start_states, resp_group[item], 0, keepdims=False)
        carried = jnp.einsum(
            "tn,hdn->thd",
            resp_c[item].astype(jnp.float32),
            initial,
            precision=lax.Precision.HIGHEST,
        )
        corrected = out + jnp.exp(decays_to).T[:, :, None] * carried
        valid = positions < resp_len[item]
        resp_outs.append(jnp.where(valid[:, None], head_norm(corrected), 0.0).astype(jnp.bfloat16))
    resp_ssm_out = jnp.stack(resp_outs)
    return (resp_attn_out, resp_ssm_out, prompt_ssm_out)


ROWS = 512

def response_attention(resp_query, prompt_keys, prompt_values, resp_keys, resp_values, group, length, head):
    items, slots, width = resp_query.shape
    heads = width // HDIM
    rows = slots * heads
    queries = resp_query.reshape(items, rows, HDIM)
    prompt_len = prompt_keys.shape[1]
    tile = min(ROWS, rows)
    scale = 1.0 / math.sqrt(HDIM)

    def kernel(group_ref, len_ref, head_ref, q_ref, pk_ref, pv_ref, rk_ref, rv_ref, o_ref):
        item = pl.program_id(0)
        block = pl.program_id(1)
        window_extent = len_ref[item]
        first = block * (tile // heads)

        @pl.when(first >= window_extent)
        def _():
            o_ref[...] = jnp.zeros_like(o_ref)

        @pl.when(first < window_extent)
        def _():
            q = q_ref[0]
            dims = (((1,), (1,)), ((), ()))
            s1 = lax.dot_general(q, pk_ref[0], dims, preferred_element_type=jnp.float32) * scale
            s2 = lax.dot_general(q, rk_ref[0], dims, preferred_element_type=jnp.float32) * scale
            position = first + lax.broadcasted_iota(jnp.int32, (tile, 1), 0) // heads
            column = lax.broadcasted_iota(jnp.int32, s2.shape, 1)
            s2 = jnp.where(column <= position, s2, -jnp.inf)
            top = jnp.maximum(
                jnp.max(s1, axis=1, keepdims=True), jnp.max(s2, axis=1, keepdims=True)
            )
            e1 = jnp.exp(s1 - top)
            e2 = jnp.exp(s2 - top)
            total = jnp.sum(e1, axis=1, keepdims=True) + jnp.sum(e2, axis=1, keepdims=True)
            mixed = jnp.dot(
                e1.astype(jnp.bfloat16), pv_ref[0], preferred_element_type=jnp.float32
            ) + jnp.dot(e2.astype(jnp.bfloat16), rv_ref[0], preferred_element_type=jnp.float32)
            mixed = mixed / total
            o_ref[0] = jnp.where(position < window_extent, mixed, 0.0).astype(o_ref.dtype)

    keys_total = prompt_len + slots
    cost = pl.CostEstimate(
        flops=4 * items * rows * keys_total * HDIM,
        transcendentals=items * rows * keys_total,
        bytes_accessed=2 * (2 * items * rows * HDIM + 2 * items * keys_total * HDIM),
    )
    grid_spec = pltpu.PrefetchScalarGridSpec(
        num_scalar_prefetch=3,
        grid=(items, rows // tile),
        in_specs=[
            pl.BlockSpec((1, tile, HDIM), lambda i, b, g, n, h: (i, b, 0)),
            pl.BlockSpec((1, prompt_len, HDIM), lambda i, b, g, n, h: (g[i], 0, 0)),
            pl.BlockSpec((1, prompt_len, HDIM), lambda i, b, g, n, h: (g[i], 0, 0)),
            pl.BlockSpec((1, slots, HDIM), lambda i, b, g, n, h: (i, 0, h[0])),
            pl.BlockSpec((1, slots, HDIM), lambda i, b, g, n, h: (i, 0, h[0])),
        ],
        out_specs=pl.BlockSpec((1, tile, HDIM), lambda i, b, g, n, h: (i, b, 0)),
    )
    out = pl.pallas_call(
        kernel,
        grid_spec=grid_spec,
        out_shape=jax.ShapeDtypeStruct((items, rows, HDIM), jnp.bfloat16),
        compiler_params=pltpu.CompilerParams(vmem_limit_bytes=60 * 1024 * 1024),
        cost_estimate=cost,
    )(group.astype(jnp.int32), length.astype(jnp.int32), jnp.reshape(head, (1,)).astype(jnp.int32),
      queries, prompt_keys, prompt_values, resp_keys, resp_values)
    return out.reshape(items, slots, width)


def solution(mesh):
    placed = (
        P(None, "seq", None),
        P(None, "seq", None),
        P("resp", None, "seq"),
        P("resp", None, None),
        P("resp", None, None),
        P(None, "seq", "resp"),
        P(None, "resp", "seq"),
        P(None, "seq", None),
        P(None, "seq", None),
        P("resp", None, "seq"),
        P("resp", "seq", None),
        P("resp", None, None),
        P("resp", None, None),
        P(),
        P("resp"),
        P("resp"),
    )
    return jax.shard_map(
        body,
        mesh=mesh,
        in_specs=placed,
        out_specs=(P("resp", None, "seq"), P("resp", None, "seq"), P(None, "seq", "resp")),
        check_vma=False,
    )
```

```python
import math

import jax
import jax.numpy as jnp
from jax import lax
from jax.experimental import pallas as pl
from jax.experimental.pallas import tpu as pltpu
from jax.sharding import PartitionSpec as P

HDIM = 128
SP = 64
NST = 128
QS = 128


EPS = 1e-05


def from_behind(block, axis, distance):
    devices = range(lax.axis_size(axis))
    route = [(i - distance, i) for i in devices if i - distance in devices]
    return lax.ppermute(block, axis, route)


def broadcast(value, axis, source):
    kept = jnp.where(lax.axis_index(axis) == source, value, 0).astype(value.dtype)
    return lax.psum(kept, axis)


def block_pass(inputs, steps, b_rows, c_rows, rates, state):
    exponent = jnp.cumsum(-steps * rates[:, None], axis=1)
    width = inputs.shape[0]
    lower = lax.broadcasted_iota(jnp.int32, (width, width), 0) >= lax.broadcasted_iota(
        jnp.int32, (width, width), 1
    )
    spread = jnp.where(lower[None], exponent[:, :, None] - exponent[:, None, :], -jnp.inf)
    gram = jnp.dot(c_rows, b_rows.T, preferred_element_type=jnp.float32)
    mixing = (jnp.exp(spread) * gram[None] * steps[:, None, :]).astype(jnp.bfloat16)
    local = jnp.einsum("hts,shp->thp", mixing, inputs, preferred_element_type=jnp.float32)
    carried = jnp.einsum(
        "tn,hpn->thp", c_rows.astype(jnp.float32), state, precision=lax.Precision.HIGHEST
    )
    output = local + carried * jnp.exp(exponent).T[:, :, None]
    last = exponent[:, -1]
    weighted = (
        inputs.astype(jnp.float32) * (jnp.exp(last[:, None] - exponent) * steps).T[:, :, None]
    ).astype(jnp.bfloat16)
    fresh = jnp.einsum("thp,tn->hpn", weighted, b_rows, preferred_element_type=jnp.float32)
    return (output, jnp.exp(last)[:, None, None] * state + fresh, exponent)


def sequence_pass(inputs, steps, b_rows, c_rows, rates):
    window_extent = inputs.shape[0]
    heads = steps.shape[0]
    blocks = window_extent // QS
    xs = inputs.reshape(blocks, QS, heads, SP)
    ss = steps.reshape(heads, blocks, QS).transpose(1, 0, 2)
    bs = b_rows.reshape(blocks, QS, NST)
    cs = c_rows.reshape(blocks, QS, NST)

    def advance(carry, block):
        state, offset = carry
        out, state_next, exponent = block_pass(block[0], block[1], block[2], block[3], rates, state)
        return ((state_next, offset + exponent[:, -1]), (out, offset[:, None] + exponent))

    start = (jnp.zeros((heads, SP, NST), jnp.float32), jnp.zeros((heads,), jnp.float32))
    (final, total), (outs, decays_to) = lax.scan(advance, start, (xs, ss, bs, cs))
    decays_to = decays_to.transpose(1, 0, 2).reshape(heads, window_extent)
    return (outs.reshape(window_extent, heads, SP), final, decays_to, total)


def chunked_pass(inputs, steps, b_rows, c_rows, rates):
    window_extent = inputs.shape[0]
    heads = steps.shape[0]
    blocks = window_extent // QS
    xs = inputs.reshape(blocks, QS, heads, SP)
    ss = steps.reshape(heads, blocks, QS).transpose(1, 0, 2)
    bs = b_rows.reshape(blocks, QS, NST)
    cs = c_rows.reshape(blocks, QS, NST)
    exponent = jnp.cumsum(-ss * rates[None, :, None], axis=2)
    lower = lax.broadcasted_iota(jnp.int32, (QS, QS), 0) >= lax.broadcasted_iota(
        jnp.int32, (QS, QS), 1
    )
    spread = jnp.where(
        lower[None, None], exponent[:, :, :, None] - exponent[:, :, None, :], -jnp.inf
    )
    gram = jnp.einsum("ctn,cun->ctu", cs, bs, preferred_element_type=jnp.float32)
    mixing = (jnp.exp(spread) * gram[:, None] * ss[:, :, None, :]).astype(jnp.bfloat16)
    local = jnp.einsum("chtu,cuhp->cthp", mixing, xs, preferred_element_type=jnp.float32)
    last = exponent[:, :, -1]
    scaled = (jnp.exp(last[:, :, None] - exponent) * ss).transpose(0, 2, 1)
    weighted = (xs.astype(jnp.float32) * scaled[:, :, :, None]).astype(jnp.bfloat16)
    fresh = jnp.einsum("cuhp,cun->chpn", weighted, bs, preferred_element_type=jnp.float32)
    decay = jnp.exp(last)
    target = lax.broadcasted_iota(jnp.int32, (blocks, blocks, blocks), 0)
    source = lax.broadcasted_iota(jnp.int32, (blocks, blocks, blocks), 1)
    middle = lax.broadcasted_iota(jnp.int32, (blocks, blocks, blocks), 2)
    inside = (middle > source) & (middle < target)
    weights = jnp.prod(jnp.where(inside[..., None], decay[None, None], 1.0), axis=2)
    weights = jnp.where((source[:, :, 0] < target[:, :, 0])[..., None], weights, 0.0)
    before = jnp.sum(weights[:, :, :, None, None] * fresh[None], axis=1)
    tail = jnp.prod(jnp.where((middle[0] > source[0])[..., None], decay[None], 1.0), axis=1)
    state = jnp.sum(tail[:, :, None, None] * fresh, axis=0)
    offsets = jnp.sum(
        jnp.where((source[:, :, 0] < target[:, :, 0])[..., None], last[None], 0.0), axis=1
    )
    offset = jnp.sum(last, axis=0)
    carried = jnp.einsum(
        "ctn,chpn->cthp", cs.astype(jnp.float32), before, precision=lax.Precision.HIGHEST
    )
    output = local + carried * jnp.exp(exponent).transpose(0, 2, 1)[:, :, :, None]
    decays_to = offsets[:, :, None] + exponent
    output = output.reshape(window_extent, heads, SP)
    decays_to = decays_to.transpose(1, 0, 2).reshape(heads, window_extent)
    return (output, state, decays_to, offset)


def head_norm(values):
    scale = lax.rsqrt(jnp.mean(values * values, axis=-1, keepdims=True) + EPS)
    return (values * scale).reshape(values.shape[0], -1)


def linkage_merge(earlier, later):
    return (earlier[0] * later[0], later[0][:, :, None, None] * earlier[1] + later[1])


def body(
    prompt_keys,
    prompt_values,
    resp_query,
    resp_keys,
    resp_values,
    prompt_x,
    prompt_dt,
    prompt_b,
    prompt_c,
    resp_x,
    resp_dt,
    resp_b,
    resp_c,
    ssm_rate,
    resp_group,
    resp_len,
):
    seq_index = lax.axis_index("seq")
    resp_index = lax.axis_index("resp")
    seq_count = lax.axis_size("seq")
    prompt_count = prompt_x.shape[0]
    prompt_heads = prompt_dt.shape[1]
    resp_heads = resp_dt.shape[1]
    responses_here = resp_x.shape[0]
    slots = resp_x.shape[1]
    memory_head_number = prompt_keys.shape[2] // HDIM
    repeat = seq_count // memory_head_number
    shard_rows = prompt_keys.shape[1]
    spread_keys = jnp.repeat(
        prompt_keys.reshape(prompt_count, shard_rows, memory_head_number, HDIM), repeat, axis=2
    ).reshape(prompt_count, shard_rows, seq_count * HDIM)
    spread_values = jnp.repeat(
        prompt_values.reshape(prompt_count, shard_rows, memory_head_number, HDIM), repeat, axis=2
    ).reshape(prompt_count, shard_rows, seq_count * HDIM)
    moved_keys, moved_values = (
        lax.all_to_all(spread_keys, "seq", split_axis=2, concat_axis=1, tiled=True),
        lax.all_to_all(spread_values, "seq", split_axis=2, concat_axis=1, tiled=True),
    )
    resp_rates = lax.dynamic_slice_in_dim(ssm_rate, seq_index * resp_heads, resp_heads)
    resp_locals = []
    for item in range(responses_here):
        resp_locals.append(
            chunked_pass(resp_x[item], resp_dt[item], resp_b[item], resp_c[item], resp_rates)
        )
    heads_per_chain = prompt_heads // seq_count
    chain_x = lax.all_to_all(prompt_x, "seq", split_axis=2, concat_axis=1, tiled=True)
    chain_dt = lax.all_to_all(prompt_dt, "seq", split_axis=1, concat_axis=2, tiled=True)
    chain_b = lax.all_gather(prompt_b, "seq", axis=1, tiled=True)
    chain_c = lax.all_gather(prompt_c, "seq", axis=1, tiled=True)
    chain_rates = lax.dynamic_slice_in_dim(
        ssm_rate, resp_index * prompt_heads + seq_index * heads_per_chain, heads_per_chain
    )
    chain_outs = []
    chain_finals = []
    for prompt in range(prompt_count):
        out, final, decays_to, total = chunked_pass(
            chain_x[prompt], chain_dt[prompt], chain_b[prompt], chain_c[prompt], chain_rates
        )
        chain_outs.append(head_norm(out).astype(jnp.bfloat16))
        chain_finals.append(final)
    prompt_ssm_out = lax.all_to_all(
        jnp.stack(chain_outs), "seq", split_axis=1, concat_axis=2, tiled=True
    )
    finals = lax.all_gather(jnp.stack(chain_finals), "seq", axis=1, tiled=True)
    heads_here = resp_query.shape[2] // HDIM
    own_head = seq_index // repeat
    resp_attn_out = response_attention(
        resp_query, moved_keys, moved_values, resp_keys, resp_values, resp_group, resp_len, own_head
    )
    ratio = seq_count // lax.axis_size("resp")
    piece = lax.dynamic_slice_in_dim(finals, seq_index % ratio * resp_heads, resp_heads, 1)
    start_states = broadcast(piece, "resp", seq_index // ratio)
    positions = lax.broadcasted_iota(jnp.int32, (slots,), 0)
    resp_outs = []
    for item in range(responses_here):
        out, final, decays_to, total = resp_locals[item]
        initial = lax.dynamic_index_in_dim(start_states, resp_group[item], 0, keepdims=False)
        carried = jnp.einsum(
            "tn,hdn->thd",
            resp_c[item].astype(jnp.float32),
            initial,
            precision=lax.Precision.HIGHEST,
        )
        corrected = out + jnp.exp(decays_to).T[:, :, None] * carried
        valid = positions < resp_len[item]
        resp_outs.append(jnp.where(valid[:, None], head_norm(corrected), 0.0).astype(jnp.bfloat16))
    resp_ssm_out = jnp.stack(resp_outs)
    return (resp_attn_out, resp_ssm_out, prompt_ssm_out)


ROWS = 512

def response_attention(resp_query, prompt_keys, prompt_values, resp_keys, resp_values, group, length, head):
    items, slots, width = resp_query.shape
    heads = width // HDIM
    rows = slots * heads
    queries = resp_query.reshape(items, rows, HDIM)
    prompt_len = prompt_keys.shape[1]
    tile = min(ROWS, rows)
    scale = 1.0 / math.sqrt(HDIM)

    def kernel(group_ref, len_ref, head_ref, q_ref, pk_ref, pv_ref, rk_ref, rv_ref, o_ref):
        item = pl.program_id(0)
        block = pl.program_id(1)
        window_extent = len_ref[item]
        first = block * (tile // heads)

        @pl.when(first >= window_extent)
        def _():
            o_ref[...] = jnp.zeros_like(o_ref)

        @pl.when(first < window_extent)
        def _():
            q = q_ref[0]
            dims = (((1,), (1,)), ((), ()))
            s1 = lax.dot_general(q, pk_ref[0], dims, preferred_element_type=jnp.float32) * scale
            s2 = lax.dot_general(q, rk_ref[0], dims, preferred_element_type=jnp.float32) * scale
            position = first + lax.broadcasted_iota(jnp.int32, (tile, 1), 0) // heads
            column = lax.broadcasted_iota(jnp.int32, s2.shape, 1)
            s2 = jnp.where(column <= position, s2, -jnp.inf)
            top = jnp.maximum(
                jnp.max(s1, axis=1, keepdims=True), jnp.max(s2, axis=1, keepdims=True)
            )
            e1 = jnp.exp(s1 - top)
            e2 = jnp.exp(s2 - top)
            total = jnp.sum(e1, axis=1, keepdims=True) + jnp.sum(e2, axis=1, keepdims=True)
            mixed = jnp.dot(
                e1.astype(jnp.bfloat16), pv_ref[0], preferred_element_type=jnp.float32
            ) + jnp.dot(e2.astype(jnp.bfloat16), rv_ref[0], preferred_element_type=jnp.float32)
            mixed = mixed / total
            o_ref[0] = jnp.where(position < window_extent, mixed, 0.0).astype(o_ref.dtype)

    keys_total = prompt_len + slots
    cost = pl.CostEstimate(
        flops=4 * items * rows * keys_total * HDIM,
        transcendentals=items * rows * keys_total,
        bytes_accessed=2 * (2 * items * rows * HDIM + 2 * items * keys_total * HDIM),
    )
    grid_spec = pltpu.PrefetchScalarGridSpec(
        num_scalar_prefetch=3,
        grid=(items, rows // tile),
        in_specs=[
            pl.BlockSpec((1, tile, HDIM), lambda i, b, g, n, h: (i, b, 0)),
            pl.BlockSpec((1, prompt_len, HDIM), lambda i, b, g, n, h: (g[i], 0, 0)),
            pl.BlockSpec((1, prompt_len, HDIM), lambda i, b, g, n, h: (g[i], 0, 0)),
            pl.BlockSpec((1, slots, HDIM), lambda i, b, g, n, h: (i, 0, h[0])),
            pl.BlockSpec((1, slots, HDIM), lambda i, b, g, n, h: (i, 0, h[0])),
        ],
        out_specs=pl.BlockSpec((1, tile, HDIM), lambda i, b, g, n, h: (i, b, 0)),
    )
    out = pl.pallas_call(
        kernel,
        grid_spec=grid_spec,
        out_shape=jax.ShapeDtypeStruct((items, rows, HDIM), jnp.bfloat16),
        compiler_params=pltpu.CompilerParams(vmem_limit_bytes=60 * 1024 * 1024),
        cost_estimate=cost,
    )(group.astype(jnp.int32), length.astype(jnp.int32), jnp.reshape(head, (1,)).astype(jnp.int32),
      queries, prompt_keys, prompt_values, resp_keys, resp_values)
    return out.reshape(items, slots, width)


def solution(mesh):
    placed = (
        P(None, "seq", None),
        P(None, "seq", None),
        P("resp", None, "seq"),
        P("resp", None, None),
        P("resp", None, None),
        P(None, "seq", "resp"),
        P(None, "resp", "seq"),
        P(None, "seq", None),
        P(None, "seq", None),
        P("resp", None, "seq"),
        P("resp", "seq", None),
        P("resp", None, None),
        P("resp", None, None),
        P(),
        P("resp"),
        P("resp"),
    )
    return jax.shard_map(
        body,
        mesh=mesh,
        in_specs=placed,
        out_specs=(P("resp", None, "seq"), P("resp", None, "seq"), P(None, "seq", "resp")),
        check_vma=False,
    )
```

```python
import math

import jax
import jax.numpy as jnp
from jax import lax
from jax.experimental import pallas as pl
from jax.experimental.pallas import tpu as pltpu
from jax.sharding import PartitionSpec as P

HDIM = 128
SP = 64
NST = 128
QS = 128


EPS = 1e-05


def from_behind(block, axis, distance):
    devices = range(lax.axis_size(axis))
    route = [(i - distance, i) for i in devices if i - distance in devices]
    return lax.ppermute(block, axis, route)


def broadcast(value, axis, source):
    kept = jnp.where(lax.axis_index(axis) == source, value, 0).astype(value.dtype)
    return lax.psum(kept, axis)


def block_pass(inputs, steps, b_rows, c_rows, rates, state):
    exponent = jnp.cumsum(-steps * rates[:, None], axis=1)
    width = inputs.shape[0]
    lower = lax.broadcasted_iota(jnp.int32, (width, width), 0) >= lax.broadcasted_iota(
        jnp.int32, (width, width), 1
    )
    spread = jnp.where(lower[None], exponent[:, :, None] - exponent[:, None, :], -jnp.inf)
    gram = jnp.dot(c_rows, b_rows.T, preferred_element_type=jnp.float32)
    mixing = (jnp.exp(spread) * gram[None] * steps[:, None, :]).astype(jnp.bfloat16)
    local = jnp.einsum("hts,shp->thp", mixing, inputs, preferred_element_type=jnp.float32)
    carried = jnp.einsum(
        "tn,hpn->thp", c_rows.astype(jnp.float32), state, precision=lax.Precision.HIGHEST
    )
    output = local + carried * jnp.exp(exponent).T[:, :, None]
    last = exponent[:, -1]
    weighted = (
        inputs.astype(jnp.float32) * (jnp.exp(last[:, None] - exponent) * steps).T[:, :, None]
    ).astype(jnp.bfloat16)
    fresh = jnp.einsum("thp,tn->hpn", weighted, b_rows, preferred_element_type=jnp.float32)
    return (output, jnp.exp(last)[:, None, None] * state + fresh, exponent)


def sequence_pass(inputs, steps, b_rows, c_rows, rates):
    window_extent = inputs.shape[0]
    heads = steps.shape[0]
    blocks = window_extent // QS
    xs = inputs.reshape(blocks, QS, heads, SP)
    ss = steps.reshape(heads, blocks, QS).transpose(1, 0, 2)
    bs = b_rows.reshape(blocks, QS, NST)
    cs = c_rows.reshape(blocks, QS, NST)

    def advance(carry, block):
        state, offset = carry
        out, state_next, exponent = block_pass(block[0], block[1], block[2], block[3], rates, state)
        return ((state_next, offset + exponent[:, -1]), (out, offset[:, None] + exponent))

    start = (jnp.zeros((heads, SP, NST), jnp.float32), jnp.zeros((heads,), jnp.float32))
    (final, total), (outs, decays_to) = lax.scan(advance, start, (xs, ss, bs, cs))
    decays_to = decays_to.transpose(1, 0, 2).reshape(heads, window_extent)
    return (outs.reshape(window_extent, heads, SP), final, decays_to, total)


def chunked_pass(inputs, steps, b_rows, c_rows, rates):
    window_extent = inputs.shape[0]
    heads = steps.shape[0]
    blocks = window_extent // QS
    xs = inputs.reshape(blocks, QS, heads, SP).transpose(0, 2, 1, 3)
    ss = steps.reshape(heads, blocks, QS).transpose(1, 0, 2)
    bs = b_rows.reshape(blocks, QS, NST)
    cs = c_rows.reshape(blocks, QS, NST)
    exponent = jnp.cumsum(-ss * rates[None, :, None], axis=2)
    lower = lax.broadcasted_iota(jnp.int32, (QS, QS), 0) >= lax.broadcasted_iota(
        jnp.int32, (QS, QS), 1
    )
    spread = jnp.where(
        lower[None, None], exponent[:, :, :, None] - exponent[:, :, None, :], -jnp.inf
    )
    gram = jnp.einsum("ctn,cun->ctu", cs, bs, preferred_element_type=jnp.float32)
    mixing = (jnp.exp(spread) * gram[:, None] * ss[:, :, None, :]).astype(jnp.bfloat16)
    local = jnp.einsum("chtu,chup->chtp", mixing, xs, preferred_element_type=jnp.float32)
    last = exponent[:, :, -1]
    weighted = (
        xs.astype(jnp.float32) * (jnp.exp(last[:, :, None] - exponent) * ss)[:, :, :, None]
    ).astype(jnp.bfloat16)
    fresh = jnp.einsum("chup,cun->chpn", weighted, bs, preferred_element_type=jnp.float32)
    decay = jnp.exp(last)
    state = jnp.zeros((heads, SP, NST), jnp.float32)
    offset = jnp.zeros((heads,), jnp.float32)
    befores = []
    offsets = []
    for index in range(blocks):
        befores.append(state)
        offsets.append(offset)
        state = decay[index][:, None, None] * state + fresh[index]
        offset = offset + last[index]
    before = jnp.stack(befores)
    carried = jnp.einsum(
        "ctn,chpn->chtp", cs.astype(jnp.float32), before, precision=lax.Precision.HIGHEST
    )
    output = local + carried * jnp.exp(exponent)[:, :, :, None]
    decays_to = jnp.stack(offsets)[:, :, None] + exponent
    output = output.transpose(0, 2, 1, 3).reshape(window_extent, heads, SP)
    decays_to = decays_to.transpose(1, 0, 2).reshape(heads, window_extent)
    return (output, state, decays_to, offset)


def head_norm(values):
    scale = lax.rsqrt(jnp.mean(values * values, axis=-1, keepdims=True) + EPS)
    return (values * scale).reshape(values.shape[0], -1)


def linkage_merge(earlier, later):
    return (earlier[0] * later[0], later[0][:, :, None, None] * earlier[1] + later[1])


def body(
    prompt_keys,
    prompt_values,
    resp_query,
    resp_keys,
    resp_values,
    prompt_x,
    prompt_dt,
    prompt_b,
    prompt_c,
    resp_x,
    resp_dt,
    resp_b,
    resp_c,
    ssm_rate,
    resp_group,
    resp_len,
):
    seq_index = lax.axis_index("seq")
    resp_index = lax.axis_index("resp")
    seq_count = lax.axis_size("seq")
    prompt_count = prompt_x.shape[0]
    prompt_heads = prompt_dt.shape[1]
    resp_heads = resp_dt.shape[1]
    responses_here = resp_x.shape[0]
    slots = resp_x.shape[1]
    memory_head_number = prompt_keys.shape[2] // HDIM
    repeat = seq_count // memory_head_number
    shard_rows = prompt_keys.shape[1]
    spread_keys = jnp.repeat(
        prompt_keys.reshape(prompt_count, shard_rows, memory_head_number, HDIM), repeat, axis=2
    ).reshape(prompt_count, shard_rows, seq_count * HDIM)
    spread_values = jnp.repeat(
        prompt_values.reshape(prompt_count, shard_rows, memory_head_number, HDIM), repeat, axis=2
    ).reshape(prompt_count, shard_rows, seq_count * HDIM)
    moved_keys, moved_values = (
        lax.all_to_all(spread_keys, "seq", split_axis=2, concat_axis=1, tiled=True),
        lax.all_to_all(spread_values, "seq", split_axis=2, concat_axis=1, tiled=True),
    )
    resp_rates = lax.dynamic_slice_in_dim(ssm_rate, seq_index * resp_heads, resp_heads)
    resp_locals = []
    for item in range(responses_here):
        resp_locals.append(
            chunked_pass(resp_x[item], resp_dt[item], resp_b[item], resp_c[item], resp_rates)
        )
    heads_per_chain = prompt_heads // seq_count
    chain_x = lax.all_to_all(prompt_x, "seq", split_axis=2, concat_axis=1, tiled=True)
    chain_dt = lax.all_to_all(prompt_dt, "seq", split_axis=1, concat_axis=2, tiled=True)
    chain_b = lax.all_gather(prompt_b, "seq", axis=1, tiled=True)
    chain_c = lax.all_gather(prompt_c, "seq", axis=1, tiled=True)
    chain_x, chain_dt, resp_locals = lax.optimization_barrier((chain_x, chain_dt, resp_locals))
    chain_rates = lax.dynamic_slice_in_dim(
        ssm_rate, resp_index * prompt_heads + seq_index * heads_per_chain, heads_per_chain
    )
    chain_outs = []
    chain_finals = []
    for prompt in range(prompt_count):
        out, final, decays_to, total = chunked_pass(
            chain_x[prompt], chain_dt[prompt], chain_b[prompt], chain_c[prompt], chain_rates
        )
        chain_outs.append(head_norm(out).astype(jnp.bfloat16))
        chain_finals.append(final)
    prompt_ssm_out = lax.all_to_all(
        jnp.stack(chain_outs), "seq", split_axis=1, concat_axis=2, tiled=True
    )
    chain_final, resp_query = lax.optimization_barrier((jnp.stack(chain_finals), resp_query))
    finals = lax.all_gather(chain_final, "seq", axis=1, tiled=True)
    own_head = seq_index // repeat
    attention_args = (moved_keys, moved_values, resp_keys, resp_values, resp_group, resp_len, own_head)
    first_out = response_attention(resp_query, *attention_args, 0)
    ratio = seq_count // lax.axis_size("resp")
    piece = lax.dynamic_slice_in_dim(finals, seq_index % ratio * resp_heads, resp_heads, 1)
    piece, first_out, resp_query = lax.optimization_barrier((piece, first_out, resp_query))
    start_states = broadcast(piece, "resp", seq_index // ratio)
    outs = [first_out]
    for item in range(1, responses_here):
        outs.append(response_attention(resp_query, *attention_args, item))
    start_states, outs = lax.optimization_barrier((start_states, outs))
    resp_attn_out = jnp.concatenate(outs, axis=0)
    positions = lax.broadcasted_iota(jnp.int32, (slots,), 0)
    resp_outs = []
    for item in range(responses_here):
        out, final, decays_to, total = resp_locals[item]
        initial = lax.dynamic_index_in_dim(start_states, resp_group[item], 0, keepdims=False)
        carried = jnp.einsum(
            "tn,hdn->thd",
            resp_c[item].astype(jnp.float32),
            initial,
            precision=lax.Precision.HIGHEST,
        )
        corrected = out + jnp.exp(decays_to).T[:, :, None] * carried
        valid = positions < resp_len[item]
        resp_outs.append(jnp.where(valid[:, None], head_norm(corrected), 0.0).astype(jnp.bfloat16))
    resp_ssm_out = jnp.stack(resp_outs)
    return (resp_attn_out, resp_ssm_out, prompt_ssm_out)


ROWS = 512

def response_attention(resp_query, prompt_keys, prompt_values, resp_keys, resp_values, group, length, head, which):
    _, slots, width = resp_query.shape
    items = 1
    heads = width // HDIM
    rows = slots * heads
    queries = resp_query.reshape(resp_query.shape[0], rows, HDIM)
    prompt_len = prompt_keys.shape[1]
    tile = min(ROWS, rows)
    scale = 1.0 / math.sqrt(HDIM)

    def kernel(group_ref, len_ref, head_ref, q_ref, pk_ref, pv_ref, rk_ref, rv_ref, o_ref):
        item = pl.program_id(0)
        block = pl.program_id(1)
        window_extent = len_ref[which + item]
        first = block * (tile // heads)

        @pl.when(first >= window_extent)
        def _():
            o_ref[...] = jnp.zeros_like(o_ref)

        @pl.when(first < window_extent)
        def _():
            q = q_ref[0]
            dims = (((1,), (1,)), ((), ()))
            s1 = lax.dot_general(q, pk_ref[0], dims, preferred_element_type=jnp.float32) * scale
            s2 = lax.dot_general(q, rk_ref[0], dims, preferred_element_type=jnp.float32) * scale
            position = first + lax.broadcasted_iota(jnp.int32, (tile, 1), 0) // heads
            column = lax.broadcasted_iota(jnp.int32, s2.shape, 1)
            s2 = jnp.where(column <= position, s2, -jnp.inf)
            top = jnp.maximum(
                jnp.max(s1, axis=1, keepdims=True), jnp.max(s2, axis=1, keepdims=True)
            )
            e1 = jnp.exp(s1 - top)
            e2 = jnp.exp(s2 - top)
            total = jnp.sum(e1, axis=1, keepdims=True) + jnp.sum(e2, axis=1, keepdims=True)
            mixed = jnp.dot(
                e1.astype(jnp.bfloat16), pv_ref[0], preferred_element_type=jnp.float32
            ) + jnp.dot(e2.astype(jnp.bfloat16), rv_ref[0], preferred_element_type=jnp.float32)
            mixed = mixed / total
            o_ref[0] = jnp.where(position < window_extent, mixed, 0.0).astype(o_ref.dtype)

    keys_total = prompt_len + slots
    cost = pl.CostEstimate(
        flops=4 * items * rows * keys_total * HDIM,
        transcendentals=items * rows * keys_total,
        bytes_accessed=2 * (2 * items * rows * HDIM + 2 * items * keys_total * HDIM),
    )
    grid_spec = pltpu.PrefetchScalarGridSpec(
        num_scalar_prefetch=3,
        grid=(items, rows // tile),
        in_specs=[
            pl.BlockSpec((1, tile, HDIM), lambda i, b, g, n, h: (which + i, b, 0)),
            pl.BlockSpec((1, prompt_len, HDIM), lambda i, b, g, n, h: (g[which + i], 0, 0)),
            pl.BlockSpec((1, prompt_len, HDIM), lambda i, b, g, n, h: (g[which + i], 0, 0)),
            pl.BlockSpec((1, slots, HDIM), lambda i, b, g, n, h: (which + i, 0, h[0])),
            pl.BlockSpec((1, slots, HDIM), lambda i, b, g, n, h: (which + i, 0, h[0])),
        ],
        out_specs=pl.BlockSpec((1, tile, HDIM), lambda i, b, g, n, h: (i, b, 0)),
    )
    out = pl.pallas_call(
        kernel,
        grid_spec=grid_spec,
        out_shape=jax.ShapeDtypeStruct((items, rows, HDIM), jnp.bfloat16),
        compiler_params=pltpu.CompilerParams(vmem_limit_bytes=60 * 1024 * 1024),
        cost_estimate=cost,
    )(group.astype(jnp.int32), length.astype(jnp.int32), jnp.reshape(head, (1,)).astype(jnp.int32),
      queries, prompt_keys, prompt_values, resp_keys, resp_values)
    return out.reshape(items, slots, width)


def solution(mesh):
    placed = (
        P(None, "seq", None),
        P(None, "seq", None),
        P("resp", None, "seq"),
        P("resp", None, None),
        P("resp", None, None),
        P(None, "seq", "resp"),
        P(None, "resp", "seq"),
        P(None, "seq", None),
        P(None, "seq", None),
        P("resp", None, "seq"),
        P("resp", "seq", None),
        P("resp", None, None),
        P("resp", None, None),
        P(),
        P("resp"),
        P("resp"),
    )
    return jax.shard_map(
        body,
        mesh=mesh,
        in_specs=placed,
        out_specs=(P("resp", None, "seq"), P("resp", None, "seq"), P(None, "seq", "resp")),
        check_vma=False,
    )
```

```python
import math

import jax
import jax.numpy as jnp
from jax import lax
from jax.experimental import pallas as pl
from jax.experimental.pallas import tpu as pltpu
from jax.sharding import PartitionSpec as P

HDIM = 128
SP = 64
NST = 128
QS = 128


EPS = 1e-05


def from_behind(block, axis, distance):
    devices = range(lax.axis_size(axis))
    route = [(i - distance, i) for i in devices if i - distance in devices]
    return lax.ppermute(block, axis, route)


def broadcast(value, axis, source):
    kept = jnp.where(lax.axis_index(axis) == source, value, 0).astype(value.dtype)
    return lax.psum(kept, axis)


def block_pass(inputs, steps, b_rows, c_rows, rates, state):
    exponent = jnp.cumsum(-steps * rates[:, None], axis=1)
    width = inputs.shape[0]
    lower = lax.broadcasted_iota(jnp.int32, (width, width), 0) >= lax.broadcasted_iota(
        jnp.int32, (width, width), 1
    )
    spread = jnp.where(lower[None], exponent[:, :, None] - exponent[:, None, :], -jnp.inf)
    gram = jnp.dot(c_rows, b_rows.T, preferred_element_type=jnp.float32)
    mixing = (jnp.exp(spread) * gram[None] * steps[:, None, :]).astype(jnp.bfloat16)
    local = jnp.einsum("hts,shp->thp", mixing, inputs, preferred_element_type=jnp.float32)
    carried = jnp.einsum(
        "tn,hpn->thp", c_rows.astype(jnp.float32), state, precision=lax.Precision.HIGHEST
    )
    output = local + carried * jnp.exp(exponent).T[:, :, None]
    last = exponent[:, -1]
    weighted = (
        inputs.astype(jnp.float32) * (jnp.exp(last[:, None] - exponent) * steps).T[:, :, None]
    ).astype(jnp.bfloat16)
    fresh = jnp.einsum("thp,tn->hpn", weighted, b_rows, preferred_element_type=jnp.float32)
    return (output, jnp.exp(last)[:, None, None] * state + fresh, exponent)


def sequence_pass(inputs, steps, b_rows, c_rows, rates):
    window_extent = inputs.shape[0]
    heads = steps.shape[0]
    blocks = window_extent // QS
    xs = inputs.reshape(blocks, QS, heads, SP)
    ss = steps.reshape(heads, blocks, QS).transpose(1, 0, 2)
    bs = b_rows.reshape(blocks, QS, NST)
    cs = c_rows.reshape(blocks, QS, NST)

    def advance(carry, block):
        state, offset = carry
        out, state_next, exponent = block_pass(block[0], block[1], block[2], block[3], rates, state)
        return ((state_next, offset + exponent[:, -1]), (out, offset[:, None] + exponent))

    start = (jnp.zeros((heads, SP, NST), jnp.float32), jnp.zeros((heads,), jnp.float32))
    (final, total), (outs, decays_to) = lax.scan(advance, start, (xs, ss, bs, cs))
    decays_to = decays_to.transpose(1, 0, 2).reshape(heads, window_extent)
    return (outs.reshape(window_extent, heads, SP), final, decays_to, total)


def chunked_pass(inputs, steps, b_rows, c_rows, rates):
    window_extent = inputs.shape[0]
    heads = steps.shape[0]
    blocks = window_extent // QS
    xs = inputs.reshape(blocks, QS, heads, SP).transpose(0, 2, 1, 3)
    ss = steps.reshape(heads, blocks, QS).transpose(1, 0, 2)
    bs = b_rows.reshape(blocks, QS, NST)
    cs = c_rows.reshape(blocks, QS, NST)
    exponent = jnp.cumsum(-ss * rates[None, :, None], axis=2)
    lower = lax.broadcasted_iota(jnp.int32, (QS, QS), 0) >= lax.broadcasted_iota(
        jnp.int32, (QS, QS), 1
    )
    spread = jnp.where(
        lower[None, None], exponent[:, :, :, None] - exponent[:, :, None, :], -jnp.inf
    )
    gram = jnp.einsum("ctn,cun->ctu", cs, bs, preferred_element_type=jnp.float32)
    mixing = (jnp.exp(spread) * gram[:, None] * ss[:, :, None, :]).astype(jnp.bfloat16)
    local = jnp.einsum("chtu,chup->chtp", mixing, xs, preferred_element_type=jnp.float32)
    last = exponent[:, :, -1]
    weighted = (
        xs.astype(jnp.float32) * (jnp.exp(last[:, :, None] - exponent) * ss)[:, :, :, None]
    ).astype(jnp.bfloat16)
    fresh = jnp.einsum("chup,cun->chpn", weighted, bs, preferred_element_type=jnp.float32)
    decay = jnp.exp(last)
    state = jnp.zeros((heads, SP, NST), jnp.float32)
    offset = jnp.zeros((heads,), jnp.float32)
    befores = []
    offsets = []
    for index in range(blocks):
        befores.append(state)
        offsets.append(offset)
        state = decay[index][:, None, None] * state + fresh[index]
        offset = offset + last[index]
    before = jnp.stack(befores)
    carried = jnp.einsum(
        "ctn,chpn->chtp", cs.astype(jnp.float32), before, precision=lax.Precision.HIGHEST
    )
    output = local + carried * jnp.exp(exponent)[:, :, :, None]
    decays_to = jnp.stack(offsets)[:, :, None] + exponent
    output = output.transpose(0, 2, 1, 3).reshape(window_extent, heads, SP)
    decays_to = decays_to.transpose(1, 0, 2).reshape(heads, window_extent)
    return (output, state, decays_to, offset)


def head_norm(values):
    scale = lax.rsqrt(jnp.mean(values * values, axis=-1, keepdims=True) + EPS)
    return (values * scale).reshape(values.shape[0], -1)


def linkage_merge(earlier, later):
    return (earlier[0] * later[0], later[0][:, :, None, None] * earlier[1] + later[1])


def body(
    prompt_keys,
    prompt_values,
    resp_query,
    resp_keys,
    resp_values,
    prompt_x,
    prompt_dt,
    prompt_b,
    prompt_c,
    resp_x,
    resp_dt,
    resp_b,
    resp_c,
    ssm_rate,
    resp_group,
    resp_len,
):
    seq_index = lax.axis_index("seq")
    resp_index = lax.axis_index("resp")
    seq_count = lax.axis_size("seq")
    prompt_count = prompt_x.shape[0]
    prompt_heads = prompt_dt.shape[1]
    resp_heads = resp_dt.shape[1]
    responses_here = resp_x.shape[0]
    slots = resp_x.shape[1]
    memory_head_number = prompt_keys.shape[2] // HDIM
    repeat = seq_count // memory_head_number
    shard_rows = prompt_keys.shape[1]
    spread_keys = jnp.repeat(
        prompt_keys.reshape(prompt_count, shard_rows, memory_head_number, HDIM), repeat, axis=2
    ).reshape(prompt_count, shard_rows, seq_count * HDIM)
    spread_values = jnp.repeat(
        prompt_values.reshape(prompt_count, shard_rows, memory_head_number, HDIM), repeat, axis=2
    ).reshape(prompt_count, shard_rows, seq_count * HDIM)
    moved_keys, moved_values = (
        lax.all_to_all(spread_keys, "seq", split_axis=2, concat_axis=1, tiled=True),
        lax.all_to_all(spread_values, "seq", split_axis=2, concat_axis=1, tiled=True),
    )
    resp_rates = lax.dynamic_slice_in_dim(ssm_rate, seq_index * resp_heads, resp_heads)
    resp_locals = []
    for item in range(responses_here):
        resp_locals.append(
            chunked_pass(resp_x[item], resp_dt[item], resp_b[item], resp_c[item], resp_rates)
        )
    resp_count = lax.axis_size("resp")
    heads_per_chain = prompt_heads // seq_count
    halves = seq_count // resp_count
    width = heads_per_chain * SP
    shard_rows = prompt_x.shape[1]
    spread_x = prompt_x.reshape(prompt_count, shard_rows, halves, resp_count, width)
    spread_x = lax.all_to_all(spread_x, "resp", 3, 3, tiled=True)
    spread_x = spread_x.transpose(0, 1, 3, 2, 4).reshape(prompt_count, shard_rows, seq_count, width)
    chain_x = lax.all_to_all(spread_x, "seq", 2, 1, tiled=True).reshape(
        prompt_count, shard_rows * seq_count, width
    )
    spread_dt = prompt_dt.reshape(prompt_count, halves, resp_count, heads_per_chain, shard_rows)
    spread_dt = lax.all_to_all(spread_dt, "resp", 2, 2, tiled=True)
    spread_dt = spread_dt.transpose(0, 2, 1, 3, 4).reshape(
        prompt_count, seq_count, heads_per_chain, shard_rows
    )
    chain_dt = lax.all_to_all(spread_dt, "seq", 1, 3, tiled=True).reshape(
        prompt_count, heads_per_chain, shard_rows * seq_count
    )
    chain_b = lax.all_gather(prompt_b, "seq", axis=1, tiled=True)
    chain_c = lax.all_gather(prompt_c, "seq", axis=1, tiled=True)
    chain_x, chain_dt, resp_locals = lax.optimization_barrier((chain_x, chain_dt, resp_locals))
    chain_rates = lax.dynamic_slice_in_dim(
        ssm_rate, seq_index * resp_heads + resp_index * heads_per_chain, heads_per_chain
    )
    chain_outs = []
    chain_finals = []
    for prompt in range(prompt_count):
        out, final, decays_to, total = chunked_pass(
            chain_x[prompt], chain_dt[prompt], chain_b[prompt], chain_c[prompt], chain_rates
        )
        chain_outs.append(head_norm(out).astype(jnp.bfloat16))
        chain_finals.append(final)
    chain_final, resp_query = lax.optimization_barrier((jnp.stack(chain_finals), resp_query))
    start_states = lax.all_gather(chain_final, "resp", axis=1, tiled=True)
    back = jnp.stack(chain_outs).reshape(prompt_count, shard_rows * seq_count, 1, width)
    back = lax.all_to_all(back, "seq", 1, 2, tiled=True)
    back = back.reshape(prompt_count, shard_rows, resp_count, halves, width).transpose(0, 1, 3, 2, 4)
    back = lax.all_to_all(back, "resp", 3, 3, tiled=True)
    prompt_ssm_out = back.reshape(prompt_count, shard_rows, halves * resp_count * width)
    own_head = seq_index // repeat
    attention_args = (moved_keys, moved_values, resp_keys, resp_values, resp_group, resp_len, own_head)
    outs = []
    for item in range(responses_here):
        outs.append(response_attention(resp_query, *attention_args, item))
    start_states, outs = lax.optimization_barrier((start_states, outs))
    resp_attn_out = jnp.concatenate(outs, axis=0)
    positions = lax.broadcasted_iota(jnp.int32, (slots,), 0)
    resp_outs = []
    for item in range(responses_here):
        out, final, decays_to, total = resp_locals[item]
        initial = lax.dynamic_index_in_dim(start_states, resp_group[item], 0, keepdims=False)
        carried = jnp.einsum(
            "tn,hdn->thd",
            resp_c[item].astype(jnp.float32),
            initial,
            precision=lax.Precision.HIGHEST,
        )
        corrected = out + jnp.exp(decays_to).T[:, :, None] * carried
        valid = positions < resp_len[item]
        resp_outs.append(jnp.where(valid[:, None], head_norm(corrected), 0.0).astype(jnp.bfloat16))
    resp_ssm_out = jnp.stack(resp_outs)
    return (resp_attn_out, resp_ssm_out, prompt_ssm_out)


ROWS = 512

def response_attention(resp_query, prompt_keys, prompt_values, resp_keys, resp_values, group, length, head, which):
    _, slots, width = resp_query.shape
    items = 1
    heads = width // HDIM
    rows = slots * heads
    queries = resp_query.reshape(resp_query.shape[0], rows, HDIM)
    prompt_len = prompt_keys.shape[1]
    tile = min(ROWS, rows)
    scale = 1.0 / math.sqrt(HDIM)

    def kernel(group_ref, len_ref, head_ref, q_ref, pk_ref, pv_ref, rk_ref, rv_ref, o_ref):
        item = pl.program_id(0)
        block = pl.program_id(1)
        window_extent = len_ref[which + item]
        first = block * (tile // heads)

        @pl.when(first >= window_extent)
        def _():
            o_ref[...] = jnp.zeros_like(o_ref)

        @pl.when(first < window_extent)
        def _():
            q = q_ref[0]
            dims = (((1,), (1,)), ((), ()))
            s1 = lax.dot_general(q, pk_ref[0], dims, preferred_element_type=jnp.float32) * scale
            s2 = lax.dot_general(q, rk_ref[0], dims, preferred_element_type=jnp.float32) * scale
            position = first + lax.broadcasted_iota(jnp.int32, (tile, 1), 0) // heads
            column = lax.broadcasted_iota(jnp.int32, s2.shape, 1)
            s2 = jnp.where(column <= position, s2, -jnp.inf)
            top = jnp.maximum(
                jnp.max(s1, axis=1, keepdims=True), jnp.max(s2, axis=1, keepdims=True)
            )
            e1 = jnp.exp(s1 - top)
            e2 = jnp.exp(s2 - top)
            total = jnp.sum(e1, axis=1, keepdims=True) + jnp.sum(e2, axis=1, keepdims=True)
            mixed = jnp.dot(
                e1.astype(jnp.bfloat16), pv_ref[0], preferred_element_type=jnp.float32
            ) + jnp.dot(e2.astype(jnp.bfloat16), rv_ref[0], preferred_element_type=jnp.float32)
            mixed = mixed / total
            o_ref[0] = jnp.where(position < window_extent, mixed, 0.0).astype(o_ref.dtype)

    keys_total = prompt_len + slots
    cost = pl.CostEstimate(
        flops=4 * items * rows * keys_total * HDIM,
        transcendentals=items * rows * keys_total,
        bytes_accessed=2 * (2 * items * rows * HDIM + 2 * items * keys_total * HDIM),
    )
    grid_spec = pltpu.PrefetchScalarGridSpec(
        num_scalar_prefetch=3,
        grid=(items, rows // tile),
        in_specs=[
            pl.BlockSpec((1, tile, HDIM), lambda i, b, g, n, h: (which + i, b, 0)),
            pl.BlockSpec((1, prompt_len, HDIM), lambda i, b, g, n, h: (g[which + i], 0, 0)),
            pl.BlockSpec((1, prompt_len, HDIM), lambda i, b, g, n, h: (g[which + i], 0, 0)),
            pl.BlockSpec((1, slots, HDIM), lambda i, b, g, n, h: (which + i, 0, h[0])),
            pl.BlockSpec((1, slots, HDIM), lambda i, b, g, n, h: (which + i, 0, h[0])),
        ],
        out_specs=pl.BlockSpec((1, tile, HDIM), lambda i, b, g, n, h: (i, b, 0)),
    )
    out = pl.pallas_call(
        kernel,
        grid_spec=grid_spec,
        out_shape=jax.ShapeDtypeStruct((items, rows, HDIM), jnp.bfloat16),
        compiler_params=pltpu.CompilerParams(vmem_limit_bytes=60 * 1024 * 1024),
        cost_estimate=cost,
    )(group.astype(jnp.int32), length.astype(jnp.int32), jnp.reshape(head, (1,)).astype(jnp.int32),
      queries, prompt_keys, prompt_values, resp_keys, resp_values)
    return out.reshape(items, slots, width)


def solution(mesh):
    placed = (
        P(None, "seq", None),
        P(None, "seq", None),
        P("resp", None, "seq"),
        P("resp", None, None),
        P("resp", None, None),
        P(None, "seq", "resp"),
        P(None, "resp", "seq"),
        P(None, "seq", None),
        P(None, "seq", None),
        P("resp", None, "seq"),
        P("resp", "seq", None),
        P("resp", None, None),
        P("resp", None, None),
        P(),
        P("resp"),
        P("resp"),
    )
    return jax.shard_map(
        body,
        mesh=mesh,
        in_specs=placed,
        out_specs=(P("resp", None, "seq"), P("resp", None, "seq"), P(None, "seq", "resp")),
        check_vma=False,
    )
```

```python
import math

import jax
import jax.numpy as jnp
from jax import lax
from jax.experimental import pallas as pl
from jax.experimental.pallas import tpu as pltpu
from jax.sharding import PartitionSpec as P

HDIM = 128
SP = 64
NST = 128
QS = 128


EPS = 1e-05


def from_behind(block, axis, distance):
    devices = range(lax.axis_size(axis))
    route = [(i - distance, i) for i in devices if i - distance in devices]
    return lax.ppermute(block, axis, route)


def broadcast(value, axis, source):
    kept = jnp.where(lax.axis_index(axis) == source, value, 0).astype(value.dtype)
    return lax.psum(kept, axis)


def block_pass(inputs, steps, b_rows, c_rows, rates, state):
    exponent = jnp.cumsum(-steps * rates[:, None], axis=1)
    width = inputs.shape[0]
    lower = lax.broadcasted_iota(jnp.int32, (width, width), 0) >= lax.broadcasted_iota(
        jnp.int32, (width, width), 1
    )
    spread = jnp.where(lower[None], exponent[:, :, None] - exponent[:, None, :], -jnp.inf)
    gram = jnp.dot(c_rows, b_rows.T, preferred_element_type=jnp.float32)
    mixing = (jnp.exp(spread) * gram[None] * steps[:, None, :]).astype(jnp.bfloat16)
    local = jnp.einsum("hts,shp->thp", mixing, inputs, preferred_element_type=jnp.float32)
    carried = jnp.einsum(
        "tn,hpn->thp", c_rows.astype(jnp.float32), state, precision=lax.Precision.HIGHEST
    )
    output = local + carried * jnp.exp(exponent).T[:, :, None]
    last = exponent[:, -1]
    weighted = (
        inputs.astype(jnp.float32) * (jnp.exp(last[:, None] - exponent) * steps).T[:, :, None]
    ).astype(jnp.bfloat16)
    fresh = jnp.einsum("thp,tn->hpn", weighted, b_rows, preferred_element_type=jnp.float32)
    return (output, jnp.exp(last)[:, None, None] * state + fresh, exponent)


def sequence_pass(inputs, steps, b_rows, c_rows, rates):
    window_extent = inputs.shape[0]
    heads = steps.shape[0]
    blocks = window_extent // QS
    xs = inputs.reshape(blocks, QS, heads, SP)
    ss = steps.reshape(heads, blocks, QS).transpose(1, 0, 2)
    bs = b_rows.reshape(blocks, QS, NST)
    cs = c_rows.reshape(blocks, QS, NST)

    def advance(carry, block):
        state, offset = carry
        out, state_next, exponent = block_pass(block[0], block[1], block[2], block[3], rates, state)
        return ((state_next, offset + exponent[:, -1]), (out, offset[:, None] + exponent))

    start = (jnp.zeros((heads, SP, NST), jnp.float32), jnp.zeros((heads,), jnp.float32))
    (final, total), (outs, decays_to) = lax.scan(advance, start, (xs, ss, bs, cs))
    decays_to = decays_to.transpose(1, 0, 2).reshape(heads, window_extent)
    return (outs.reshape(window_extent, heads, SP), final, decays_to, total)


def chunked_pass(inputs, steps, b_rows, c_rows, rates):
    window_extent = inputs.shape[0]
    heads = steps.shape[0]
    blocks = window_extent // QS
    xs = inputs.reshape(blocks, QS, heads, SP).transpose(0, 2, 1, 3)
    ss = steps.reshape(heads, blocks, QS).transpose(1, 0, 2)
    bs = b_rows.reshape(blocks, QS, NST)
    cs = c_rows.reshape(blocks, QS, NST)
    exponent = jnp.cumsum(-ss * rates[None, :, None], axis=2)
    lower = lax.broadcasted_iota(jnp.int32, (QS, QS), 0) >= lax.broadcasted_iota(
        jnp.int32, (QS, QS), 1
    )
    spread = jnp.where(
        lower[None, None], exponent[:, :, :, None] - exponent[:, :, None, :], -jnp.inf
    )
    gram = jnp.einsum("ctn,cun->ctu", cs, bs, preferred_element_type=jnp.float32)
    mixing = (jnp.exp(spread) * gram[:, None] * ss[:, :, None, :]).astype(jnp.bfloat16)
    local = jnp.einsum("chtu,chup->chtp", mixing, xs, preferred_element_type=jnp.float32)
    last = exponent[:, :, -1]
    weighted = (
        xs.astype(jnp.float32) * (jnp.exp(last[:, :, None] - exponent) * ss)[:, :, :, None]
    ).astype(jnp.bfloat16)
    fresh = jnp.einsum("chup,cun->chpn", weighted, bs, preferred_element_type=jnp.float32)
    decay = jnp.exp(last)
    state = jnp.zeros((heads, SP, NST), jnp.float32)
    offset = jnp.zeros((heads,), jnp.float32)
    befores = []
    offsets = []
    for index in range(blocks):
        befores.append(state)
        offsets.append(offset)
        state = decay[index][:, None, None] * state + fresh[index]
        offset = offset + last[index]
    before = jnp.stack(befores)
    carried = jnp.einsum(
        "ctn,chpn->chtp", cs.astype(jnp.float32), before, precision=lax.Precision.HIGHEST
    )
    output = local + carried * jnp.exp(exponent)[:, :, :, None]
    decays_to = jnp.stack(offsets)[:, :, None] + exponent
    output = output.transpose(0, 2, 1, 3).reshape(window_extent, heads, SP)
    decays_to = decays_to.transpose(1, 0, 2).reshape(heads, window_extent)
    return (output, state, decays_to, offset)


def head_norm(values):
    scale = lax.rsqrt(jnp.mean(values * values, axis=-1, keepdims=True) + EPS)
    return (values * scale).reshape(values.shape[0], -1)


def linkage_merge(earlier, later):
    return (earlier[0] * later[0], later[0][:, :, None, None] * earlier[1] + later[1])


def body(
    prompt_keys,
    prompt_values,
    resp_query,
    resp_keys,
    resp_values,
    prompt_x,
    prompt_dt,
    prompt_b,
    prompt_c,
    resp_x,
    resp_dt,
    resp_b,
    resp_c,
    ssm_rate,
    resp_group,
    resp_len,
):
    seq_index = lax.axis_index("seq")
    resp_index = lax.axis_index("resp")
    seq_count = lax.axis_size("seq")
    prompt_count = prompt_x.shape[0]
    prompt_heads = prompt_dt.shape[1]
    resp_heads = resp_dt.shape[1]
    responses_here = resp_x.shape[0]
    slots = resp_x.shape[1]
    memory_head_number = prompt_keys.shape[2] // HDIM
    repeat = seq_count // memory_head_number
    shard_rows = prompt_keys.shape[1]
    spread_keys = jnp.repeat(
        prompt_keys.reshape(prompt_count, shard_rows, memory_head_number, HDIM), repeat, axis=2
    ).reshape(prompt_count, shard_rows, seq_count * HDIM)
    spread_values = jnp.repeat(
        prompt_values.reshape(prompt_count, shard_rows, memory_head_number, HDIM), repeat, axis=2
    ).reshape(prompt_count, shard_rows, seq_count * HDIM)
    moved_keys, moved_values = (
        lax.all_to_all(spread_keys, "seq", split_axis=2, concat_axis=1, tiled=True),
        lax.all_to_all(spread_values, "seq", split_axis=2, concat_axis=1, tiled=True),
    )
    resp_rates = lax.dynamic_slice_in_dim(ssm_rate, seq_index * resp_heads, resp_heads)
    resp_count = lax.axis_size("resp")
    heads_per_chain = prompt_heads // seq_count
    halves = seq_count // resp_count
    width = heads_per_chain * SP
    shard_rows = prompt_x.shape[1]
    spread_x = prompt_x.reshape(prompt_count, shard_rows, halves, resp_count, width)
    spread_x = lax.all_to_all(spread_x, "resp", 3, 3, tiled=True)
    spread_x = spread_x.transpose(0, 1, 3, 2, 4).reshape(prompt_count, shard_rows, seq_count, width)
    chain_x = lax.all_to_all(spread_x, "seq", 2, 1, tiled=True).reshape(
        prompt_count, shard_rows * seq_count, width
    )
    spread_dt = prompt_dt.reshape(prompt_count, halves, resp_count, heads_per_chain, shard_rows)
    spread_dt = lax.all_to_all(spread_dt, "resp", 2, 2, tiled=True)
    spread_dt = spread_dt.transpose(0, 2, 1, 3, 4).reshape(
        prompt_count, seq_count, heads_per_chain, shard_rows
    )
    chain_dt = lax.all_to_all(spread_dt, "seq", 1, 3, tiled=True).reshape(
        prompt_count, heads_per_chain, shard_rows * seq_count
    )
    chain_b = lax.all_gather(prompt_b, "seq", axis=1, tiled=True)
    chain_c = lax.all_gather(prompt_c, "seq", axis=1, tiled=True)
    own_head = seq_index // repeat
    attention_args = (moved_keys, moved_values, resp_keys, resp_values, resp_group, resp_len, own_head)
    outs = []
    for item in range(responses_here):
        outs.append(response_attention(resp_query, *attention_args, item))
    chain_x, chain_dt, outs = lax.optimization_barrier((chain_x, chain_dt, outs))
    chain_rates = lax.dynamic_slice_in_dim(
        ssm_rate, seq_index * resp_heads + resp_index * heads_per_chain, heads_per_chain
    )
    chain_outs = []
    chain_finals = []
    for prompt in range(prompt_count):
        out, final, decays_to, total = chunked_pass(
            chain_x[prompt], chain_dt[prompt], chain_b[prompt], chain_c[prompt], chain_rates
        )
        chain_outs.append(head_norm(out).astype(jnp.bfloat16))
        chain_finals.append(final)
    chain_final, resp_x = lax.optimization_barrier((jnp.stack(chain_finals), resp_x))
    start_states = lax.all_gather(chain_final, "resp", axis=1, tiled=True)
    back = jnp.stack(chain_outs).reshape(prompt_count, shard_rows * seq_count, 1, width)
    back = lax.all_to_all(back, "seq", 1, 2, tiled=True)
    back = back.reshape(prompt_count, shard_rows, resp_count, halves, width).transpose(0, 1, 3, 2, 4)
    back = lax.all_to_all(back, "resp", 3, 3, tiled=True)
    prompt_ssm_out = back.reshape(prompt_count, shard_rows, halves * resp_count * width)
    resp_locals = []
    for item in range(responses_here):
        resp_locals.append(
            chunked_pass(resp_x[item], resp_dt[item], resp_b[item], resp_c[item], resp_rates)
        )
    start_states, resp_locals = lax.optimization_barrier((start_states, resp_locals))
    resp_attn_out = jnp.concatenate(outs, axis=0)
    positions = lax.broadcasted_iota(jnp.int32, (slots,), 0)
    resp_outs = []
    for item in range(responses_here):
        out, final, decays_to, total = resp_locals[item]
        initial = lax.dynamic_index_in_dim(start_states, resp_group[item], 0, keepdims=False)
        carried = jnp.einsum(
            "tn,hdn->thd",
            resp_c[item].astype(jnp.float32),
            initial,
            precision=lax.Precision.HIGHEST,
        )
        corrected = out + jnp.exp(decays_to).T[:, :, None] * carried
        valid = positions < resp_len[item]
        resp_outs.append(jnp.where(valid[:, None], head_norm(corrected), 0.0).astype(jnp.bfloat16))
    resp_ssm_out = jnp.stack(resp_outs)
    return (resp_attn_out, resp_ssm_out, prompt_ssm_out)


ROWS = 512

def response_attention(resp_query, prompt_keys, prompt_values, resp_keys, resp_values, group, length, head, which):
    _, slots, width = resp_query.shape
    items = 1
    heads = width // HDIM
    rows = slots * heads
    queries = resp_query.reshape(resp_query.shape[0], rows, HDIM)
    prompt_len = prompt_keys.shape[1]
    tile = min(ROWS, rows)
    scale = 1.0 / math.sqrt(HDIM)

    def kernel(group_ref, len_ref, head_ref, q_ref, pk_ref, pv_ref, rk_ref, rv_ref, o_ref):
        item = pl.program_id(0)
        block = pl.program_id(1)
        window_extent = len_ref[which + item]
        first = block * (tile // heads)

        @pl.when(first >= window_extent)
        def _():
            o_ref[...] = jnp.zeros_like(o_ref)

        @pl.when(first < window_extent)
        def _():
            q = q_ref[0]
            dims = (((1,), (1,)), ((), ()))
            s1 = lax.dot_general(q, pk_ref[0], dims, preferred_element_type=jnp.float32) * scale
            s2 = lax.dot_general(q, rk_ref[0], dims, preferred_element_type=jnp.float32) * scale
            position = first + lax.broadcasted_iota(jnp.int32, (tile, 1), 0) // heads
            column = lax.broadcasted_iota(jnp.int32, s2.shape, 1)
            s2 = jnp.where(column <= position, s2, -jnp.inf)
            top = jnp.maximum(
                jnp.max(s1, axis=1, keepdims=True), jnp.max(s2, axis=1, keepdims=True)
            )
            e1 = jnp.exp(s1 - top)
            e2 = jnp.exp(s2 - top)
            total = jnp.sum(e1, axis=1, keepdims=True) + jnp.sum(e2, axis=1, keepdims=True)
            mixed = jnp.dot(
                e1.astype(jnp.bfloat16), pv_ref[0], preferred_element_type=jnp.float32
            ) + jnp.dot(e2.astype(jnp.bfloat16), rv_ref[0], preferred_element_type=jnp.float32)
            mixed = mixed / total
            o_ref[0] = jnp.where(position < window_extent, mixed, 0.0).astype(o_ref.dtype)

    keys_total = prompt_len + slots
    cost = pl.CostEstimate(
        flops=4 * items * rows * keys_total * HDIM,
        transcendentals=items * rows * keys_total,
        bytes_accessed=2 * (2 * items * rows * HDIM + 2 * items * keys_total * HDIM),
    )
    grid_spec = pltpu.PrefetchScalarGridSpec(
        num_scalar_prefetch=3,
        grid=(items, rows // tile),
        in_specs=[
            pl.BlockSpec((1, tile, HDIM), lambda i, b, g, n, h: (which + i, b, 0)),
            pl.BlockSpec((1, prompt_len, HDIM), lambda i, b, g, n, h: (g[which + i], 0, 0)),
            pl.BlockSpec((1, prompt_len, HDIM), lambda i, b, g, n, h: (g[which + i], 0, 0)),
            pl.BlockSpec((1, slots, HDIM), lambda i, b, g, n, h: (which + i, 0, h[0])),
            pl.BlockSpec((1, slots, HDIM), lambda i, b, g, n, h: (which + i, 0, h[0])),
        ],
        out_specs=pl.BlockSpec((1, tile, HDIM), lambda i, b, g, n, h: (i, b, 0)),
    )
    out = pl.pallas_call(
        kernel,
        grid_spec=grid_spec,
        out_shape=jax.ShapeDtypeStruct((items, rows, HDIM), jnp.bfloat16),
        compiler_params=pltpu.CompilerParams(vmem_limit_bytes=60 * 1024 * 1024),
        cost_estimate=cost,
    )(group.astype(jnp.int32), length.astype(jnp.int32), jnp.reshape(head, (1,)).astype(jnp.int32),
      queries, prompt_keys, prompt_values, resp_keys, resp_values)
    return out.reshape(items, slots, width)


def solution(mesh):
    placed = (
        P(None, "seq", None),
        P(None, "seq", None),
        P("resp", None, "seq"),
        P("resp", None, None),
        P("resp", None, None),
        P(None, "seq", "resp"),
        P(None, "resp", "seq"),
        P(None, "seq", None),
        P(None, "seq", None),
        P("resp", None, "seq"),
        P("resp", "seq", None),
        P("resp", None, None),
        P("resp", None, None),
        P(),
        P("resp"),
        P("resp"),
    )
    return jax.shard_map(
        body,
        mesh=mesh,
        in_specs=placed,
        out_specs=(P("resp", None, "seq"), P("resp", None, "seq"), P(None, "seq", "resp")),
        check_vma=False,
    )
```

```python
import math

import jax
import jax.numpy as jnp
from jax import lax
from jax.experimental import pallas as pl
from jax.experimental.pallas import tpu as pltpu
from jax.sharding import PartitionSpec as P

HDIM = 128
SP = 64
NST = 128
QS = 128


EPS = 1e-05


def from_behind(block, axis, distance):
    devices = range(lax.axis_size(axis))
    route = [(i - distance, i) for i in devices if i - distance in devices]
    return lax.ppermute(block, axis, route)


def broadcast(value, axis, source):
    kept = jnp.where(lax.axis_index(axis) == source, value, 0).astype(value.dtype)
    return lax.psum(kept, axis)


def block_pass(inputs, steps, b_rows, c_rows, rates, state):
    exponent = jnp.cumsum(-steps * rates[:, None], axis=1)
    width = inputs.shape[0]
    lower = lax.broadcasted_iota(jnp.int32, (width, width), 0) >= lax.broadcasted_iota(
        jnp.int32, (width, width), 1
    )
    spread = jnp.where(lower[None], exponent[:, :, None] - exponent[:, None, :], -jnp.inf)
    gram = jnp.dot(c_rows, b_rows.T, preferred_element_type=jnp.float32)
    mixing = (jnp.exp(spread) * gram[None] * steps[:, None, :]).astype(jnp.bfloat16)
    local = jnp.einsum("hts,shp->thp", mixing, inputs, preferred_element_type=jnp.float32)
    carried = jnp.einsum(
        "tn,hpn->thp", c_rows.astype(jnp.float32), state, precision=lax.Precision.HIGHEST
    )
    output = local + carried * jnp.exp(exponent).T[:, :, None]
    last = exponent[:, -1]
    weighted = (
        inputs.astype(jnp.float32) * (jnp.exp(last[:, None] - exponent) * steps).T[:, :, None]
    ).astype(jnp.bfloat16)
    fresh = jnp.einsum("thp,tn->hpn", weighted, b_rows, preferred_element_type=jnp.float32)
    return (output, jnp.exp(last)[:, None, None] * state + fresh, exponent)


def sequence_pass(inputs, steps, b_rows, c_rows, rates):
    window_extent = inputs.shape[0]
    heads = steps.shape[0]
    blocks = window_extent // QS
    xs = inputs.reshape(blocks, QS, heads, SP)
    ss = steps.reshape(heads, blocks, QS).transpose(1, 0, 2)
    bs = b_rows.reshape(blocks, QS, NST)
    cs = c_rows.reshape(blocks, QS, NST)

    def advance(carry, block):
        state, offset = carry
        out, state_next, exponent = block_pass(block[0], block[1], block[2], block[3], rates, state)
        return ((state_next, offset + exponent[:, -1]), (out, offset[:, None] + exponent))

    start = (jnp.zeros((heads, SP, NST), jnp.float32), jnp.zeros((heads,), jnp.float32))
    (final, total), (outs, decays_to) = lax.scan(advance, start, (xs, ss, bs, cs))
    decays_to = decays_to.transpose(1, 0, 2).reshape(heads, window_extent)
    return (outs.reshape(window_extent, heads, SP), final, decays_to, total)


def chunked_pass(inputs, steps, b_rows, c_rows, rates):
    window_extent = inputs.shape[0]
    heads = steps.shape[0]
    blocks = window_extent // QS
    xs = inputs.reshape(blocks, QS, heads, SP).transpose(0, 2, 1, 3)
    ss = steps.reshape(heads, blocks, QS).transpose(1, 0, 2)
    bs = b_rows.reshape(blocks, QS, NST)
    cs = c_rows.reshape(blocks, QS, NST)
    exponent = jnp.cumsum(-ss * rates[None, :, None], axis=2)
    lower = lax.broadcasted_iota(jnp.int32, (QS, QS), 0) >= lax.broadcasted_iota(
        jnp.int32, (QS, QS), 1
    )
    spread = jnp.where(
        lower[None, None], exponent[:, :, :, None] - exponent[:, :, None, :], -jnp.inf
    )
    gram = jnp.einsum("ctn,cun->ctu", cs, bs, preferred_element_type=jnp.float32)
    mixing = (jnp.exp(spread) * gram[:, None] * ss[:, :, None, :]).astype(jnp.bfloat16)
    local = jnp.einsum("chtu,chup->chtp", mixing, xs, preferred_element_type=jnp.float32)
    last = exponent[:, :, -1]
    weighted = (
        xs.astype(jnp.float32) * (jnp.exp(last[:, :, None] - exponent) * ss)[:, :, :, None]
    ).astype(jnp.bfloat16)
    fresh = jnp.einsum("chup,cun->chpn", weighted, bs, preferred_element_type=jnp.float32)
    decay = jnp.exp(last)
    state = jnp.zeros((heads, SP, NST), jnp.float32)
    offset = jnp.zeros((heads,), jnp.float32)
    befores = []
    offsets = []
    for index in range(blocks):
        befores.append(state)
        offsets.append(offset)
        state = decay[index][:, None, None] * state + fresh[index]
        offset = offset + last[index]
    before = jnp.stack(befores)
    carried = jnp.einsum(
        "ctn,chpn->chtp", cs.astype(jnp.float32), before, precision=lax.Precision.HIGHEST
    )
    output = local + carried * jnp.exp(exponent)[:, :, :, None]
    decays_to = jnp.stack(offsets)[:, :, None] + exponent
    output = output.transpose(0, 2, 1, 3).reshape(window_extent, heads, SP)
    decays_to = decays_to.transpose(1, 0, 2).reshape(heads, window_extent)
    return (output, state, decays_to, offset)


def head_norm(values):
    scale = lax.rsqrt(jnp.mean(values * values, axis=-1, keepdims=True) + EPS)
    return (values * scale).reshape(values.shape[0], -1)


def linkage_merge(earlier, later):
    return (earlier[0] * later[0], later[0][:, :, None, None] * earlier[1] + later[1])


def body(
    prompt_keys,
    prompt_values,
    resp_query,
    resp_keys,
    resp_values,
    prompt_x,
    prompt_dt,
    prompt_b,
    prompt_c,
    resp_x,
    resp_dt,
    resp_b,
    resp_c,
    ssm_rate,
    resp_group,
    resp_len,
):
    seq_index = lax.axis_index("seq")
    resp_index = lax.axis_index("resp")
    seq_count = lax.axis_size("seq")
    prompt_count = prompt_x.shape[0]
    prompt_heads = prompt_dt.shape[1]
    resp_heads = resp_dt.shape[1]
    responses_here = resp_x.shape[0]
    slots = resp_x.shape[1]
    memory_head_number = prompt_keys.shape[2] // HDIM
    repeat = seq_count // memory_head_number
    shard_rows = prompt_keys.shape[1]
    spread_keys = jnp.repeat(
        prompt_keys.reshape(prompt_count, shard_rows, memory_head_number, HDIM), repeat, axis=2
    ).reshape(prompt_count, shard_rows, seq_count * HDIM)
    spread_values = jnp.repeat(
        prompt_values.reshape(prompt_count, shard_rows, memory_head_number, HDIM), repeat, axis=2
    ).reshape(prompt_count, shard_rows, seq_count * HDIM)
    moved_pair = lax.all_to_all(
        jnp.stack([spread_keys, spread_values]), "seq", split_axis=3, concat_axis=2, tiled=True
    )
    resp_rates = lax.dynamic_slice_in_dim(ssm_rate, seq_index * resp_heads, resp_heads)
    resp_count = lax.axis_size("resp")
    heads_per_chain = prompt_heads // seq_count
    halves = seq_count // resp_count
    width = heads_per_chain * SP
    shard_rows = prompt_x.shape[1]
    own_head = seq_index // repeat

    def local_pass(item, inputs):
        return chunked_pass(inputs[item], resp_dt[item], resp_b[item], resp_c[item], resp_rates)

    resp_locals = [local_pass(0, resp_x)]
    moved_pair, resp_locals = lax.optimization_barrier((moved_pair, resp_locals))
    attention_args = (
        moved_pair[0], moved_pair[1], resp_keys, resp_values, resp_group, resp_len, own_head
    )
    spread_x = prompt_x.reshape(prompt_count, shard_rows, halves, resp_count, width)
    spread_x = lax.all_to_all(spread_x, "resp", 3, 3, tiled=True)
    outs = [response_attention(resp_query, *attention_args, 0)]
    spread_x, outs, resp_x, prompt_dt = lax.optimization_barrier((spread_x, outs, resp_x, prompt_dt))
    spread_dt = prompt_dt.reshape(prompt_count, halves, resp_count, heads_per_chain, shard_rows)
    spread_dt = lax.all_to_all(spread_dt, "resp", 2, 2, tiled=True)
    for item in range(1, responses_here):
        resp_locals.append(local_pass(item, resp_x))
    spread_dt, resp_locals, resp_query = lax.optimization_barrier(
        (spread_dt, resp_locals, resp_query)
    )
    spread_x = spread_x.transpose(0, 1, 3, 2, 4).reshape(prompt_count, shard_rows, seq_count, width)
    chain_x = lax.all_to_all(spread_x, "seq", 2, 1, tiled=True).reshape(
        prompt_count, shard_rows * seq_count, width
    )
    for item in range(1, responses_here):
        outs.append(response_attention(resp_query, *attention_args, item))
    chain_x, outs, spread_dt = lax.optimization_barrier((chain_x, outs, spread_dt))
    spread_dt = spread_dt.transpose(0, 2, 1, 3, 4).reshape(
        prompt_count, seq_count, heads_per_chain, shard_rows
    )
    chain_dt = lax.all_to_all(spread_dt, "seq", 1, 3, tiled=True).reshape(
        prompt_count, heads_per_chain, shard_rows * seq_count
    )
    chain_b = lax.all_gather(prompt_b, "seq", axis=1, tiled=True)
    chain_c = lax.all_gather(prompt_c, "seq", axis=1, tiled=True)
    chain_rates = lax.dynamic_slice_in_dim(
        ssm_rate, seq_index * resp_heads + resp_index * heads_per_chain, heads_per_chain
    )
    chain_outs = []
    chain_finals = []
    for prompt in range(prompt_count):
        out, final, decays_to, total = chunked_pass(
            chain_x[prompt], chain_dt[prompt], chain_b[prompt], chain_c[prompt], chain_rates
        )
        chain_outs.append(head_norm(out).astype(jnp.bfloat16))
        chain_finals.append(final)
    chain_final = jnp.stack(chain_finals)
    start_states = lax.all_gather(chain_final, "resp", axis=1, tiled=True)
    back = jnp.stack(chain_outs).reshape(prompt_count, shard_rows * seq_count, 1, width)
    back = lax.all_to_all(back, "seq", 1, 2, tiled=True)
    back = back.reshape(prompt_count, shard_rows, resp_count, halves, width).transpose(0, 1, 3, 2, 4)
    back = lax.all_to_all(back, "resp", 3, 3, tiled=True)
    prompt_ssm_out = back.reshape(prompt_count, shard_rows, halves * resp_count * width)
    resp_attn_out = jnp.concatenate(outs, axis=0)
    positions = lax.broadcasted_iota(jnp.int32, (slots,), 0)
    resp_outs = []
    for item in range(responses_here):
        out, final, decays_to, total = resp_locals[item]
        initial = lax.dynamic_index_in_dim(start_states, resp_group[item], 0, keepdims=False)
        carried = jnp.einsum(
            "tn,hdn->thd",
            resp_c[item].astype(jnp.float32),
            initial,
            precision=lax.Precision.HIGHEST,
        )
        corrected = out + jnp.exp(decays_to).T[:, :, None] * carried
        valid = positions < resp_len[item]
        resp_outs.append(jnp.where(valid[:, None], head_norm(corrected), 0.0).astype(jnp.bfloat16))
    resp_ssm_out = jnp.stack(resp_outs)
    return (resp_attn_out, resp_ssm_out, prompt_ssm_out)


ROWS = 512

def response_attention(resp_query, prompt_keys, prompt_values, resp_keys, resp_values, group, length, head, which):
    _, slots, width = resp_query.shape
    items = 1
    heads = width // HDIM
    rows = slots * heads
    queries = resp_query.reshape(resp_query.shape[0], rows, HDIM)
    prompt_len = prompt_keys.shape[1]
    tile = min(ROWS, rows)
    scale = 1.0 / math.sqrt(HDIM)

    def kernel(group_ref, len_ref, head_ref, q_ref, pk_ref, pv_ref, rk_ref, rv_ref, o_ref):
        item = pl.program_id(0)
        block = pl.program_id(1)
        window_extent = len_ref[which + item]
        first = block * (tile // heads)

        @pl.when(first >= window_extent)
        def _():
            o_ref[...] = jnp.zeros_like(o_ref)

        @pl.when(first < window_extent)
        def _():
            q = q_ref[0]
            dims = (((1,), (1,)), ((), ()))
            s1 = lax.dot_general(q, pk_ref[0], dims, preferred_element_type=jnp.float32) * scale
            s2 = lax.dot_general(q, rk_ref[0], dims, preferred_element_type=jnp.float32) * scale
            position = first + lax.broadcasted_iota(jnp.int32, (tile, 1), 0) // heads
            column = lax.broadcasted_iota(jnp.int32, s2.shape, 1)
            s2 = jnp.where(column <= position, s2, -jnp.inf)
            top = jnp.maximum(
                jnp.max(s1, axis=1, keepdims=True), jnp.max(s2, axis=1, keepdims=True)
            )
            e1 = jnp.exp(s1 - top)
            e2 = jnp.exp(s2 - top)
            total = jnp.sum(e1, axis=1, keepdims=True) + jnp.sum(e2, axis=1, keepdims=True)
            mixed = jnp.dot(
                e1.astype(jnp.bfloat16), pv_ref[0], preferred_element_type=jnp.float32
            ) + jnp.dot(e2.astype(jnp.bfloat16), rv_ref[0], preferred_element_type=jnp.float32)
            mixed = mixed / total
            o_ref[0] = jnp.where(position < window_extent, mixed, 0.0).astype(o_ref.dtype)

    keys_total = prompt_len + slots
    cost = pl.CostEstimate(
        flops=4 * items * rows * keys_total * HDIM,
        transcendentals=items * rows * keys_total,
        bytes_accessed=2 * (2 * items * rows * HDIM + 2 * items * keys_total * HDIM),
    )
    grid_spec = pltpu.PrefetchScalarGridSpec(
        num_scalar_prefetch=3,
        grid=(items, rows // tile),
        in_specs=[
            pl.BlockSpec((1, tile, HDIM), lambda i, b, g, n, h: (which + i, b, 0)),
            pl.BlockSpec((1, prompt_len, HDIM), lambda i, b, g, n, h: (g[which + i], 0, 0)),
            pl.BlockSpec((1, prompt_len, HDIM), lambda i, b, g, n, h: (g[which + i], 0, 0)),
            pl.BlockSpec((1, slots, HDIM), lambda i, b, g, n, h: (which + i, 0, h[0])),
            pl.BlockSpec((1, slots, HDIM), lambda i, b, g, n, h: (which + i, 0, h[0])),
        ],
        out_specs=pl.BlockSpec((1, tile, HDIM), lambda i, b, g, n, h: (i, b, 0)),
    )
    out = pl.pallas_call(
        kernel,
        grid_spec=grid_spec,
        out_shape=jax.ShapeDtypeStruct((items, rows, HDIM), jnp.bfloat16),
        compiler_params=pltpu.CompilerParams(vmem_limit_bytes=60 * 1024 * 1024),
        cost_estimate=cost,
    )(group.astype(jnp.int32), length.astype(jnp.int32), jnp.reshape(head, (1,)).astype(jnp.int32),
      queries, prompt_keys, prompt_values, resp_keys, resp_values)
    return out.reshape(items, slots, width)


def solution(mesh):
    placed = (
        P(None, "seq", None),
        P(None, "seq", None),
        P("resp", None, "seq"),
        P("resp", None, None),
        P("resp", None, None),
        P(None, "seq", "resp"),
        P(None, "resp", "seq"),
        P(None, "seq", None),
        P(None, "seq", None),
        P("resp", None, "seq"),
        P("resp", "seq", None),
        P("resp", None, None),
        P("resp", None, None),
        P(),
        P("resp"),
        P("resp"),
    )
    return jax.shard_map(
        body,
        mesh=mesh,
        in_specs=placed,
        out_specs=(P("resp", None, "seq"), P("resp", None, "seq"), P(None, "seq", "resp")),
        check_vma=False,
    )
```

```python
import math

import jax
import jax.numpy as jnp
from jax import lax
from jax.experimental import pallas as pl
from jax.experimental.pallas import tpu as pltpu
from jax.sharding import PartitionSpec as P

HDIM = 128
SP = 64
NST = 128
QS = 128


EPS = 1e-05


def from_behind(block, axis, distance):
    devices = range(lax.axis_size(axis))
    route = [(i - distance, i) for i in devices if i - distance in devices]
    return lax.ppermute(block, axis, route)


def broadcast(value, axis, source):
    kept = jnp.where(lax.axis_index(axis) == source, value, 0).astype(value.dtype)
    return lax.psum(kept, axis)


def block_pass(inputs, steps, b_rows, c_rows, rates, state):
    exponent = jnp.cumsum(-steps * rates[:, None], axis=1)
    width = inputs.shape[0]
    lower = lax.broadcasted_iota(jnp.int32, (width, width), 0) >= lax.broadcasted_iota(
        jnp.int32, (width, width), 1
    )
    spread = jnp.where(lower[None], exponent[:, :, None] - exponent[:, None, :], -jnp.inf)
    gram = jnp.dot(c_rows, b_rows.T, preferred_element_type=jnp.float32)
    mixing = (jnp.exp(spread) * gram[None] * steps[:, None, :]).astype(jnp.bfloat16)
    local = jnp.einsum("hts,shp->thp", mixing, inputs, preferred_element_type=jnp.float32)
    carried = jnp.einsum(
        "tn,hpn->thp", c_rows.astype(jnp.float32), state, precision=lax.Precision.HIGHEST
    )
    output = local + carried * jnp.exp(exponent).T[:, :, None]
    last = exponent[:, -1]
    weighted = (
        inputs.astype(jnp.float32) * (jnp.exp(last[:, None] - exponent) * steps).T[:, :, None]
    ).astype(jnp.bfloat16)
    fresh = jnp.einsum("thp,tn->hpn", weighted, b_rows, preferred_element_type=jnp.float32)
    return (output, jnp.exp(last)[:, None, None] * state + fresh, exponent)


def sequence_pass(inputs, steps, b_rows, c_rows, rates):
    window_extent = inputs.shape[0]
    heads = steps.shape[0]
    blocks = window_extent // QS
    xs = inputs.reshape(blocks, QS, heads, SP)
    ss = steps.reshape(heads, blocks, QS).transpose(1, 0, 2)
    bs = b_rows.reshape(blocks, QS, NST)
    cs = c_rows.reshape(blocks, QS, NST)

    def advance(carry, block):
        state, offset = carry
        out, state_next, exponent = block_pass(block[0], block[1], block[2], block[3], rates, state)
        return ((state_next, offset + exponent[:, -1]), (out, offset[:, None] + exponent))

    start = (jnp.zeros((heads, SP, NST), jnp.float32), jnp.zeros((heads,), jnp.float32))
    (final, total), (outs, decays_to) = lax.scan(advance, start, (xs, ss, bs, cs))
    decays_to = decays_to.transpose(1, 0, 2).reshape(heads, window_extent)
    return (outs.reshape(window_extent, heads, SP), final, decays_to, total)


def chunked_pass(inputs, steps, b_rows, c_rows, rates):
    window_extent = inputs.shape[0]
    heads = steps.shape[0]
    blocks = window_extent // QS
    xs = inputs.reshape(blocks, QS, heads, SP)
    ss = steps.reshape(heads, blocks, QS).transpose(1, 0, 2)
    bs = b_rows.reshape(blocks, QS, NST)
    cs = c_rows.reshape(blocks, QS, NST)
    exponent = jnp.cumsum(-ss * rates[None, :, None], axis=2)
    lower = lax.broadcasted_iota(jnp.int32, (QS, QS), 0) >= lax.broadcasted_iota(
        jnp.int32, (QS, QS), 1
    )
    spread = jnp.where(
        lower[None, None], exponent[:, :, :, None] - exponent[:, :, None, :], -jnp.inf
    )
    gram = jnp.einsum("ctn,cun->ctu", cs, bs, preferred_element_type=jnp.float32)
    mixing = (jnp.exp(spread) * gram[:, None] * ss[:, :, None, :]).astype(jnp.bfloat16)
    local = jnp.einsum("chtu,cuhp->cthp", mixing, xs, preferred_element_type=jnp.float32)
    last = exponent[:, :, -1]
    scaled = (jnp.exp(last[:, :, None] - exponent) * ss).transpose(0, 2, 1)
    weighted = (xs.astype(jnp.float32) * scaled[:, :, :, None]).astype(jnp.bfloat16)
    fresh = jnp.einsum("cuhp,cun->chpn", weighted, bs, preferred_element_type=jnp.float32)
    decay = jnp.exp(last)
    state = jnp.zeros((heads, SP, NST), jnp.float32)
    offset = jnp.zeros((heads,), jnp.float32)
    befores = []
    offsets = []
    for index in range(blocks):
        befores.append(state)
        offsets.append(offset)
        state = decay[index][:, None, None] * state + fresh[index]
        offset = offset + last[index]
    before = jnp.stack(befores)
    carried = jnp.einsum(
        "ctn,chpn->cthp", cs.astype(jnp.float32), before, precision=lax.Precision.HIGHEST
    )
    output = local + carried * jnp.exp(exponent).transpose(0, 2, 1)[:, :, :, None]
    decays_to = jnp.stack(offsets)[:, :, None] + exponent
    output = output.reshape(window_extent, heads, SP)
    decays_to = decays_to.transpose(1, 0, 2).reshape(heads, window_extent)
    return (output, state, decays_to, offset)


def head_norm(values):
    scale = lax.rsqrt(jnp.mean(values * values, axis=-1, keepdims=True) + EPS)
    return (values * scale).reshape(values.shape[0], -1)


def linkage_merge(earlier, later):
    return (earlier[0] * later[0], later[0][:, :, None, None] * earlier[1] + later[1])


def body(
    prompt_keys,
    prompt_values,
    resp_query,
    resp_keys,
    resp_values,
    prompt_x,
    prompt_dt,
    prompt_b,
    prompt_c,
    resp_x,
    resp_dt,
    resp_b,
    resp_c,
    ssm_rate,
    resp_group,
    resp_len,
):
    seq_index = lax.axis_index("seq")
    resp_index = lax.axis_index("resp")
    seq_count = lax.axis_size("seq")
    prompt_count = prompt_x.shape[0]
    prompt_heads = prompt_dt.shape[1]
    resp_heads = resp_dt.shape[1]
    responses_here = resp_x.shape[0]
    slots = resp_x.shape[1]
    memory_head_number = prompt_keys.shape[2] // HDIM
    repeat = seq_count // memory_head_number
    shard_rows = prompt_keys.shape[1]
    spread_keys = jnp.repeat(
        prompt_keys.reshape(prompt_count, shard_rows, memory_head_number, HDIM), repeat, axis=2
    ).reshape(prompt_count, shard_rows, seq_count * HDIM)
    spread_values = jnp.repeat(
        prompt_values.reshape(prompt_count, shard_rows, memory_head_number, HDIM), repeat, axis=2
    ).reshape(prompt_count, shard_rows, seq_count * HDIM)
    moved_keys, moved_values = (
        lax.all_to_all(spread_keys, "seq", split_axis=2, concat_axis=1, tiled=True),
        lax.all_to_all(spread_values, "seq", split_axis=2, concat_axis=1, tiled=True),
    )
    resp_rates = lax.dynamic_slice_in_dim(ssm_rate, seq_index * resp_heads, resp_heads)
    resp_locals = []
    for item in range(responses_here):
        resp_locals.append(
            chunked_pass(resp_x[item], resp_dt[item], resp_b[item], resp_c[item], resp_rates)
        )
    heads_per_chain = prompt_heads // seq_count
    chain_x = lax.all_to_all(prompt_x, "seq", split_axis=2, concat_axis=1, tiled=True)
    chain_dt = lax.all_to_all(prompt_dt, "seq", split_axis=1, concat_axis=2, tiled=True)
    chain_b = lax.all_gather(prompt_b, "seq", axis=1, tiled=True)
    chain_c = lax.all_gather(prompt_c, "seq", axis=1, tiled=True)
    chain_rates = lax.dynamic_slice_in_dim(
        ssm_rate, resp_index * prompt_heads + seq_index * heads_per_chain, heads_per_chain
    )
    chain_outs = []
    chain_finals = []
    for prompt in range(prompt_count):
        out, final, decays_to, total = chunked_pass(
            chain_x[prompt], chain_dt[prompt], chain_b[prompt], chain_c[prompt], chain_rates
        )
        chain_outs.append(head_norm(out).astype(jnp.bfloat16))
        chain_finals.append(final)
    prompt_ssm_out = lax.all_to_all(
        jnp.stack(chain_outs), "seq", split_axis=1, concat_axis=2, tiled=True
    )
    finals = lax.all_gather(jnp.stack(chain_finals), "seq", axis=1, tiled=True)
    heads_here = resp_query.shape[2] // HDIM
    own_head = seq_index // repeat
    resp_attn_out = response_attention(
        resp_query, moved_keys, moved_values, resp_keys, resp_values, resp_group, resp_len, own_head
    )
    ratio = seq_count // lax.axis_size("resp")
    piece = lax.dynamic_slice_in_dim(finals, seq_index % ratio * resp_heads, resp_heads, 1)
    start_states = broadcast(piece, "resp", seq_index // ratio)
    positions = lax.broadcasted_iota(jnp.int32, (slots,), 0)
    resp_outs = []
    for item in range(responses_here):
        out, final, decays_to, total = resp_locals[item]
        initial = lax.dynamic_index_in_dim(start_states, resp_group[item], 0, keepdims=False)
        carried = jnp.einsum(
            "tn,hdn->thd",
            resp_c[item].astype(jnp.float32),
            initial,
            precision=lax.Precision.HIGHEST,
        )
        corrected = out + jnp.exp(decays_to).T[:, :, None] * carried
        valid = positions < resp_len[item]
        resp_outs.append(jnp.where(valid[:, None], head_norm(corrected), 0.0).astype(jnp.bfloat16))
    resp_ssm_out = jnp.stack(resp_outs)
    return (resp_attn_out, resp_ssm_out, prompt_ssm_out)


ROWS = 512

def response_attention(resp_query, prompt_keys, prompt_values, resp_keys, resp_values, group, length, head):
    items, slots, width = resp_query.shape
    heads = width // HDIM
    rows = slots * heads
    queries = resp_query.reshape(items, rows, HDIM)
    prompt_len = prompt_keys.shape[1]
    tile = min(ROWS, rows)
    scale = 1.0 / math.sqrt(HDIM)

    def kernel(group_ref, len_ref, head_ref, q_ref, pk_ref, pv_ref, rk_ref, rv_ref, o_ref):
        item = pl.program_id(0)
        block = pl.program_id(1)
        window_extent = len_ref[item]
        first = block * (tile // heads)

        @pl.when(first >= window_extent)
        def _():
            o_ref[...] = jnp.zeros_like(o_ref)

        @pl.when(first < window_extent)
        def _():
            q = q_ref[0]
            dims = (((1,), (1,)), ((), ()))
            s1 = lax.dot_general(q, pk_ref[0], dims, preferred_element_type=jnp.float32) * scale
            s2 = lax.dot_general(q, rk_ref[0], dims, preferred_element_type=jnp.float32) * scale
            position = first + lax.broadcasted_iota(jnp.int32, (tile, 1), 0) // heads
            column = lax.broadcasted_iota(jnp.int32, s2.shape, 1)
            s2 = jnp.where(column <= position, s2, -jnp.inf)
            top = jnp.maximum(
                jnp.max(s1, axis=1, keepdims=True), jnp.max(s2, axis=1, keepdims=True)
            )
            e1 = jnp.exp(s1 - top)
            e2 = jnp.exp(s2 - top)
            total = jnp.sum(e1, axis=1, keepdims=True) + jnp.sum(e2, axis=1, keepdims=True)
            mixed = jnp.dot(
                e1.astype(jnp.bfloat16), pv_ref[0], preferred_element_type=jnp.float32
            ) + jnp.dot(e2.astype(jnp.bfloat16), rv_ref[0], preferred_element_type=jnp.float32)
            mixed = mixed / total
            o_ref[0] = jnp.where(position < window_extent, mixed, 0.0).astype(o_ref.dtype)

    keys_total = prompt_len + slots
    cost = pl.CostEstimate(
        flops=4 * items * rows * keys_total * HDIM,
        transcendentals=items * rows * keys_total,
        bytes_accessed=2 * (2 * items * rows * HDIM + 2 * items * keys_total * HDIM),
    )
    grid_spec = pltpu.PrefetchScalarGridSpec(
        num_scalar_prefetch=3,
        grid=(items, rows // tile),
        in_specs=[
            pl.BlockSpec((1, tile, HDIM), lambda i, b, g, n, h: (i, b, 0)),
            pl.BlockSpec((1, prompt_len, HDIM), lambda i, b, g, n, h: (g[i], 0, 0)),
            pl.BlockSpec((1, prompt_len, HDIM), lambda i, b, g, n, h: (g[i], 0, 0)),
            pl.BlockSpec((1, slots, HDIM), lambda i, b, g, n, h: (i, 0, h[0])),
            pl.BlockSpec((1, slots, HDIM), lambda i, b, g, n, h: (i, 0, h[0])),
        ],
        out_specs=pl.BlockSpec((1, tile, HDIM), lambda i, b, g, n, h: (i, b, 0)),
    )
    out = pl.pallas_call(
        kernel,
        grid_spec=grid_spec,
        out_shape=jax.ShapeDtypeStruct((items, rows, HDIM), jnp.bfloat16),
        compiler_params=pltpu.CompilerParams(vmem_limit_bytes=60 * 1024 * 1024),
        cost_estimate=cost,
    )(group.astype(jnp.int32), length.astype(jnp.int32), jnp.reshape(head, (1,)).astype(jnp.int32),
      queries, prompt_keys, prompt_values, resp_keys, resp_values)
    return out.reshape(items, slots, width)


def solution(mesh):
    placed = (
        P(None, "seq", None),
        P(None, "seq", None),
        P("resp", None, "seq"),
        P("resp", None, None),
        P("resp", None, None),
        P(None, "seq", "resp"),
        P(None, "resp", "seq"),
        P(None, "seq", None),
        P(None, "seq", None),
        P("resp", None, "seq"),
        P("resp", "seq", None),
        P("resp", None, None),
        P("resp", None, None),
        P(),
        P("resp"),
        P("resp"),
    )
    return jax.shard_map(
        body,
        mesh=mesh,
        in_specs=placed,
        out_specs=(P("resp", None, "seq"), P("resp", None, "seq"), P(None, "seq", "resp")),
        check_vma=False,
    )
```

```python
import math

import jax
import jax.numpy as jnp
from jax import lax
from jax.experimental import pallas as pl
from jax.experimental.pallas import tpu as pltpu
from jax.sharding import PartitionSpec as P

HDIM = 128
SP = 64
NST = 128
QS = 128


EPS = 1e-05


def from_behind(block, axis, distance):
    devices = range(lax.axis_size(axis))
    route = [(i - distance, i) for i in devices if i - distance in devices]
    return lax.ppermute(block, axis, route)


def broadcast(value, axis, source):
    kept = jnp.where(lax.axis_index(axis) == source, value, 0).astype(value.dtype)
    return lax.psum(kept, axis)


def block_pass(inputs, steps, b_rows, c_rows, rates, state):
    exponent = jnp.cumsum(-steps * rates[:, None], axis=1)
    width = inputs.shape[0]
    lower = lax.broadcasted_iota(jnp.int32, (width, width), 0) >= lax.broadcasted_iota(
        jnp.int32, (width, width), 1
    )
    spread = jnp.where(lower[None], exponent[:, :, None] - exponent[:, None, :], -jnp.inf)
    gram = jnp.dot(c_rows, b_rows.T, preferred_element_type=jnp.float32)
    mixing = (jnp.exp(spread) * gram[None] * steps[:, None, :]).astype(jnp.bfloat16)
    local = jnp.einsum("hts,shp->thp", mixing, inputs, preferred_element_type=jnp.float32)
    carried = jnp.einsum(
        "tn,hpn->thp", c_rows.astype(jnp.float32), state, precision=lax.Precision.HIGHEST
    )
    output = local + carried * jnp.exp(exponent).T[:, :, None]
    last = exponent[:, -1]
    weighted = (
        inputs.astype(jnp.float32) * (jnp.exp(last[:, None] - exponent) * steps).T[:, :, None]
    ).astype(jnp.bfloat16)
    fresh = jnp.einsum("thp,tn->hpn", weighted, b_rows, preferred_element_type=jnp.float32)
    return (output, jnp.exp(last)[:, None, None] * state + fresh, exponent)


def sequence_pass(inputs, steps, b_rows, c_rows, rates):
    window_extent = inputs.shape[0]
    heads = steps.shape[0]
    blocks = window_extent // QS
    xs = inputs.reshape(blocks, QS, heads, SP)
    ss = steps.reshape(heads, blocks, QS).transpose(1, 0, 2)
    bs = b_rows.reshape(blocks, QS, NST)
    cs = c_rows.reshape(blocks, QS, NST)

    def advance(carry, block):
        state, offset = carry
        out, state_next, exponent = block_pass(block[0], block[1], block[2], block[3], rates, state)
        return ((state_next, offset + exponent[:, -1]), (out, offset[:, None] + exponent))

    start = (jnp.zeros((heads, SP, NST), jnp.float32), jnp.zeros((heads,), jnp.float32))
    (final, total), (outs, decays_to) = lax.scan(advance, start, (xs, ss, bs, cs))
    decays_to = decays_to.transpose(1, 0, 2).reshape(heads, window_extent)
    return (outs.reshape(window_extent, heads, SP), final, decays_to, total)


def chunked_pass(inputs, steps, b_rows, c_rows, rates):
    window_extent = inputs.shape[0]
    heads = steps.shape[0]
    blocks = window_extent // QS
    xs = inputs.reshape(blocks, QS, heads, SP).transpose(0, 2, 1, 3)
    ss = steps.reshape(heads, blocks, QS).transpose(1, 0, 2)
    bs = b_rows.reshape(blocks, QS, NST)
    cs = c_rows.reshape(blocks, QS, NST)
    exponent = jnp.cumsum(-ss * rates[None, :, None], axis=2)
    lower = lax.broadcasted_iota(jnp.int32, (QS, QS), 0) >= lax.broadcasted_iota(
        jnp.int32, (QS, QS), 1
    )
    spread = jnp.where(
        lower[None, None], exponent[:, :, :, None] - exponent[:, :, None, :], -jnp.inf
    )
    gram = jnp.einsum("ctn,cun->ctu", cs, bs, preferred_element_type=jnp.float32)
    mixing = (jnp.exp(spread) * gram[:, None] * ss[:, :, None, :]).astype(jnp.bfloat16)
    local = jnp.einsum("chtu,chup->chtp", mixing, xs, preferred_element_type=jnp.float32)
    last = exponent[:, :, -1]
    weighted = (
        xs.astype(jnp.float32) * (jnp.exp(last[:, :, None] - exponent) * ss)[:, :, :, None]
    ).astype(jnp.bfloat16)
    fresh = jnp.einsum("chup,cun->chpn", weighted, bs, preferred_element_type=jnp.float32)
    decay = jnp.exp(last)
    state = jnp.zeros((heads, SP, NST), jnp.float32)
    offset = jnp.zeros((heads,), jnp.float32)
    befores = []
    offsets = []
    for index in range(blocks):
        befores.append(state)
        offsets.append(offset)
        state = decay[index][:, None, None] * state + fresh[index]
        offset = offset + last[index]
    before = jnp.stack(befores)
    carried = jnp.einsum(
        "ctn,chpn->chtp", cs.astype(jnp.float32), before, precision=lax.Precision.HIGHEST
    )
    output = local + carried * jnp.exp(exponent)[:, :, :, None]
    decays_to = jnp.stack(offsets)[:, :, None] + exponent
    output = output.transpose(0, 2, 1, 3).reshape(window_extent, heads, SP)
    decays_to = decays_to.transpose(1, 0, 2).reshape(heads, window_extent)
    return (output, state, decays_to, offset)


def head_norm(values):
    scale = lax.rsqrt(jnp.mean(values * values, axis=-1, keepdims=True) + EPS)
    return (values * scale).reshape(values.shape[0], -1)


def linkage_merge(earlier, later):
    return (earlier[0] * later[0], later[0][:, :, None, None] * earlier[1] + later[1])


def body(
    prompt_keys,
    prompt_values,
    resp_query,
    resp_keys,
    resp_values,
    prompt_x,
    prompt_dt,
    prompt_b,
    prompt_c,
    resp_x,
    resp_dt,
    resp_b,
    resp_c,
    ssm_rate,
    resp_group,
    resp_len,
):
    seq_index = lax.axis_index("seq")
    resp_index = lax.axis_index("resp")
    seq_count = lax.axis_size("seq")
    prompt_count = prompt_x.shape[0]
    prompt_heads = prompt_dt.shape[1]
    resp_heads = resp_dt.shape[1]
    responses_here = resp_x.shape[0]
    slots = resp_x.shape[1]
    memory_head_number = prompt_keys.shape[2] // HDIM
    repeat = seq_count // memory_head_number
    shard_rows = prompt_keys.shape[1]
    spread_keys = jnp.repeat(
        prompt_keys.reshape(prompt_count, shard_rows, memory_head_number, HDIM), repeat, axis=2
    ).reshape(prompt_count, shard_rows, seq_count * HDIM)
    spread_values = jnp.repeat(
        prompt_values.reshape(prompt_count, shard_rows, memory_head_number, HDIM), repeat, axis=2
    ).reshape(prompt_count, shard_rows, seq_count * HDIM)
    moved_keys, moved_values = (
        lax.all_to_all(spread_keys, "seq", split_axis=2, concat_axis=1, tiled=True),
        lax.all_to_all(spread_values, "seq", split_axis=2, concat_axis=1, tiled=True),
    )
    resp_rates = lax.dynamic_slice_in_dim(ssm_rate, seq_index * resp_heads, resp_heads)
    resp_locals = []
    for item in range(responses_here):
        resp_locals.append(
            chunked_pass(resp_x[item], resp_dt[item], resp_b[item], resp_c[item], resp_rates)
        )
    heads_per_chain = prompt_heads // seq_count
    chain_x = lax.all_to_all(prompt_x, "seq", split_axis=2, concat_axis=1, tiled=True)
    chain_dt = lax.all_to_all(prompt_dt, "seq", split_axis=1, concat_axis=2, tiled=True)
    chain_b = lax.all_gather(prompt_b, "seq", axis=1, tiled=True)
    chain_c = lax.all_gather(prompt_c, "seq", axis=1, tiled=True)
    chain_rates = lax.dynamic_slice_in_dim(
        ssm_rate, resp_index * prompt_heads + seq_index * heads_per_chain, heads_per_chain
    )
    chain_outs = []
    chain_finals = []
    for prompt in range(prompt_count):
        out, final, decays_to, total = chunked_pass(
            chain_x[prompt], chain_dt[prompt], chain_b[prompt], chain_c[prompt], chain_rates
        )
        chain_outs.append(head_norm(out).astype(jnp.bfloat16))
        chain_finals.append(final)
    prompt_ssm_out = lax.all_to_all(
        jnp.stack(chain_outs), "seq", split_axis=1, concat_axis=2, tiled=True
    )
    finals = lax.all_gather(jnp.stack(chain_finals), "seq", axis=1, tiled=True)
    heads_here = resp_query.shape[2] // HDIM
    own_head = seq_index // repeat
    resp_attn_out = response_attention(
        resp_query, moved_keys, moved_values, resp_keys, resp_values, resp_group, resp_len, own_head
    )
    ratio = seq_count // lax.axis_size("resp")
    piece = lax.dynamic_slice_in_dim(finals, seq_index % ratio * resp_heads, resp_heads, 1)
    start_states = broadcast(piece, "resp", seq_index // ratio)
    positions = lax.broadcasted_iota(jnp.int32, (slots,), 0)
    resp_outs = []
    for item in range(responses_here):
        out, final, decays_to, total = resp_locals[item]
        initial = lax.dynamic_index_in_dim(start_states, resp_group[item], 0, keepdims=False)
        carried = jnp.einsum(
            "tn,hdn->thd",
            resp_c[item].astype(jnp.float32),
            initial,
            precision=lax.Precision.HIGHEST,
        )
        corrected = out + jnp.exp(decays_to).T[:, :, None] * carried
        valid = positions < resp_len[item]
        resp_outs.append(jnp.where(valid[:, None], head_norm(corrected), 0.0).astype(jnp.bfloat16))
    resp_ssm_out = jnp.stack(resp_outs)
    return (resp_attn_out, resp_ssm_out, prompt_ssm_out)


ROWS = 512

def response_attention(resp_query, prompt_keys, prompt_values, resp_keys, resp_values, group, length, head):
    items, slots, width = resp_query.shape
    heads = width // HDIM
    rows = slots * heads
    queries = resp_query.reshape(items, rows, HDIM)
    prompt_len = prompt_keys.shape[1]
    tile = min(ROWS, rows)
    scale = 1.0 / math.sqrt(HDIM)

    def kernel(group_ref, len_ref, head_ref, q_ref, pk_ref, pv_ref, rk_ref, rv_ref, o_ref):
        item = pl.program_id(0)
        block = pl.program_id(1)
        window_extent = len_ref[item]
        first = block * (tile // heads)

        @pl.when(first >= window_extent)
        def _():
            o_ref[...] = jnp.zeros_like(o_ref)

        def attend(reach):
            q = q_ref[0]
            dims = (((1,), (1,)), ((), ()))
            s1 = lax.dot_general(q, pk_ref[0], dims, preferred_element_type=jnp.float32) * scale
            s2 = lax.dot_general(
                q, rk_ref[0, :reach, :], dims, preferred_element_type=jnp.float32
            ) * scale
            position = first + lax.broadcasted_iota(jnp.int32, (tile, 1), 0) // heads
            column = lax.broadcasted_iota(jnp.int32, s2.shape, 1)
            s2 = jnp.where(column <= position, s2, -jnp.inf)
            top = jnp.maximum(
                jnp.max(s1, axis=1, keepdims=True), jnp.max(s2, axis=1, keepdims=True)
            )
            e1 = jnp.exp(s1 - top)
            e2 = jnp.exp(s2 - top)
            total = jnp.sum(e1, axis=1, keepdims=True) + jnp.sum(e2, axis=1, keepdims=True)
            mixed = jnp.dot(
                e1.astype(jnp.bfloat16), pv_ref[0], preferred_element_type=jnp.float32
            ) + jnp.dot(
                e2.astype(jnp.bfloat16), rv_ref[0, :reach, :], preferred_element_type=jnp.float32
            )
            mixed = mixed / total
            o_ref[0] = jnp.where(position < window_extent, mixed, 0.0).astype(o_ref.dtype)

        near = (block + 1) * (tile // heads) <= slots // 2

        @pl.when((first < window_extent) & near)
        def _():
            attend(slots // 2)

        @pl.when((first < window_extent) & jnp.logical_not(near))
        def _():
            attend(slots)

    keys_total = prompt_len + slots
    cost = pl.CostEstimate(
        flops=4 * items * rows * keys_total * HDIM,
        transcendentals=items * rows * keys_total,
        bytes_accessed=2 * (2 * items * rows * HDIM + 2 * items * keys_total * HDIM),
    )
    grid_spec = pltpu.PrefetchScalarGridSpec(
        num_scalar_prefetch=3,
        grid=(items, rows // tile),
        in_specs=[
            pl.BlockSpec((1, tile, HDIM), lambda i, b, g, n, h: (i, b, 0)),
            pl.BlockSpec((1, prompt_len, HDIM), lambda i, b, g, n, h: (g[i], 0, 0)),
            pl.BlockSpec((1, prompt_len, HDIM), lambda i, b, g, n, h: (g[i], 0, 0)),
            pl.BlockSpec((1, slots, HDIM), lambda i, b, g, n, h: (i, 0, h[0])),
            pl.BlockSpec((1, slots, HDIM), lambda i, b, g, n, h: (i, 0, h[0])),
        ],
        out_specs=pl.BlockSpec((1, tile, HDIM), lambda i, b, g, n, h: (i, b, 0)),
    )
    out = pl.pallas_call(
        kernel,
        grid_spec=grid_spec,
        out_shape=jax.ShapeDtypeStruct((items, rows, HDIM), jnp.bfloat16),
        compiler_params=pltpu.CompilerParams(vmem_limit_bytes=60 * 1024 * 1024),
        cost_estimate=cost,
    )(group.astype(jnp.int32), length.astype(jnp.int32), jnp.reshape(head, (1,)).astype(jnp.int32),
      queries, prompt_keys, prompt_values, resp_keys, resp_values)
    return out.reshape(items, slots, width)


def solution(mesh):
    placed = (
        P(None, "seq", None),
        P(None, "seq", None),
        P("resp", None, "seq"),
        P("resp", None, None),
        P("resp", None, None),
        P(None, "seq", "resp"),
        P(None, "resp", "seq"),
        P(None, "seq", None),
        P(None, "seq", None),
        P("resp", None, "seq"),
        P("resp", "seq", None),
        P("resp", None, None),
        P("resp", None, None),
        P(),
        P("resp"),
        P("resp"),
    )
    return jax.shard_map(
        body,
        mesh=mesh,
        in_specs=placed,
        out_specs=(P("resp", None, "seq"), P("resp", None, "seq"), P(None, "seq", "resp")),
        check_vma=False,
    )
```

```python
import math

import jax
import jax.numpy as jnp
from jax import lax
from jax.experimental import pallas as pl
from jax.experimental.pallas import tpu as pltpu
from jax.sharding import PartitionSpec as P

HDIM = 128
SP = 64
NST = 128
QS = 128


EPS = 1e-05


def from_behind(block, axis, distance):
    devices = range(lax.axis_size(axis))
    route = [(i - distance, i) for i in devices if i - distance in devices]
    return lax.ppermute(block, axis, route)


def broadcast(value, axis, source):
    kept = jnp.where(lax.axis_index(axis) == source, value, 0).astype(value.dtype)
    return lax.psum(kept, axis)


def block_pass(inputs, steps, b_rows, c_rows, rates, state):
    exponent = jnp.cumsum(-steps * rates[:, None], axis=1)
    width = inputs.shape[0]
    lower = lax.broadcasted_iota(jnp.int32, (width, width), 0) >= lax.broadcasted_iota(
        jnp.int32, (width, width), 1
    )
    spread = jnp.where(lower[None], exponent[:, :, None] - exponent[:, None, :], -jnp.inf)
    gram = jnp.dot(c_rows, b_rows.T, preferred_element_type=jnp.float32)
    mixing = (jnp.exp(spread) * gram[None] * steps[:, None, :]).astype(jnp.bfloat16)
    local = jnp.einsum("hts,shp->thp", mixing, inputs, preferred_element_type=jnp.float32)
    carried = jnp.einsum(
        "tn,hpn->thp", c_rows.astype(jnp.float32), state, precision=lax.Precision.HIGHEST
    )
    output = local + carried * jnp.exp(exponent).T[:, :, None]
    last = exponent[:, -1]
    weighted = (
        inputs.astype(jnp.float32) * (jnp.exp(last[:, None] - exponent) * steps).T[:, :, None]
    ).astype(jnp.bfloat16)
    fresh = jnp.einsum("thp,tn->hpn", weighted, b_rows, preferred_element_type=jnp.float32)
    return (output, jnp.exp(last)[:, None, None] * state + fresh, exponent)


def sequence_pass(inputs, steps, b_rows, c_rows, rates):
    window_extent = inputs.shape[0]
    heads = steps.shape[0]
    blocks = window_extent // QS
    xs = inputs.reshape(blocks, QS, heads, SP)
    ss = steps.reshape(heads, blocks, QS).transpose(1, 0, 2)
    bs = b_rows.reshape(blocks, QS, NST)
    cs = c_rows.reshape(blocks, QS, NST)

    def advance(carry, block):
        state, offset = carry
        out, state_next, exponent = block_pass(block[0], block[1], block[2], block[3], rates, state)
        return ((state_next, offset + exponent[:, -1]), (out, offset[:, None] + exponent))

    start = (jnp.zeros((heads, SP, NST), jnp.float32), jnp.zeros((heads,), jnp.float32))
    (final, total), (outs, decays_to) = lax.scan(advance, start, (xs, ss, bs, cs))
    decays_to = decays_to.transpose(1, 0, 2).reshape(heads, window_extent)
    return (outs.reshape(window_extent, heads, SP), final, decays_to, total)


def chunked_pass(inputs, steps, b_rows, c_rows, rates):
    window_extent = inputs.shape[0]
    heads = steps.shape[0]
    blocks = window_extent // QS
    xs = inputs.reshape(blocks, QS, heads, SP).transpose(0, 2, 1, 3)
    ss = steps.reshape(heads, blocks, QS).transpose(1, 0, 2)
    bs = b_rows.reshape(blocks, QS, NST)
    cs = c_rows.reshape(blocks, QS, NST)
    exponent = jnp.cumsum(-ss * rates[None, :, None], axis=2)
    lower = lax.broadcasted_iota(jnp.int32, (QS, QS), 0) >= lax.broadcasted_iota(
        jnp.int32, (QS, QS), 1
    )
    spread = jnp.where(
        lower[None, None], exponent[:, :, :, None] - exponent[:, :, None, :], -jnp.inf
    )
    gram = jnp.einsum("ctn,cun->ctu", cs, bs, preferred_element_type=jnp.float32)
    mixing = (jnp.exp(spread) * gram[:, None] * ss[:, :, None, :]).astype(jnp.bfloat16)
    local = jnp.einsum("chtu,chup->chtp", mixing, xs, preferred_element_type=jnp.float32)
    last = exponent[:, :, -1]
    weighted = (
        xs.astype(jnp.float32) * (jnp.exp(last[:, :, None] - exponent) * ss)[:, :, :, None]
    ).astype(jnp.bfloat16)
    fresh = jnp.einsum("chup,cun->chpn", weighted, bs, preferred_element_type=jnp.float32)
    decay = jnp.exp(last)
    state = jnp.zeros((heads, SP, NST), jnp.float32)
    offset = jnp.zeros((heads,), jnp.float32)
    befores = []
    offsets = []
    for index in range(blocks):
        befores.append(state)
        offsets.append(offset)
        state = decay[index][:, None, None] * state + fresh[index]
        offset = offset + last[index]
    before = jnp.stack(befores)
    carried = jnp.einsum(
        "ctn,chpn->chtp", cs.astype(jnp.float32), before, precision=lax.Precision.HIGHEST
    )
    output = local + carried * jnp.exp(exponent)[:, :, :, None]
    decays_to = jnp.stack(offsets)[:, :, None] + exponent
    output = output.transpose(0, 2, 1, 3).reshape(window_extent, heads, SP)
    decays_to = decays_to.transpose(1, 0, 2).reshape(heads, window_extent)
    return (output, state, decays_to, offset)


def head_norm(values):
    scale = lax.rsqrt(jnp.mean(values * values, axis=-1, keepdims=True) + EPS)
    return (values * scale).reshape(values.shape[0], -1)


def linkage_merge(earlier, later):
    return (earlier[0] * later[0], later[0][:, :, None, None] * earlier[1] + later[1])


def body(
    prompt_keys,
    prompt_values,
    resp_query,
    resp_keys,
    resp_values,
    prompt_x,
    prompt_dt,
    prompt_b,
    prompt_c,
    resp_x,
    resp_dt,
    resp_b,
    resp_c,
    ssm_rate,
    resp_group,
    resp_len,
):
    seq_index = lax.axis_index("seq")
    resp_index = lax.axis_index("resp")
    seq_count = lax.axis_size("seq")
    prompt_count = prompt_x.shape[0]
    prompt_heads = prompt_dt.shape[1]
    resp_heads = resp_dt.shape[1]
    responses_here = resp_x.shape[0]
    slots = resp_x.shape[1]
    memory_head_number = prompt_keys.shape[2] // HDIM
    repeat = seq_count // memory_head_number
    shard_rows = prompt_keys.shape[1]
    spread_keys = jnp.repeat(
        prompt_keys.reshape(prompt_count, shard_rows, memory_head_number, HDIM), repeat, axis=2
    ).reshape(prompt_count, shard_rows, seq_count * HDIM)
    spread_values = jnp.repeat(
        prompt_values.reshape(prompt_count, shard_rows, memory_head_number, HDIM), repeat, axis=2
    ).reshape(prompt_count, shard_rows, seq_count * HDIM)
    moved_keys, moved_values = (
        lax.all_to_all(spread_keys, "seq", split_axis=2, concat_axis=1, tiled=True),
        lax.all_to_all(spread_values, "seq", split_axis=2, concat_axis=1, tiled=True),
    )
    resp_rates = lax.dynamic_slice_in_dim(ssm_rate, seq_index * resp_heads, resp_heads)
    resp_locals = []
    for item in range(responses_here):
        resp_locals.append(
            chunked_pass(resp_x[item], resp_dt[item], resp_b[item], resp_c[item], resp_rates)
        )
    heads_per_chain = prompt_heads // seq_count
    chain_x = lax.all_to_all(prompt_x, "seq", split_axis=2, concat_axis=1, tiled=True)
    chain_dt = lax.all_to_all(prompt_dt, "seq", split_axis=1, concat_axis=2, tiled=True)
    chain_b = lax.all_gather(prompt_b, "seq", axis=1, tiled=True)
    chain_c = lax.all_gather(prompt_c, "seq", axis=1, tiled=True)
    chain_rates = lax.dynamic_slice_in_dim(
        ssm_rate, resp_index * prompt_heads + seq_index * heads_per_chain, heads_per_chain
    )
    chain_outs = []
    chain_finals = []
    for prompt in range(prompt_count):
        out, final, decays_to, total = chunked_pass(
            chain_x[prompt], chain_dt[prompt], chain_b[prompt], chain_c[prompt], chain_rates
        )
        chain_outs.append(head_norm(out).astype(jnp.bfloat16))
        chain_finals.append(final)
    prompt_ssm_out = lax.all_to_all(
        jnp.stack(chain_outs), "seq", split_axis=1, concat_axis=2, tiled=True
    )
    finals = lax.all_gather(jnp.stack(chain_finals), "seq", axis=1, tiled=True)
    heads_here = resp_query.shape[2] // HDIM
    own_head = seq_index // repeat
    resp_attn_out = response_attention(
        resp_query, moved_keys, moved_values, resp_keys, resp_values, resp_group, resp_len, own_head
    )
    ratio = seq_count // lax.axis_size("resp")
    piece = lax.dynamic_slice_in_dim(finals, seq_index % ratio * resp_heads, resp_heads, 1)
    start_states = broadcast(piece, "resp", seq_index // ratio)
    positions = lax.broadcasted_iota(jnp.int32, (slots,), 0)
    resp_outs = []
    for item in range(responses_here):
        out, final, decays_to, total = resp_locals[item]
        initial = lax.dynamic_index_in_dim(start_states, resp_group[item], 0, keepdims=False)
        carried = jnp.einsum(
            "tn,hdn->thd",
            resp_c[item].astype(jnp.float32),
            initial,
            precision=lax.Precision.HIGHEST,
        )
        corrected = out + jnp.exp(decays_to).T[:, :, None] * carried
        valid = positions < resp_len[item]
        resp_outs.append(jnp.where(valid[:, None], head_norm(corrected), 0.0).astype(jnp.bfloat16))
    resp_ssm_out = jnp.stack(resp_outs)
    return (resp_attn_out, resp_ssm_out, prompt_ssm_out)


ROWS = 512

def response_attention(resp_query, prompt_keys, prompt_values, resp_keys, resp_values, group, length, head):
    items, slots, width = resp_query.shape
    heads = width // HDIM
    rows = slots * heads
    queries = resp_query.reshape(items, rows, HDIM)
    prompt_len = prompt_keys.shape[1]
    tile = min(ROWS, rows)
    scale = 1.0 / math.sqrt(HDIM)

    def kernel(group_ref, len_ref, head_ref, q_ref, pk_ref, pv_ref, rk_ref, rv_ref, o_ref):
        item = pl.program_id(0)
        block = pl.program_id(1)
        window_extent = len_ref[item]
        first = block * (tile // heads)

        @pl.when(first >= window_extent)
        def _():
            o_ref[...] = jnp.zeros_like(o_ref)

        def attend(reach):
            q = q_ref[0]
            dims = (((1,), (1,)), ((), ()))
            s1 = lax.dot_general(q, pk_ref[0], dims, preferred_element_type=jnp.float32) * scale
            s2 = lax.dot_general(
                q, rk_ref[0, :reach, :], dims, preferred_element_type=jnp.float32
            ) * scale
            position = first + lax.broadcasted_iota(jnp.int32, (tile, 1), 0) // heads
            column = lax.broadcasted_iota(jnp.int32, s2.shape, 1)
            s2 = jnp.where(column <= position, s2, -jnp.inf)
            top = jnp.maximum(
                jnp.max(s1, axis=1, keepdims=True), jnp.max(s2, axis=1, keepdims=True)
            )
            e1 = jnp.exp(s1 - top)
            e2 = jnp.exp(s2 - top)
            total = jnp.sum(e1, axis=1, keepdims=True) + jnp.sum(e2, axis=1, keepdims=True)
            mixed = jnp.dot(
                e1.astype(jnp.bfloat16), pv_ref[0], preferred_element_type=jnp.float32
            ) + jnp.dot(
                e2.astype(jnp.bfloat16), rv_ref[0, :reach, :], preferred_element_type=jnp.float32
            )
            mixed = mixed / total
            o_ref[0] = jnp.where(position < window_extent, mixed, 0.0).astype(o_ref.dtype)

        reach_end = (block + 1) * (tile // heads)
        parts = 4
        for part in range(parts):
            low = part * slots // parts
            high = (part + 1) * slots // parts

            @pl.when((first < window_extent) & (reach_end > low) & (reach_end <= high))
            def _():
                attend(high)

    keys_total = prompt_len + slots
    cost = pl.CostEstimate(
        flops=4 * items * rows * keys_total * HDIM,
        transcendentals=items * rows * keys_total,
        bytes_accessed=2 * (2 * items * rows * HDIM + 2 * items * keys_total * HDIM),
    )
    grid_spec = pltpu.PrefetchScalarGridSpec(
        num_scalar_prefetch=3,
        grid=(items, rows // tile),
        in_specs=[
            pl.BlockSpec((1, tile, HDIM), lambda i, b, g, n, h: (i, b, 0)),
            pl.BlockSpec((1, prompt_len, HDIM), lambda i, b, g, n, h: (g[i], 0, 0)),
            pl.BlockSpec((1, prompt_len, HDIM), lambda i, b, g, n, h: (g[i], 0, 0)),
            pl.BlockSpec((1, slots, HDIM), lambda i, b, g, n, h: (i, 0, h[0])),
            pl.BlockSpec((1, slots, HDIM), lambda i, b, g, n, h: (i, 0, h[0])),
        ],
        out_specs=pl.BlockSpec((1, tile, HDIM), lambda i, b, g, n, h: (i, b, 0)),
    )
    out = pl.pallas_call(
        kernel,
        grid_spec=grid_spec,
        out_shape=jax.ShapeDtypeStruct((items, rows, HDIM), jnp.bfloat16),
        compiler_params=pltpu.CompilerParams(vmem_limit_bytes=60 * 1024 * 1024),
        cost_estimate=cost,
    )(group.astype(jnp.int32), length.astype(jnp.int32), jnp.reshape(head, (1,)).astype(jnp.int32),
      queries, prompt_keys, prompt_values, resp_keys, resp_values)
    return out.reshape(items, slots, width)


def solution(mesh):
    placed = (
        P(None, "seq", None),
        P(None, "seq", None),
        P("resp", None, "seq"),
        P("resp", None, None),
        P("resp", None, None),
        P(None, "seq", "resp"),
        P(None, "resp", "seq"),
        P(None, "seq", None),
        P(None, "seq", None),
        P("resp", None, "seq"),
        P("resp", "seq", None),
        P("resp", None, None),
        P("resp", None, None),
        P(),
        P("resp"),
        P("resp"),
    )
    return jax.shard_map(
        body,
        mesh=mesh,
        in_specs=placed,
        out_specs=(P("resp", None, "seq"), P("resp", None, "seq"), P(None, "seq", "resp")),
        check_vma=False,
    )
```
